32 devices in a mesh: rows: 8 (over z, y), cols: 4 (over x, core).
Axes of the slice: x: 2, y: 2, z: 4, core: 2. Of those that a mesh axis runs over, the one named last changes fastest.
Arguments:
- snapshots: float32 [512, 65536], P(('cols', 'rows'))
- pair_table: int32 [4], replicated, may hold values from 0 to 3, as said below
Outputs:
- rotated: float32 [512, 65536], P('cols', 'rows')
The draws below stay inside these ranges and needn't reach their ends.
Inputs may be any that keep to these rules, and one draw needn't show every extreme that they name: pair_table[c] = c XOR m for one m shared by all c, m a power of two below 4, so blocks are paired two by two along one binary digit.
All inputs are finite; a program needn't handle non-finite values.
Results may differ from the reference program's by a relative error of at most 0.0003.
Values sent between devices are 32-bit elements; how exact they have to be, the bound alone decides.
No kernel may reach another device: no remote copies, remote signals or barrier semaphores. Data moves between devices by JAX's collectives and lax.ppermute only.
A program may use at most 64 MiB of HBM per device.

```python
import math
import jax
import jax.numpy as jnp
import numpy as np
from jax import lax

BLOCK = 128
ROUNDS = 8
SNAPS = 512
CELLS = 65536
PAIR_BITS = 2
N_COLS = 4


def draw_snapshots(key, part):
    keys = jax.random.split(jax.random.fold_in(key, 11), 5)
    base = jax.random.normal(keys[0], (SNAPS, CELLS), jnp.float32)
    shared_weight = 0.7
    column_scale = jnp.exp(jax.random.uniform(keys[3], (SNAPS,), jnp.float32, math.log(0.3), math.log(3.0)))
    common = jax.random.normal(keys[1], (CELLS,), jnp.float32)
    weights = jax.random.normal(keys[2], (SNAPS,), jnp.float32)
    ramp = jnp.exp(0.5 * math.log(3.0) * jnp.arange(CELLS, dtype=jnp.float32) / CELLS)
    cell_scale = ramp * jnp.exp(jax.random.uniform(keys[4], (CELLS,), jnp.float32, math.log(0.5), math.log(1.5)))
    field = base + shared_weight * weights[:, None] * common[None, :]
    return (column_scale[:, None] * cell_scale[None, :] * field).astype(jnp.float32)


def draw_pair_table(key, part):
    bit_pos = jax.random.randint(jax.random.fold_in(key, 23), (), 0, PAIR_BITS, dtype=jnp.int32)
    mask_val = jnp.left_shift(jnp.int32(1), bit_pos)
    return jnp.bitwise_xor(jnp.arange(N_COLS, dtype=jnp.int32), mask_val)


def setup_inputs(seed: int = 0) -> dict:
    key_list = jax.random.split(jax.random.key(seed), 3)
    return {
        "snapshots": draw_snapshots(jax.random.fold_in(key_list[2], 71), 0),
        "pair_table": draw_pair_table(jax.random.fold_in(key_list[2], 71), 0),
    }


def round_tables(order_dim, round_idx):
    last_idx = order_dim - 1
    width = order_dim // 2
    first_list = [last_idx] + [(round_idx + offset) % last_idx for offset in range(1, width)]
    second_list = [round_idx % last_idx] + [(round_idx - offset) % last_idx for offset in range(1, width)]
    first_one = np.zeros((order_dim, width), np.float32)
    second_one = np.zeros((order_dim, width), np.float32)
    first_one[first_list, np.arange(width)] = 1.0
    second_one[second_list, np.arange(width)] = 1.0
    return (jnp.asarray(first_one), jnp.asarray(second_one))

def jacobi_rounds(gram_full):
    highest = lax.Precision.HIGHEST
    order_dim = gram_full.shape[0]
    rotation = jnp.eye(order_dim, dtype=gram_full.dtype)
    for round_idx in range(ROUNDS):
        first_one, second_one = round_tables(order_dim, round_idx)
        gram_first = jnp.dot(gram_full, first_one, precision=highest)
        gram_second = jnp.dot(gram_full, second_one, precision=highest)
        diag_first = lax.optimization_barrier(jnp.sum(first_one * gram_first, axis=0))
        cross_val = lax.optimization_barrier(jnp.sum(second_one * gram_first, axis=0))
        diag_second = lax.optimization_barrier(jnp.sum(second_one * gram_second, axis=0))
        spread = diag_second - diag_first
        hypot_val = jnp.sqrt(spread * spread + 4.0 * cross_val * cross_val)
        denom = jnp.sqrt(2.0 * hypot_val * (hypot_val + jnp.abs(spread)))
        sign_val = jnp.where(spread >= 0.0, 1.0, -1.0)
        cosine = (hypot_val + jnp.abs(spread)) / denom
        sine_val = 2.0 * cross_val * sign_val / denom
        turn = jnp.dot(first_one * cosine, first_one.T, precision=highest) + jnp.dot(second_one * cosine, second_one.T, precision=highest) + jnp.dot(first_one * sine_val, second_one.T, precision=highest) - jnp.dot(second_one * sine_val, first_one.T, precision=highest)
        gram_full = jnp.dot(turn.T, jnp.dot(gram_full, turn, precision=highest), precision=highest)
        rotation = jnp.dot(rotation, turn, precision=highest)
    return rotation

def reference(snapshots, pair_table):
    highest = lax.Precision.HIGHEST
    blocks = snapshots.reshape(N_COLS, BLOCK, CELLS)

    def one_block(index):
        partner = pair_table[index]
        own_block = lax.dynamic_index_in_dim(blocks, index, 0, keepdims=False)
        other_block = lax.dynamic_index_in_dim(blocks, partner, 0, keepdims=False)
        own_low = index < partner
        stacked = jnp.where(own_low, jnp.concatenate([own_block, other_block], 0), jnp.concatenate([other_block, own_block], 0))
        gram_full = lax.dot_general(stacked, stacked, (((1,), (1,)), ((), ())), precision=highest, preferred_element_type=jnp.float32)
        rotation = jacobi_rounds(gram_full)
        fresh = jnp.dot(rotation.T, stacked, precision=highest)
        return jnp.where(own_low, fresh[:BLOCK], fresh[BLOCK:])
    result = lax.map(one_block, jnp.arange(N_COLS, dtype=jnp.int32))
    return result.reshape(SNAPS, CELLS)
```

```python
import jax
import jax.numpy as jnp
import numpy as np
from jax import lax
from jax.sharding import PartitionSpec as P

ROUNDS = 8


def partner_2(value, axis, bit):
    mask = 2**bit
    pairs = [(source, source ^ mask) for source in range(lax.axis_size(axis))]
    return lax.ppermute(value, axis, pairs)


def round_tables(order_dim, round_idx):
    last_idx = order_dim - 1
    width = order_dim // 2
    first_list = [last_idx] + [(round_idx + offset) % last_idx for offset in range(1, width)]
    second_list = [round_idx % last_idx] + [
        (round_idx - offset) % last_idx for offset in range(1, width)
    ]
    first_one = np.zeros((order_dim, width), np.float32)
    second_one = np.zeros((order_dim, width), np.float32)
    first_one[first_list, np.arange(width)] = 1.0
    second_one[second_list, np.arange(width)] = 1.0
    return (jnp.asarray(first_one), jnp.asarray(second_one))


def jacobi_rounds(gram_full):
    highest = lax.Precision.HIGHEST
    order_dim = gram_full.shape[0]
    rotation = jnp.eye(order_dim, dtype=gram_full.dtype)
    for round_idx in range(ROUNDS):
        first_one, second_one = round_tables(order_dim, round_idx)
        gram_first = jnp.dot(gram_full, first_one, precision=highest)
        gram_second = jnp.dot(gram_full, second_one, precision=highest)
        diag_first = jnp.sum(first_one * gram_first, axis=0)
        cross_val = jnp.sum(second_one * gram_first, axis=0)
        diag_second = jnp.sum(second_one * gram_second, axis=0)
        spread = diag_second - diag_first
        hypot_val = jnp.sqrt(spread * spread + 4.0 * cross_val * cross_val)
        denom = jnp.sqrt(2.0 * hypot_val * (hypot_val + jnp.abs(spread)))
        sign_val = jnp.where(spread >= 0.0, 1.0, -1.0)
        cosine = (hypot_val + jnp.abs(spread)) / denom
        sine_val = 2.0 * cross_val * sign_val / denom
        turn = (
            jnp.dot(first_one * cosine, first_one.T, precision=highest)
            + jnp.dot(second_one * cosine, second_one.T, precision=highest)
            + jnp.dot(first_one * sine_val, second_one.T, precision=highest)
            - jnp.dot(second_one * sine_val, first_one.T, precision=highest)
        )
        gram_full = jnp.dot(turn.T, jnp.dot(gram_full, turn, precision=highest), precision=highest)
        rotation = jnp.dot(rotation, turn, precision=highest)
    return rotation


def cross_product(left, right):
    return lax.dot_general(
        left,
        right,
        (((1,), (1,)), ((), ())),
        precision=lax.Precision.HIGHEST,
        preferred_element_type=jnp.float32,
    )


def pair_gram(mine, theirs, own_low):
    terms = jnp.stack(
        [cross_product(mine, mine), cross_product(mine, theirs), cross_product(theirs, theirs)]
    )
    terms = row_total(terms)
    gram_mine, gram_mixed, gram_theirs = terms[0], terms[1], terms[2]
    upper_left = jnp.where(own_low, gram_mine, gram_theirs)
    lower_right = jnp.where(own_low, gram_theirs, gram_mine)
    upper_right = jnp.where(own_low, gram_mixed, gram_mixed.T)
    top_rows = jnp.concatenate([upper_left, upper_right], 1)
    bottom_rows = jnp.concatenate([upper_right.T, lower_right], 1)
    return jnp.concatenate([top_rows, bottom_rows], 0)


def row_total(part):
    count = lax.axis_size("rows")
    bit = 1
    while bit < count:
        pairs = [(source, source ^ bit) for source in range(count)]
        part = part + lax.ppermute(part, "rows", pairs)
        bit *= 2
    return part


def toward_partner(value, bit_index, bit_count, sender):
    branches = [
        lambda moving, bit_pos=bit_pos: sender(moving, bit_pos) for bit_pos in range(bit_count)
    ]
    return lax.switch(bit_index, branches, value)


def rotate_part(columns_sel, own_low, mine, theirs):
    highest = lax.Precision.HIGHEST
    width = mine.shape[0]
    coef_mine = jnp.where(own_low, columns_sel[:width], columns_sel[width:])
    coef_theirs = jnp.where(own_low, columns_sel[width:], columns_sel[:width])
    return jnp.dot(coef_mine.T, mine, precision=highest) + jnp.dot(
        coef_theirs.T, theirs, precision=highest
    )


def shards(snapshots, pair_table):
    block = lax.all_to_all(snapshots, "rows", split_axis=1, concat_axis=0, tiled=True)
    bit_count = lax.axis_size("cols").bit_length() - 1
    column = lax.axis_index("cols")
    mask_val = pair_table[0]
    bit_index = jnp.int32(0)
    for bit_pos in range(bit_count):
        bit_index = bit_index + (mask_val >> bit_pos & 1) * bit_pos
    partner = jnp.bitwise_xor(column, mask_val)
    own_low = column < partner
    width = block.shape[0]
    other_block = toward_partner(
        block, bit_index, bit_count, lambda value, bit_pos: partner_2(value, "cols", bit_pos)
    )
    gram_full = pair_gram(block, other_block, own_low)
    rotation = jacobi_rounds(gram_full)
    own_columns = jnp.where(own_low, rotation[:, :width], rotation[:, width:])
    return rotate_part(own_columns, own_low, block, other_block)


def solution(mesh):
    in_specs = (P(("cols", "rows"), None), P())
    out_specs = P("cols", "rows")
    return jax.shard_map(shards, mesh=mesh, in_specs=in_specs, out_specs=out_specs, check_vma=False)
```

```python
import functools

import jax
import jax.numpy as jnp
import numpy as np
from jax import lax
from jax.sharding import PartitionSpec as P

ROUNDS = 8


def partner_2(value, axis, bit):
    mask = 2**bit
    pairs = [(source, source ^ mask) for source in range(lax.axis_size(axis))]
    return lax.ppermute(value, axis, pairs)


def round_tables(order_dim, round_idx):
    last_idx = order_dim - 1
    width = order_dim // 2
    first_list = [last_idx] + [(round_idx + offset) % last_idx for offset in range(1, width)]
    second_list = [round_idx % last_idx] + [
        (round_idx - offset) % last_idx for offset in range(1, width)
    ]
    first_one = np.zeros((order_dim, width), np.float32)
    second_one = np.zeros((order_dim, width), np.float32)
    first_one[first_list, np.arange(width)] = 1.0
    second_one[second_list, np.arange(width)] = 1.0
    return (jnp.asarray(first_one), jnp.asarray(second_one))


def jacobi_rounds(gram_full):
    highest = lax.Precision.HIGHEST
    order_dim = gram_full.shape[0]
    rotation = jnp.eye(order_dim, dtype=gram_full.dtype)
    for round_idx in range(ROUNDS):
        first_one, second_one = round_tables(order_dim, round_idx)
        gram_first = jnp.dot(gram_full, first_one, precision=highest)
        gram_second = jnp.dot(gram_full, second_one, precision=highest)
        diag_first = jnp.sum(first_one * gram_first, axis=0)
        cross_val = jnp.sum(second_one * gram_first, axis=0)
        diag_second = jnp.sum(second_one * gram_second, axis=0)
        spread = diag_second - diag_first
        hypot_val = jnp.sqrt(spread * spread + 4.0 * cross_val * cross_val)
        denom = jnp.sqrt(2.0 * hypot_val * (hypot_val + jnp.abs(spread)))
        sign_val = jnp.where(spread >= 0.0, 1.0, -1.0)
        cosine = (hypot_val + jnp.abs(spread)) / denom
        sine_val = 2.0 * cross_val * sign_val / denom
        turn = (
            jnp.dot(first_one * cosine, first_one.T, precision=highest)
            + jnp.dot(second_one * cosine, second_one.T, precision=highest)
            + jnp.dot(first_one * sine_val, second_one.T, precision=highest)
            - jnp.dot(second_one * sine_val, first_one.T, precision=highest)
        )
        gram_full = jnp.dot(turn.T, jnp.dot(gram_full, turn, precision=highest), precision=highest)
        rotation = jnp.dot(rotation, turn, precision=highest)
    return rotation


def cross_product(left, right):
    return lax.dot_general(
        left,
        right,
        (((1,), (1,)), ((), ())),
        precision=lax.Precision.HIGHEST,
        preferred_element_type=jnp.float32,
    )


def row_total(part):
    count = lax.axis_size("rows")
    bit = 1
    while bit < count:
        pairs = [(source, source ^ bit) for source in range(count)]
        part = part + lax.ppermute(part, "rows", pairs)
        bit *= 2
    return part


CHUNKS = 4


def exchange(bit_pos, snapshots):
    rows_n = lax.axis_size("rows")
    local_rows, cells = snapshots.shape
    piece = cells // rows_n // CHUNKS
    laid = snapshots.reshape(local_rows, rows_n, CHUNKS, piece)

    def chunk_of(chunk):
        return laid[:, :, chunk, :].reshape(local_rows, rows_n * piece)

    def spread(sent):
        return lax.all_to_all(sent, "rows", split_axis=1, concat_axis=0, tiled=True)

    own_parts = [spread(chunk_of(0))]
    other_parts = []
    for chunk in range(1, CHUNKS):
        held = (own_parts[-1], chunk_of(chunk)) + tuple(other_parts[-1:])
        held = lax.optimization_barrier(held)
        own_parts[-1] = held[0]
        if other_parts:
            other_parts[-1] = held[2]
        other_parts.append(partner_2(held[0], "cols", bit_pos))
        own_parts.append(spread(held[1]))
    other_parts.append(partner_2(own_parts[-1], "cols", bit_pos))
    terms = None
    for mine, theirs in zip(own_parts, other_parts):
        part = jnp.stack(
            [cross_product(mine, mine), cross_product(mine, theirs), cross_product(theirs, theirs)]
        )
        terms = part if terms is None else terms + part
    return tuple(own_parts), tuple(other_parts), terms


def assemble(terms, own_low):
    gram_mine, gram_mixed, gram_theirs = terms[0], terms[1], terms[2]
    upper_left = jnp.where(own_low, gram_mine, gram_theirs)
    lower_right = jnp.where(own_low, gram_theirs, gram_mine)
    upper_right = jnp.where(own_low, gram_mixed, gram_mixed.T)
    top_rows = jnp.concatenate([upper_left, upper_right], 1)
    bottom_rows = jnp.concatenate([upper_right.T, lower_right], 1)
    return jnp.concatenate([top_rows, bottom_rows], 0)


def rotate_part(columns_sel, own_low, mine, theirs):
    highest = lax.Precision.HIGHEST
    width = mine.shape[0]
    coef_mine = jnp.where(own_low, columns_sel[:width], columns_sel[width:])
    coef_theirs = jnp.where(own_low, columns_sel[width:], columns_sel[:width])
    return jnp.dot(coef_mine.T, mine, precision=highest) + jnp.dot(
        coef_theirs.T, theirs, precision=highest
    )


def shards(snapshots, pair_table):
    bit_count = lax.axis_size("cols").bit_length() - 1
    column = lax.axis_index("cols")
    mask_val = pair_table[0]
    bit_index = jnp.int32(0)
    for bit_pos in range(bit_count):
        bit_index = bit_index + (mask_val >> bit_pos & 1) * bit_pos
    partner = jnp.bitwise_xor(column, mask_val)
    own_low = column < partner
    branches = [functools.partial(exchange, bit_pos) for bit_pos in range(bit_count)]
    own_parts, other_parts, terms = lax.switch(bit_index, branches, snapshots)
    gram_full = assemble(row_total(terms), own_low)
    rotation = jacobi_rounds(gram_full)
    width = own_parts[0].shape[0]
    own_columns = jnp.where(own_low, rotation[:, :width], rotation[:, width:])
    outs = [rotate_part(own_columns, own_low, mine, theirs) for mine, theirs in zip(own_parts, other_parts)]
    return jnp.concatenate(outs, 1)


def solution(mesh):
    in_specs = (P(("cols", "rows"), None), P())
    out_specs = P("cols", "rows")
    return jax.shard_map(shards, mesh=mesh, in_specs=in_specs, out_specs=out_specs, check_vma=False)
```

```python
import functools

import jax
import jax.numpy as jnp
import numpy as np
from jax import lax
from jax.sharding import PartitionSpec as P

ROUNDS = 8


def partner_2(value, axis, bit):
    mask = 2**bit
    pairs = [(source, source ^ mask) for source in range(lax.axis_size(axis))]
    return lax.ppermute(value, axis, pairs)


def round_tables(order_dim, round_idx):
    last_idx = order_dim - 1
    width = order_dim // 2
    first_list = [last_idx] + [(round_idx + offset) % last_idx for offset in range(1, width)]
    second_list = [round_idx % last_idx] + [
        (round_idx - offset) % last_idx for offset in range(1, width)
    ]
    first_one = np.zeros((order_dim, width), np.float32)
    second_one = np.zeros((order_dim, width), np.float32)
    first_one[first_list, np.arange(width)] = 1.0
    second_one[second_list, np.arange(width)] = 1.0
    return (jnp.asarray(first_one), jnp.asarray(second_one))


def jacobi_rounds(gram_full):
    highest = lax.Precision.HIGHEST
    order_dim = gram_full.shape[0]
    rotation = jnp.eye(order_dim, dtype=gram_full.dtype)
    for round_idx in range(ROUNDS):
        first_one, second_one = round_tables(order_dim, round_idx)
        gram_first = jnp.dot(gram_full, first_one, precision=highest)
        gram_second = jnp.dot(gram_full, second_one, precision=highest)
        diag_first = jnp.sum(first_one * gram_first, axis=0)
        cross_val = jnp.sum(second_one * gram_first, axis=0)
        diag_second = jnp.sum(second_one * gram_second, axis=0)
        spread = diag_second - diag_first
        hypot_val = jnp.sqrt(spread * spread + 4.0 * cross_val * cross_val)
        denom = jnp.sqrt(2.0 * hypot_val * (hypot_val + jnp.abs(spread)))
        sign_val = jnp.where(spread >= 0.0, 1.0, -1.0)
        cosine = (hypot_val + jnp.abs(spread)) / denom
        sine_val = 2.0 * cross_val * sign_val / denom
        turn = (
            jnp.dot(first_one * cosine, first_one.T, precision=highest)
            + jnp.dot(second_one * cosine, second_one.T, precision=highest)
            + jnp.dot(first_one * sine_val, second_one.T, precision=highest)
            - jnp.dot(second_one * sine_val, first_one.T, precision=highest)
        )
        gram_full = jnp.dot(turn.T, jnp.dot(gram_full, turn, precision=highest), precision=highest)
        rotation = jnp.dot(rotation, turn, precision=highest)
    return rotation


def cross_product(left, right):
    return lax.dot_general(
        left,
        right,
        (((1,), (1,)), ((), ())),
        precision=lax.Precision.HIGHEST,
        preferred_element_type=jnp.float32,
    )


def row_total(part):
    count = lax.axis_size("rows")
    bit = 1
    while bit < count:
        pairs = [(source, source ^ bit) for source in range(count)]
        part = part + lax.ppermute(part, "rows", pairs)
        bit *= 2
    return part


CHUNKS = 4


def exchange(bit_pos, snapshots):
    chunks = 1 if bit_pos == 0 else CHUNKS
    rows_n = lax.axis_size("rows")
    local_rows, cells = snapshots.shape
    width = cells // rows_n
    piece = width // chunks

    def laid(chunk):
        return jnp.stack(
            [
                snapshots[:, dest * width + chunk * piece : dest * width + (chunk + 1) * piece]
                for dest in range(rows_n)
            ]
        )

    def spread(sent):
        got = lax.all_to_all(sent, "rows", split_axis=0, concat_axis=0)
        return got.reshape(rows_n * local_rows, piece)

    own_parts = [spread(laid(0))]
    other_parts = []
    for chunk in range(1, chunks):
        held = (own_parts[-1], laid(chunk)) + tuple(other_parts[-1:])
        held = lax.optimization_barrier(held)
        own_parts[-1] = held[0]
        if other_parts:
            other_parts[-1] = held[2]
        other_parts.append(partner_2(held[0], "cols", bit_pos))
        own_parts.append(spread(held[1]))
    other_parts.append(partner_2(own_parts[-1], "cols", bit_pos))
    terms = None
    for mine, theirs in zip(own_parts, other_parts):
        part = jnp.stack(
            [cross_product(mine, mine), cross_product(mine, theirs), cross_product(theirs, theirs)]
        )
        terms = part if terms is None else terms + part
    return jnp.concatenate(own_parts, 1), jnp.concatenate(other_parts, 1), terms


def assemble(terms, own_low):
    gram_mine, gram_mixed, gram_theirs = terms[0], terms[1], terms[2]
    upper_left = jnp.where(own_low, gram_mine, gram_theirs)
    lower_right = jnp.where(own_low, gram_theirs, gram_mine)
    upper_right = jnp.where(own_low, gram_mixed, gram_mixed.T)
    top_rows = jnp.concatenate([upper_left, upper_right], 1)
    bottom_rows = jnp.concatenate([upper_right.T, lower_right], 1)
    return jnp.concatenate([top_rows, bottom_rows], 0)


def rotate_part(columns_sel, own_low, mine, theirs):
    highest = lax.Precision.HIGHEST
    width = mine.shape[0]
    coef_mine = jnp.where(own_low, columns_sel[:width], columns_sel[width:])
    coef_theirs = jnp.where(own_low, columns_sel[width:], columns_sel[:width])
    return jnp.dot(coef_mine.T, mine, precision=highest) + jnp.dot(
        coef_theirs.T, theirs, precision=highest
    )


def shards(snapshots, pair_table):
    bit_count = lax.axis_size("cols").bit_length() - 1
    column = lax.axis_index("cols")
    mask_val = pair_table[0]
    bit_index = jnp.int32(0)
    for bit_pos in range(bit_count):
        bit_index = bit_index + (mask_val >> bit_pos & 1) * bit_pos
    partner = jnp.bitwise_xor(column, mask_val)
    own_low = column < partner
    branches = [functools.partial(exchange, bit_pos) for bit_pos in range(bit_count)]
    own_parts, other_parts, terms = lax.switch(bit_index, branches, snapshots)
    gram_full = assemble(row_total(terms), own_low)
    rotation = jacobi_rounds(gram_full)
    width = own_parts.shape[0]
    own_columns = jnp.where(own_low, rotation[:, :width], rotation[:, width:])
    return rotate_part(own_columns, own_low, own_parts, other_parts)


def solution(mesh):
    in_specs = (P(("cols", "rows"), None), P())
    out_specs = P("cols", "rows")
    return jax.shard_map(shards, mesh=mesh, in_specs=in_specs, out_specs=out_specs, check_vma=False)
```

```python
import functools

import jax
import jax.numpy as jnp
import numpy as np
from jax import lax
from jax.experimental import pallas as pl
from jax.experimental.pallas import tpu as pltpu
from jax.sharding import PartitionSpec as P

ROUNDS = 8


def partner_2(value, axis, bit):
    mask = 2**bit
    pairs = [(source, source ^ mask) for source in range(lax.axis_size(axis))]
    return lax.ppermute(value, axis, pairs)


def jacobi_kernel(gram_ref, rotation_ref):
    highest = lax.Precision.HIGHEST
    order_dim = gram_ref.shape[0]
    last_idx = order_dim - 1
    width = order_dim // 2
    gram = gram_ref[...]
    row_col = lax.broadcasted_iota(jnp.int32, (order_dim, 1), 0)
    row_full = lax.broadcasted_iota(jnp.int32, (order_dim, order_dim), 0)
    col_full = lax.broadcasted_iota(jnp.int32, (order_dim, order_dim), 1)
    eye = row_full == col_full
    rotation = None
    for round_idx in range(ROUNDS):
        fixed = round_idx % last_idx
        mirror = 2 * fixed - row_col
        mirror = jnp.where(mirror < 0, mirror + last_idx, mirror)
        partner = jnp.where(row_col == fixed, last_idx, jnp.where(row_col == last_idx, fixed, mirror))
        offset = row_col - fixed
        offset = jnp.where(offset < 0, offset + last_idx, offset)
        is_first = (row_col == last_idx) | ((row_col != fixed) & (offset >= 1) & (offset <= width - 1))
        swap = (col_full == partner).astype(jnp.float32)
        swapped = jnp.dot(swap, gram, precision=highest, preferred_element_type=jnp.float32)
        diag_own = jnp.sum(jnp.where(eye, gram, 0.0), axis=1, keepdims=True)
        diag_mate = jnp.sum(swapped * swap, axis=1, keepdims=True)
        cross_first = jnp.sum(jnp.where(eye, swapped, 0.0), axis=1, keepdims=True)
        cross_second = jnp.sum(gram * swap, axis=1, keepdims=True)
        cross_val = jnp.where(is_first, cross_first, cross_second)
        spread = jnp.where(is_first, diag_mate - diag_own, diag_own - diag_mate)
        hypot_val = jnp.sqrt(spread * spread + 4.0 * cross_val * cross_val)
        denom = jnp.sqrt(2.0 * hypot_val * (hypot_val + jnp.abs(spread)))
        sign_val = jnp.where(spread >= 0.0, 1.0, -1.0)
        cosine = (hypot_val + jnp.abs(spread)) / denom
        sine_val = 2.0 * cross_val * sign_val / denom
        signed = jnp.where(is_first, sine_val, -sine_val)
        diag_part = jnp.where(eye, cosine, 0.0)
        turn = diag_part + swap * signed
        turn_t = diag_part - swap * signed
        gram = jnp.dot(
            turn_t,
            jnp.dot(gram, turn, precision=highest, preferred_element_type=jnp.float32),
            precision=highest,
            preferred_element_type=jnp.float32,
        )
        rotation = turn if rotation is None else jnp.dot(
            rotation, turn, precision=highest, preferred_element_type=jnp.float32
        )
    rotation_ref[...] = rotation

def jacobi_pallas(gram):
    return pl.pallas_call(
        jacobi_kernel,
        out_shape=jax.ShapeDtypeStruct(gram.shape, jnp.float32),
        in_specs=[pl.BlockSpec(memory_space=pltpu.VMEM)],
        out_specs=pl.BlockSpec(memory_space=pltpu.VMEM),
    )(gram)


def cross_product(left, right):
    return lax.dot_general(
        left,
        right,
        (((1,), (1,)), ((), ())),
        precision=lax.Precision.HIGHEST,
        preferred_element_type=jnp.float32,
    )


def row_total(part):
    count = lax.axis_size("rows")
    bit = 1
    while bit < count:
        pairs = [(source, source ^ bit) for source in range(count)]
        part = part + lax.ppermute(part, "rows", pairs)
        bit *= 2
    return part


CHUNKS = 4


def exchange(bit_pos, snapshots):
    chunks = 1 if bit_pos == 0 else CHUNKS
    rows_n = lax.axis_size("rows")
    local_rows, cells = snapshots.shape
    width = cells // rows_n
    piece = width // chunks

    def laid(chunk):
        return jnp.stack(
            [
                snapshots[:, dest * width + chunk * piece : dest * width + (chunk + 1) * piece]
                for dest in range(rows_n)
            ]
        )

    def spread(sent):
        got = lax.all_to_all(sent, "rows", split_axis=0, concat_axis=0)
        return got.reshape(rows_n * local_rows, piece)

    own_parts = [spread(laid(0))]
    other_parts = []
    for chunk in range(1, chunks):
        held = (own_parts[-1], laid(chunk)) + tuple(other_parts[-1:])
        held = lax.optimization_barrier(held)
        own_parts[-1] = held[0]
        if other_parts:
            other_parts[-1] = held[2]
        other_parts.append(partner_2(held[0], "cols", bit_pos))
        own_parts.append(spread(held[1]))
    other_parts.append(partner_2(own_parts[-1], "cols", bit_pos))
    terms = None
    for mine, theirs in zip(own_parts, other_parts):
        part = jnp.stack(
            [cross_product(mine, mine), cross_product(mine, theirs), cross_product(theirs, theirs)]
        )
        terms = part if terms is None else terms + part
    return jnp.concatenate(own_parts, 1), jnp.concatenate(other_parts, 1), terms


def assemble(terms, own_low):
    gram_mine, gram_mixed, gram_theirs = terms[0], terms[1], terms[2]
    upper_left = jnp.where(own_low, gram_mine, gram_theirs)
    lower_right = jnp.where(own_low, gram_theirs, gram_mine)
    upper_right = jnp.where(own_low, gram_mixed, gram_mixed.T)
    top_rows = jnp.concatenate([upper_left, upper_right], 1)
    bottom_rows = jnp.concatenate([upper_right.T, lower_right], 1)
    return jnp.concatenate([top_rows, bottom_rows], 0)


def rotate_part(columns_sel, own_low, mine, theirs):
    highest = lax.Precision.HIGHEST
    width = mine.shape[0]
    coef_mine = jnp.where(own_low, columns_sel[:width], columns_sel[width:])
    coef_theirs = jnp.where(own_low, columns_sel[width:], columns_sel[:width])
    return jnp.dot(coef_mine.T, mine, precision=highest) + jnp.dot(
        coef_theirs.T, theirs, precision=highest
    )


def shards(snapshots, pair_table):
    bit_count = lax.axis_size("cols").bit_length() - 1
    column = lax.axis_index("cols")
    mask_val = pair_table[0]
    bit_index = jnp.int32(0)
    for bit_pos in range(bit_count):
        bit_index = bit_index + (mask_val >> bit_pos & 1) * bit_pos
    partner = jnp.bitwise_xor(column, mask_val)
    own_low = column < partner
    branches = [functools.partial(exchange, bit_pos) for bit_pos in range(bit_count)]
    own_parts, other_parts, terms = lax.switch(bit_index, branches, snapshots)
    gram_full = assemble(row_total(terms), own_low)
    rotation = jacobi_pallas(gram_full)
    width = own_parts.shape[0]
    own_columns = jnp.where(own_low, rotation[:, :width], rotation[:, width:])
    return rotate_part(own_columns, own_low, own_parts, other_parts)


def solution(mesh):
    in_specs = (P(("cols", "rows"), None), P())
    out_specs = P("cols", "rows")
    return jax.shard_map(shards, mesh=mesh, in_specs=in_specs, out_specs=out_specs, check_vma=False)
```

```python
import functools

import jax
import jax.numpy as jnp
import numpy as np
from jax import lax
from jax.experimental import pallas as pl
from jax.experimental.pallas import tpu as pltpu
from jax.sharding import PartitionSpec as P

ROUNDS = 8


def partner_2(value, axis, bit):
    mask = 2**bit
    pairs = [(source, source ^ mask) for source in range(lax.axis_size(axis))]
    return lax.ppermute(value, axis, pairs)


def jacobi_kernel(gram_ref, rotation_ref):
    highest = lax.Precision.HIGHEST
    order_dim = gram_ref.shape[0]
    last_idx = order_dim - 1
    width = order_dim // 2
    gram = gram_ref[...]
    row_col = lax.broadcasted_iota(jnp.int32, (order_dim, 1), 0)
    row_full = lax.broadcasted_iota(jnp.int32, (order_dim, order_dim), 0)
    col_full = lax.broadcasted_iota(jnp.int32, (order_dim, order_dim), 1)
    eye = row_full == col_full
    rotation = None
    for round_idx in range(ROUNDS):
        fixed = round_idx % last_idx
        mirror = 2 * fixed - row_col
        mirror = jnp.where(mirror < 0, mirror + last_idx, mirror)
        partner = jnp.where(row_col == fixed, last_idx, jnp.where(row_col == last_idx, fixed, mirror))
        offset = row_col - fixed
        offset = jnp.where(offset < 0, offset + last_idx, offset)
        is_first = (row_col == last_idx) | ((row_col != fixed) & (offset >= 1) & (offset <= width - 1))
        swap = (col_full == partner).astype(jnp.float32)
        swapped = jnp.dot(swap, gram, precision=highest, preferred_element_type=jnp.float32)
        diag_own = jnp.sum(jnp.where(eye, gram, 0.0), axis=1, keepdims=True)
        diag_mate = jnp.sum(swapped * swap, axis=1, keepdims=True)
        cross_first = jnp.sum(jnp.where(eye, swapped, 0.0), axis=1, keepdims=True)
        cross_second = jnp.sum(gram * swap, axis=1, keepdims=True)
        cross_val = jnp.where(is_first, cross_first, cross_second)
        spread = jnp.where(is_first, diag_mate - diag_own, diag_own - diag_mate)
        hypot_val = jnp.sqrt(spread * spread + 4.0 * cross_val * cross_val)
        denom = jnp.sqrt(2.0 * hypot_val * (hypot_val + jnp.abs(spread)))
        sign_val = jnp.where(spread >= 0.0, 1.0, -1.0)
        cosine = (hypot_val + jnp.abs(spread)) / denom
        sine_val = 2.0 * cross_val * sign_val / denom
        signed = jnp.where(is_first, sine_val, -sine_val)
        diag_part = jnp.where(eye, cosine, 0.0)
        turn = diag_part + swap * signed
        turn_t = diag_part - swap * signed
        gram = jnp.dot(
            turn_t,
            jnp.dot(gram, turn, precision=highest, preferred_element_type=jnp.float32),
            precision=highest,
            preferred_element_type=jnp.float32,
        )
        rotation = turn if rotation is None else jnp.dot(
            rotation, turn, precision=highest, preferred_element_type=jnp.float32
        )
    rotation_ref[...] = rotation

def jacobi_pallas(gram):
    return pl.pallas_call(
        jacobi_kernel,
        out_shape=jax.ShapeDtypeStruct(gram.shape, jnp.float32),
        in_specs=[pl.BlockSpec(memory_space=pltpu.VMEM)],
        out_specs=pl.BlockSpec(memory_space=pltpu.VMEM),
    )(gram)


def cross_product(left, right):
    return lax.dot_general(
        left,
        right,
        (((1,), (1,)), ((), ())),
        precision=lax.Precision.HIGHEST,
        preferred_element_type=jnp.float32,
    )


def row_total(part):
    count = lax.axis_size("rows")
    bit = 1
    while bit < count:
        pairs = [(source, source ^ bit) for source in range(count)]
        part = part + lax.ppermute(part, "rows", pairs)
        bit *= 2
    return part


CHUNKS = 4


def exchange(bit_pos, snapshots):
    chunks = 1 if bit_pos == 0 else CHUNKS
    rows_n = lax.axis_size("rows")
    local_rows, cells = snapshots.shape
    width = cells // rows_n
    piece = width // chunks
    block_rows = rows_n * local_rows

    def laid(source, chunk):
        return jnp.stack(
            [
                source[:, dest * width + chunk * piece : dest * width + (chunk + 1) * piece]
                for dest in range(rows_n)
            ]
        )

    def spread(sent):
        got = lax.all_to_all(sent, "rows", split_axis=0, concat_axis=0)
        return got.reshape(block_rows, piece)

    if chunks == 1:
        mine = spread(laid(snapshots, 0))
        theirs = partner_2(mine, "cols", bit_pos)
        part = jnp.stack(
            [cross_product(mine, mine), cross_product(mine, theirs), cross_product(theirs, theirs)]
        )
        return mine, theirs, part

    own_full = jnp.zeros((block_rows, width), snapshots.dtype)
    other_full = jnp.zeros((block_rows, width), snapshots.dtype)
    terms = None

    def take(own_full, other_full, terms, chunk, mine, theirs):
        part = jnp.stack(
            [cross_product(mine, mine), cross_product(mine, theirs), cross_product(theirs, theirs)]
        )
        terms = part if terms is None else terms + part
        own_full = lax.dynamic_update_slice(own_full, mine, (0, chunk * piece))
        other_full = lax.dynamic_update_slice(other_full, theirs, (0, chunk * piece))
        return own_full, other_full, terms

    source = snapshots
    mine = spread(laid(source, 0))
    sent = laid(source, 1)
    theirs = None
    for chunk in range(1, chunks):
        held = lax.optimization_barrier((mine, sent, source) + ((theirs,) if theirs is not None else ()))
        mine, sent, source = held[0], held[1], held[2]
        if theirs is not None:
            theirs = held[3]
            own_full, other_full, terms = take(own_full, other_full, terms, chunk - 2, prev_mine, theirs)
        prev_mine = mine
        theirs = partner_2(mine, "cols", bit_pos)
        mine = spread(sent)
        if chunk + 1 < chunks:
            sent = laid(source, chunk + 1)
    own_full, other_full, terms = take(own_full, other_full, terms, chunks - 2, prev_mine, theirs)
    last = partner_2(mine, "cols", bit_pos)
    own_full, other_full, terms = take(own_full, other_full, terms, chunks - 1, mine, last)
    return own_full, other_full, terms


def assemble(terms, own_low):
    gram_mine, gram_mixed, gram_theirs = terms[0], terms[1], terms[2]
    upper_left = jnp.where(own_low, gram_mine, gram_theirs)
    lower_right = jnp.where(own_low, gram_theirs, gram_mine)
    upper_right = jnp.where(own_low, gram_mixed, gram_mixed.T)
    top_rows = jnp.concatenate([upper_left, upper_right], 1)
    bottom_rows = jnp.concatenate([upper_right.T, lower_right], 1)
    return jnp.concatenate([top_rows, bottom_rows], 0)


def rotate_part(columns_sel, own_low, mine, theirs):
    width = mine.shape[0]
    coef_mine = jnp.where(own_low, columns_sel[:width], columns_sel[width:])
    coef_theirs = jnp.where(own_low, columns_sel[width:], columns_sel[:width])
    return jnp.dot(coef_mine.T, mine, precision=lax.Precision.HIGH) + jnp.dot(
        coef_theirs.T, theirs, precision=lax.Precision.HIGH
    )


def shards(snapshots, pair_table):
    bit_count = lax.axis_size("cols").bit_length() - 1
    column = lax.axis_index("cols")
    mask_val = pair_table[0]
    bit_index = jnp.int32(0)
    for bit_pos in range(bit_count):
        bit_index = bit_index + (mask_val >> bit_pos & 1) * bit_pos
    partner = jnp.bitwise_xor(column, mask_val)
    own_low = column < partner
    branches = [functools.partial(exchange, bit_pos) for bit_pos in range(bit_count)]
    own_parts, other_parts, terms = lax.switch(bit_index, branches, snapshots)
    gram_full = assemble(row_total(terms), own_low)
    rotation = jacobi_pallas(gram_full)
    width = own_parts.shape[0]
    own_columns = jnp.where(own_low, rotation[:, :width], rotation[:, width:])
    return rotate_part(own_columns, own_low, own_parts, other_parts)


def solution(mesh):
    in_specs = (P(("cols", "rows"), None), P())
    out_specs = P("cols", "rows")
    return jax.shard_map(shards, mesh=mesh, in_specs=in_specs, out_specs=out_specs, check_vma=False)
```

```python
import functools

import jax
import jax.numpy as jnp
import numpy as np
from jax import lax
from jax.experimental import pallas as pl
from jax.experimental.pallas import tpu as pltpu
from jax.sharding import PartitionSpec as P

ROUNDS = 8


def partner_2(value, axis, bit):
    mask = 2**bit
    pairs = [(source, source ^ mask) for source in range(lax.axis_size(axis))]
    return lax.ppermute(value, axis, pairs)


def jacobi_kernel(gram_ref, rotation_ref):
    highest = lax.Precision.HIGHEST
    order_dim = gram_ref.shape[0]
    last_idx = order_dim - 1
    width = order_dim // 2
    gram = gram_ref[...]
    row_col = lax.broadcasted_iota(jnp.int32, (order_dim, 1), 0)
    row_full = lax.broadcasted_iota(jnp.int32, (order_dim, order_dim), 0)
    col_full = lax.broadcasted_iota(jnp.int32, (order_dim, order_dim), 1)
    eye = row_full == col_full
    rotation = None
    for round_idx in range(ROUNDS):
        fixed = round_idx % last_idx
        mirror = 2 * fixed - row_col
        mirror = jnp.where(mirror < 0, mirror + last_idx, mirror)
        partner = jnp.where(row_col == fixed, last_idx, jnp.where(row_col == last_idx, fixed, mirror))
        offset = row_col - fixed
        offset = jnp.where(offset < 0, offset + last_idx, offset)
        is_first = (row_col == last_idx) | ((row_col != fixed) & (offset >= 1) & (offset <= width - 1))
        swap = (col_full == partner).astype(jnp.float32)
        on_diag = jnp.where(eye, gram, 0.0)
        diag_own = jnp.sum(on_diag, axis=1, keepdims=True)
        diag_row = jnp.sum(on_diag, axis=0, keepdims=True)
        diag_mate = jnp.sum(swap * diag_row, axis=1, keepdims=True)
        picked = gram * swap
        cross_second = jnp.sum(picked, axis=1, keepdims=True)
        cross_row = jnp.sum(picked, axis=0, keepdims=True)
        cross_first = jnp.sum(jnp.where(eye, cross_row, 0.0), axis=1, keepdims=True)
        cross_val = jnp.where(is_first, cross_first, cross_second)
        spread = jnp.where(is_first, diag_mate - diag_own, diag_own - diag_mate)
        hypot_val = jnp.sqrt(spread * spread + 4.0 * cross_val * cross_val)
        denom = jnp.sqrt(2.0 * hypot_val * (hypot_val + jnp.abs(spread)))
        sign_val = jnp.where(spread >= 0.0, 1.0, -1.0)
        cosine = (hypot_val + jnp.abs(spread)) / denom
        sine_val = 2.0 * cross_val * sign_val / denom
        signed = jnp.where(is_first, sine_val, -sine_val)
        diag_part = jnp.where(eye, cosine, 0.0)
        turn = diag_part + swap * signed
        turn_t = diag_part - swap * signed
        gram = jnp.dot(
            turn_t,
            jnp.dot(gram, turn, precision=highest, preferred_element_type=jnp.float32),
            precision=highest,
            preferred_element_type=jnp.float32,
        )
        rotation = turn if rotation is None else jnp.dot(
            rotation, turn, precision=highest, preferred_element_type=jnp.float32
        )
    rotation_ref[...] = rotation

def jacobi_pallas(gram):
    return pl.pallas_call(
        jacobi_kernel,
        out_shape=jax.ShapeDtypeStruct(gram.shape, jnp.float32),
        in_specs=[pl.BlockSpec(memory_space=pltpu.VMEM)],
        out_specs=pl.BlockSpec(memory_space=pltpu.VMEM),
    )(gram)


def cross_product(left, right):
    return lax.dot_general(
        left,
        right,
        (((1,), (1,)), ((), ())),
        precision=lax.Precision.HIGHEST,
        preferred_element_type=jnp.float32,
    )


def row_total(part):
    count = lax.axis_size("rows")
    bit = 1
    while bit < count:
        pairs = [(source, source ^ bit) for source in range(count)]
        part = part + lax.ppermute(part, "rows", pairs)
        bit *= 2
    return part


CHUNKS = 4


def exchange(bit_pos, snapshots):
    chunks = 1 if bit_pos == 0 else CHUNKS
    rows_n = lax.axis_size("rows")
    local_rows, cells = snapshots.shape
    width = cells // rows_n
    piece = width // chunks

    def laid(chunk):
        return jnp.stack(
            [
                snapshots[:, dest * width + chunk * piece : dest * width + (chunk + 1) * piece]
                for dest in range(rows_n)
            ]
        )

    def spread(sent):
        got = lax.all_to_all(sent, "rows", split_axis=0, concat_axis=0)
        return got.reshape(rows_n * local_rows, piece)

    own_parts = [spread(laid(0))]
    other_parts = []
    for chunk in range(1, chunks):
        held = (own_parts[-1], laid(chunk)) + tuple(other_parts[-1:])
        held = lax.optimization_barrier(held)
        own_parts[-1] = held[0]
        if other_parts:
            other_parts[-1] = held[2]
        other_parts.append(partner_2(held[0], "cols", bit_pos))
        own_parts.append(spread(held[1]))
    other_parts.append(partner_2(own_parts[-1], "cols", bit_pos))
    terms = None
    for mine, theirs in zip(own_parts, other_parts):
        part = jnp.stack(
            [cross_product(mine, mine), cross_product(mine, theirs), cross_product(theirs, theirs)]
        )
        terms = part if terms is None else terms + part
    return jnp.concatenate(own_parts, 1), jnp.concatenate(other_parts, 1), terms


def assemble(terms, own_low):
    gram_mine, gram_mixed, gram_theirs = terms[0], terms[1], terms[2]
    upper_left = jnp.where(own_low, gram_mine, gram_theirs)
    lower_right = jnp.where(own_low, gram_theirs, gram_mine)
    upper_right = jnp.where(own_low, gram_mixed, gram_mixed.T)
    top_rows = jnp.concatenate([upper_left, upper_right], 1)
    bottom_rows = jnp.concatenate([upper_right.T, lower_right], 1)
    return jnp.concatenate([top_rows, bottom_rows], 0)


def rotate_kernel(coef_mine_ref, coef_theirs_ref, mine_ref, theirs_ref, out_ref):
    highest = lax.Precision.HIGHEST
    out_ref[...] = jnp.dot(
        coef_mine_ref[...], mine_ref[...], precision=highest, preferred_element_type=jnp.float32
    ) + jnp.dot(
        coef_theirs_ref[...], theirs_ref[...], precision=highest, preferred_element_type=jnp.float32
    )


def rotate_part(columns_sel, own_low, mine, theirs):
    width, cells = mine.shape
    coef_mine = jnp.where(own_low, columns_sel[:width], columns_sel[width:]).T
    coef_theirs = jnp.where(own_low, columns_sel[width:], columns_sel[:width]).T
    tile = min(cells, 2048)
    coef_spec = pl.BlockSpec((width, width), lambda step: (0, 0))
    cell_spec = pl.BlockSpec((width, tile), lambda step: (0, step))
    return pl.pallas_call(
        rotate_kernel,
        out_shape=jax.ShapeDtypeStruct((width, cells), jnp.float32),
        grid=(cells // tile,),
        in_specs=[coef_spec, coef_spec, cell_spec, cell_spec],
        out_specs=cell_spec,
        cost_estimate=pl.CostEstimate(
            flops=4 * width * width * cells, transcendentals=0, bytes_accessed=12 * width * cells
        ),
    )(coef_mine, coef_theirs, mine, theirs)


def shards(snapshots, pair_table):
    bit_count = lax.axis_size("cols").bit_length() - 1
    column = lax.axis_index("cols")
    mask_val = pair_table[0]
    bit_index = jnp.int32(0)
    for bit_pos in range(bit_count):
        bit_index = bit_index + (mask_val >> bit_pos & 1) * bit_pos
    partner = jnp.bitwise_xor(column, mask_val)
    own_low = column < partner
    branches = [functools.partial(exchange, bit_pos) for bit_pos in range(bit_count)]
    own_parts, other_parts, terms = lax.switch(bit_index, branches, snapshots)
    gram_full = assemble(row_total(terms), own_low)
    rotation = jacobi_pallas(gram_full)
    width = own_parts.shape[0]
    own_columns = jnp.where(own_low, rotation[:, :width], rotation[:, width:])
    return rotate_part(own_columns, own_low, own_parts, other_parts)


def solution(mesh):
    in_specs = (P(("cols", "rows"), None), P())
    out_specs = P("cols", "rows")
    return jax.shard_map(shards, mesh=mesh, in_specs=in_specs, out_specs=out_specs, check_vma=False)
```

```python
import functools

import jax
import jax.numpy as jnp
import numpy as np
from jax import lax
from jax.experimental import pallas as pl
from jax.experimental.pallas import tpu as pltpu
from jax.sharding import PartitionSpec as P

ROUNDS = 8


def partner_2(value, axis, bit):
    mask = 2**bit
    pairs = [(source, source ^ mask) for source in range(lax.axis_size(axis))]
    return lax.ppermute(value, axis, pairs)


def jacobi_kernel(gram_ref, rotation_ref):
    highest = lax.Precision.HIGHEST
    order_dim = gram_ref.shape[0]
    last_idx = order_dim - 1
    width = order_dim // 2
    gram = gram_ref[...]
    row_col = lax.broadcasted_iota(jnp.int32, (order_dim, 1), 0)
    row_full = lax.broadcasted_iota(jnp.int32, (order_dim, order_dim), 0)
    col_full = lax.broadcasted_iota(jnp.int32, (order_dim, order_dim), 1)
    eye = row_full == col_full
    rotation = None
    for round_idx in range(ROUNDS):
        fixed = round_idx % last_idx
        mirror = 2 * fixed - row_col
        mirror = jnp.where(mirror < 0, mirror + last_idx, mirror)
        partner = jnp.where(row_col == fixed, last_idx, jnp.where(row_col == last_idx, fixed, mirror))
        offset = row_col - fixed
        offset = jnp.where(offset < 0, offset + last_idx, offset)
        is_first = (row_col == last_idx) | ((row_col != fixed) & (offset >= 1) & (offset <= width - 1))
        swap = (col_full == partner).astype(jnp.float32)
        on_diag = jnp.where(eye, gram, 0.0)
        diag_own = jnp.sum(on_diag, axis=1, keepdims=True)
        diag_row = jnp.sum(on_diag, axis=0, keepdims=True)
        diag_mate = jnp.sum(swap * diag_row, axis=1, keepdims=True)
        picked = gram * swap
        cross_second = jnp.sum(picked, axis=1, keepdims=True)
        cross_row = jnp.sum(picked, axis=0, keepdims=True)
        cross_first = jnp.sum(jnp.where(eye, cross_row, 0.0), axis=1, keepdims=True)
        cross_val = jnp.where(is_first, cross_first, cross_second)
        spread = jnp.where(is_first, diag_mate - diag_own, diag_own - diag_mate)
        hypot_val = jnp.sqrt(spread * spread + 4.0 * cross_val * cross_val)
        denom = jnp.sqrt(2.0 * hypot_val * (hypot_val + jnp.abs(spread)))
        sign_val = jnp.where(spread >= 0.0, 1.0, -1.0)
        cosine = (hypot_val + jnp.abs(spread)) / denom
        sine_val = 2.0 * cross_val * sign_val / denom
        signed = jnp.where(is_first, sine_val, -sine_val)
        diag_part = jnp.where(eye, cosine, 0.0)
        turn = diag_part + swap * signed
        turn_t = diag_part - swap * signed
        gram = jnp.dot(
            turn_t,
            jnp.dot(gram, turn, precision=highest, preferred_element_type=jnp.float32),
            precision=highest,
            preferred_element_type=jnp.float32,
        )
        rotation = turn if rotation is None else jnp.dot(
            rotation, turn, precision=highest, preferred_element_type=jnp.float32
        )
    rotation_ref[...] = rotation

def jacobi_pallas(gram):
    return pl.pallas_call(
        jacobi_kernel,
        out_shape=jax.ShapeDtypeStruct(gram.shape, jnp.float32),
        in_specs=[pl.BlockSpec(memory_space=pltpu.VMEM)],
        out_specs=pl.BlockSpec(memory_space=pltpu.VMEM),
    )(gram)


def gram_kernel(mine_ref, theirs_ref, out_ref, acc_ref):
    step = pl.program_id(0)

    @pl.when(step == 0)
    def _():
        acc_ref[...] = jnp.zeros_like(acc_ref)

    stacked = jnp.concatenate([mine_ref[...], theirs_ref[...]], 0)
    acc_ref[...] += lax.dot_general(
        stacked,
        stacked,
        (((1,), (1,)), ((), ())),
        precision=lax.Precision.HIGHEST,
        preferred_element_type=jnp.float32,
    )

    @pl.when(step == pl.num_programs(0) - 1)
    def _():
        width = mine_ref.shape[0]
        out_ref[0] = acc_ref[:width, :width]
        out_ref[1] = acc_ref[:width, width:]
        out_ref[2] = acc_ref[width:, width:]


def pair_terms(mine, theirs):
    width, cells = mine.shape
    tile = min(cells, 2048)
    cell_spec = pl.BlockSpec((width, tile), lambda step: (0, step))
    return pl.pallas_call(
        gram_kernel,
        out_shape=jax.ShapeDtypeStruct((3, width, width), jnp.float32),
        grid=(cells // tile,),
        in_specs=[cell_spec, cell_spec],
        out_specs=pl.BlockSpec((3, width, width), lambda step: (0, 0, 0)),
        scratch_shapes=[pltpu.VMEM((2 * width, 2 * width), jnp.float32)],
        cost_estimate=pl.CostEstimate(
            flops=8 * width * width * cells, transcendentals=0, bytes_accessed=8 * width * cells
        ),
    )(mine, theirs)


def row_total(part):
    count = lax.axis_size("rows")
    bit = 1
    while bit < count:
        pairs = [(source, source ^ bit) for source in range(count)]
        part = part + lax.ppermute(part, "rows", pairs)
        bit *= 2
    return part


CHUNKS = 4


def exchange(bit_pos, snapshots):
    chunks = 1 if bit_pos == 0 else CHUNKS
    rows_n = lax.axis_size("rows")
    local_rows, cells = snapshots.shape
    width = cells // rows_n
    piece = width // chunks

    def laid(chunk):
        return jnp.stack(
            [
                snapshots[:, dest * width + chunk * piece : dest * width + (chunk + 1) * piece]
                for dest in range(rows_n)
            ]
        )

    def spread(sent):
        got = lax.all_to_all(sent, "rows", split_axis=0, concat_axis=0)
        return got.reshape(rows_n * local_rows, piece)

    own_parts = [spread(laid(0))]
    other_parts = []
    for chunk in range(1, chunks):
        held = (own_parts[-1], laid(chunk)) + tuple(other_parts[-1:])
        held = lax.optimization_barrier(held)
        own_parts[-1] = held[0]
        if other_parts:
            other_parts[-1] = held[2]
        other_parts.append(partner_2(held[0], "cols", bit_pos))
        own_parts.append(spread(held[1]))
    other_parts.append(partner_2(own_parts[-1], "cols", bit_pos))
    terms = None
    for mine, theirs in zip(own_parts, other_parts):
        part = pair_terms(mine, theirs)
        terms = part if terms is None else terms + part
    return jnp.concatenate(own_parts, 1), jnp.concatenate(other_parts, 1), terms


def assemble(terms, own_low):
    gram_mine, gram_mixed, gram_theirs = terms[0], terms[1], terms[2]
    upper_left = jnp.where(own_low, gram_mine, gram_theirs)
    lower_right = jnp.where(own_low, gram_theirs, gram_mine)
    upper_right = jnp.where(own_low, gram_mixed, gram_mixed.T)
    top_rows = jnp.concatenate([upper_left, upper_right], 1)
    bottom_rows = jnp.concatenate([upper_right.T, lower_right], 1)
    return jnp.concatenate([top_rows, bottom_rows], 0)


def rotate_kernel(coef_ref, mine_ref, theirs_ref, out_ref):
    stacked = jnp.concatenate([mine_ref[...], theirs_ref[...]], 0)
    out_ref[...] = jnp.dot(
        coef_ref[...], stacked, precision=lax.Precision.HIGHEST, preferred_element_type=jnp.float32
    )


def rotate_part(columns_sel, own_low, mine, theirs):
    width, cells = mine.shape
    coef_mine = jnp.where(own_low, columns_sel[:width], columns_sel[width:])
    coef_theirs = jnp.where(own_low, columns_sel[width:], columns_sel[:width])
    coef = jnp.concatenate([coef_mine, coef_theirs], 0).T
    tile = min(cells, 2048)
    coef_spec = pl.BlockSpec((width, 2 * width), lambda step: (0, 0))
    cell_spec = pl.BlockSpec((width, tile), lambda step: (0, step))
    return pl.pallas_call(
        rotate_kernel,
        out_shape=jax.ShapeDtypeStruct((width, cells), jnp.float32),
        grid=(cells // tile,),
        in_specs=[coef_spec, cell_spec, cell_spec],
        out_specs=cell_spec,
        cost_estimate=pl.CostEstimate(
            flops=4 * width * width * cells, transcendentals=0, bytes_accessed=12 * width * cells
        ),
    )(coef, mine, theirs)


def shards(snapshots, pair_table):
    bit_count = lax.axis_size("cols").bit_length() - 1
    column = lax.axis_index("cols")
    mask_val = pair_table[0]
    bit_index = jnp.int32(0)
    for bit_pos in range(bit_count):
        bit_index = bit_index + (mask_val >> bit_pos & 1) * bit_pos
    partner = jnp.bitwise_xor(column, mask_val)
    own_low = column < partner
    branches = [functools.partial(exchange, bit_pos) for bit_pos in range(bit_count)]
    own_parts, other_parts, terms = lax.switch(bit_index, branches, snapshots)
    gram_full = assemble(row_total(terms), own_low)
    rotation = jacobi_pallas(gram_full)
    width = own_parts.shape[0]
    own_columns = jnp.where(own_low, rotation[:, :width], rotation[:, width:])
    return rotate_part(own_columns, own_low, own_parts, other_parts)


def solution(mesh):
    in_specs = (P(("cols", "rows"), None), P())
    out_specs = P("cols", "rows")
    return jax.shard_map(shards, mesh=mesh, in_specs=in_specs, out_specs=out_specs, check_vma=False)
```

```python
import functools

import jax
import jax.numpy as jnp
import numpy as np
from jax import lax
from jax.experimental import pallas as pl
from jax.experimental.pallas import tpu as pltpu
from jax.sharding import PartitionSpec as P

ROUNDS = 8


def partner_2(value, axis, bit):
    mask = 2**bit
    pairs = [(source, source ^ mask) for source in range(lax.axis_size(axis))]
    return lax.ppermute(value, axis, pairs)


def jacobi_kernel(gram_ref, rotation_ref):
    highest = lax.Precision.HIGHEST
    order_dim = gram_ref.shape[0]
    last_idx = order_dim - 1
    width = order_dim // 2
    gram = gram_ref[...]
    row_col = lax.broadcasted_iota(jnp.int32, (order_dim, 1), 0)
    row_full = lax.broadcasted_iota(jnp.int32, (order_dim, order_dim), 0)
    col_full = lax.broadcasted_iota(jnp.int32, (order_dim, order_dim), 1)
    eye = row_full == col_full
    rotation = None
    for round_idx in range(ROUNDS):
        fixed = round_idx % last_idx
        mirror = 2 * fixed - row_col
        mirror = jnp.where(mirror < 0, mirror + last_idx, mirror)
        partner = jnp.where(row_col == fixed, last_idx, jnp.where(row_col == last_idx, fixed, mirror))
        offset = row_col - fixed
        offset = jnp.where(offset < 0, offset + last_idx, offset)
        is_first = (row_col == last_idx) | ((row_col != fixed) & (offset >= 1) & (offset <= width - 1))
        swap = (col_full == partner).astype(jnp.float32)
        on_diag = jnp.where(eye, gram, 0.0)
        diag_own = jnp.sum(on_diag, axis=1, keepdims=True)
        diag_row = jnp.sum(on_diag, axis=0, keepdims=True)
        diag_mate = jnp.sum(swap * diag_row, axis=1, keepdims=True)
        picked = gram * swap
        cross_second = jnp.sum(picked, axis=1, keepdims=True)
        cross_row = jnp.sum(picked, axis=0, keepdims=True)
        cross_first = jnp.sum(jnp.where(eye, cross_row, 0.0), axis=1, keepdims=True)
        cross_val = jnp.where(is_first, cross_first, cross_second)
        spread = jnp.where(is_first, diag_mate - diag_own, diag_own - diag_mate)
        hypot_val = jnp.sqrt(spread * spread + 4.0 * cross_val * cross_val)
        denom = jnp.sqrt(2.0 * hypot_val * (hypot_val + jnp.abs(spread)))
        sign_val = jnp.where(spread >= 0.0, 1.0, -1.0)
        cosine = (hypot_val + jnp.abs(spread)) / denom
        sine_val = 2.0 * cross_val * sign_val / denom
        signed = jnp.where(is_first, sine_val, -sine_val)
        diag_part = jnp.where(eye, cosine, 0.0)
        turn = diag_part + swap * signed
        turn_t = diag_part - swap * signed
        gram = jnp.dot(
            turn_t,
            jnp.dot(gram, turn, precision=highest, preferred_element_type=jnp.float32),
            precision=highest,
            preferred_element_type=jnp.float32,
        )
        rotation = turn if rotation is None else jnp.dot(
            rotation, turn, precision=highest, preferred_element_type=jnp.float32
        )
    rotation_ref[...] = rotation

def jacobi_pallas(gram):
    return pl.pallas_call(
        jacobi_kernel,
        out_shape=jax.ShapeDtypeStruct(gram.shape, jnp.float32),
        in_specs=[pl.BlockSpec(memory_space=pltpu.VMEM)],
        out_specs=pl.BlockSpec(memory_space=pltpu.VMEM),
    )(gram)


def gram_kernel(mine_ref, theirs_ref, out_ref, acc_ref):
    step = pl.program_id(0)

    @pl.when(step == 0)
    def _():
        acc_ref[...] = jnp.zeros_like(acc_ref)

    stacked = jnp.concatenate([mine_ref[...], theirs_ref[...]], 0)
    acc_ref[...] += lax.dot_general(
        stacked,
        stacked,
        (((1,), (1,)), ((), ())),
        precision=lax.Precision.HIGHEST,
        preferred_element_type=jnp.float32,
    )

    @pl.when(step == pl.num_programs(0) - 1)
    def _():
        width = mine_ref.shape[0]
        out_ref[0] = acc_ref[:width, :width]
        out_ref[1] = acc_ref[:width, width:]
        out_ref[2] = acc_ref[width:, width:]


def pair_terms(mine, theirs):
    width, cells = mine.shape
    tile = min(cells, 2048)
    cell_spec = pl.BlockSpec((width, tile), lambda step: (0, step))
    return pl.pallas_call(
        gram_kernel,
        out_shape=jax.ShapeDtypeStruct((3, width, width), jnp.float32),
        grid=(cells // tile,),
        in_specs=[cell_spec, cell_spec],
        out_specs=pl.BlockSpec((3, width, width), lambda step: (0, 0, 0)),
        scratch_shapes=[pltpu.VMEM((2 * width, 2 * width), jnp.float32)],
        cost_estimate=pl.CostEstimate(
            flops=8 * width * width * cells, transcendentals=0, bytes_accessed=8 * width * cells
        ),
    )(mine, theirs)


def row_total(part):
    count = lax.axis_size("rows")
    bit = 1
    while bit < count:
        pairs = [(source, source ^ bit) for source in range(count)]
        part = part + lax.ppermute(part, "rows", pairs)
        bit *= 2
    return part


CHUNKS = 4


def lay_kernel(source_ref, *out_refs):
    piece = out_refs[0].shape[-1]
    for chunk, out_ref in enumerate(out_refs):
        out_ref[...] = source_ref[:, chunk * piece : (chunk + 1) * piece]


def lay_out(snapshots, rows_n, chunks):
    local_rows, cells = snapshots.shape
    width = cells // rows_n
    piece = width // chunks
    out_spec = pl.BlockSpec((None, local_rows, piece), lambda dest: (dest, 0, 0))
    return pl.pallas_call(
        lay_kernel,
        out_shape=[jax.ShapeDtypeStruct((rows_n, local_rows, piece), snapshots.dtype)] * chunks,
        grid=(rows_n,),
        in_specs=[pl.BlockSpec((local_rows, width), lambda dest: (0, dest))],
        out_specs=[out_spec] * chunks,
        cost_estimate=pl.CostEstimate(flops=0, transcendentals=0, bytes_accessed=8 * local_rows * cells),
    )(snapshots)


def exchange(bit_pos, snapshots):
    chunks = 1 if bit_pos == 0 else CHUNKS
    rows_n = lax.axis_size("rows")
    local_rows, cells = snapshots.shape
    width = cells // rows_n
    piece = width // chunks

    sends = lay_out(snapshots, rows_n, chunks)

    def laid(chunk):
        return sends[chunk]

    def spread(sent):
        got = lax.all_to_all(sent, "rows", split_axis=0, concat_axis=0)
        return got.reshape(rows_n * local_rows, piece)

    own_parts = [spread(laid(0))]
    other_parts = []
    for chunk in range(1, chunks):
        held = (own_parts[-1], laid(chunk)) + tuple(other_parts[-1:])
        held = lax.optimization_barrier(held)
        own_parts[-1] = held[0]
        if other_parts:
            other_parts[-1] = held[2]
        other_parts.append(partner_2(held[0], "cols", bit_pos))
        own_parts.append(spread(held[1]))
    other_parts.append(partner_2(own_parts[-1], "cols", bit_pos))
    terms = None
    for mine, theirs in zip(own_parts, other_parts):
        part = pair_terms(mine, theirs)
        terms = part if terms is None else terms + part
    return jnp.concatenate(own_parts, 1), jnp.concatenate(other_parts, 1), terms


def assemble(terms, own_low):
    gram_mine, gram_mixed, gram_theirs = terms[0], terms[1], terms[2]
    upper_left = jnp.where(own_low, gram_mine, gram_theirs)
    lower_right = jnp.where(own_low, gram_theirs, gram_mine)
    upper_right = jnp.where(own_low, gram_mixed, gram_mixed.T)
    top_rows = jnp.concatenate([upper_left, upper_right], 1)
    bottom_rows = jnp.concatenate([upper_right.T, lower_right], 1)
    return jnp.concatenate([top_rows, bottom_rows], 0)


def rotate_kernel(coef_ref, mine_ref, theirs_ref, out_ref):
    stacked = jnp.concatenate([mine_ref[...], theirs_ref[...]], 0)
    out_ref[...] = jnp.dot(
        coef_ref[...], stacked, precision=lax.Precision.HIGHEST, preferred_element_type=jnp.float32
    )


def rotate_part(columns_sel, own_low, mine, theirs):
    width, cells = mine.shape
    coef_mine = jnp.where(own_low, columns_sel[:width], columns_sel[width:])
    coef_theirs = jnp.where(own_low, columns_sel[width:], columns_sel[:width])
    coef = jnp.concatenate([coef_mine, coef_theirs], 0).T
    tile = min(cells, 2048)
    coef_spec = pl.BlockSpec((width, 2 * width), lambda step: (0, 0))
    cell_spec = pl.BlockSpec((width, tile), lambda step: (0, step))
    return pl.pallas_call(
        rotate_kernel,
        out_shape=jax.ShapeDtypeStruct((width, cells), jnp.float32),
        grid=(cells // tile,),
        in_specs=[coef_spec, cell_spec, cell_spec],
        out_specs=cell_spec,
        cost_estimate=pl.CostEstimate(
            flops=4 * width * width * cells, transcendentals=0, bytes_accessed=12 * width * cells
        ),
    )(coef, mine, theirs)


def shards(snapshots, pair_table):
    bit_count = lax.axis_size("cols").bit_length() - 1
    column = lax.axis_index("cols")
    mask_val = pair_table[0]
    bit_index = jnp.int32(0)
    for bit_pos in range(bit_count):
        bit_index = bit_index + (mask_val >> bit_pos & 1) * bit_pos
    partner = jnp.bitwise_xor(column, mask_val)
    own_low = column < partner
    branches = [functools.partial(exchange, bit_pos) for bit_pos in range(bit_count)]
    own_parts, other_parts, terms = lax.switch(bit_index, branches, snapshots)
    gram_full = assemble(row_total(terms), own_low)
    rotation = jacobi_pallas(gram_full)
    width = own_parts.shape[0]
    own_columns = jnp.where(own_low, rotation[:, :width], rotation[:, width:])
    return rotate_part(own_columns, own_low, own_parts, other_parts)


def solution(mesh):
    in_specs = (P(("cols", "rows"), None), P())
    out_specs = P("cols", "rows")
    return jax.shard_map(shards, mesh=mesh, in_specs=in_specs, out_specs=out_specs, check_vma=False)
```

```python
import functools

import jax
import jax.numpy as jnp
import numpy as np
from jax import lax
from jax.experimental import pallas as pl
from jax.experimental.pallas import tpu as pltpu
from jax.sharding import PartitionSpec as P

ROUNDS = 8


def partner_2(value, axis, bit):
    mask = 2**bit
    pairs = [(source, source ^ mask) for source in range(lax.axis_size(axis))]
    return lax.ppermute(value, axis, pairs)


def jacobi_kernel(gram_ref, rotation_ref):
    highest = lax.Precision.HIGHEST
    order_dim = gram_ref.shape[0]
    last_idx = order_dim - 1
    width = order_dim // 2
    gram = gram_ref[...]
    row_col = lax.broadcasted_iota(jnp.int32, (order_dim, 1), 0)
    row_full = lax.broadcasted_iota(jnp.int32, (order_dim, order_dim), 0)
    col_full = lax.broadcasted_iota(jnp.int32, (order_dim, order_dim), 1)
    eye = row_full == col_full
    rotation = None
    for round_idx in range(ROUNDS):
        fixed = round_idx % last_idx
        mirror = 2 * fixed - row_col
        mirror = jnp.where(mirror < 0, mirror + last_idx, mirror)
        partner = jnp.where(row_col == fixed, last_idx, jnp.where(row_col == last_idx, fixed, mirror))
        offset = row_col - fixed
        offset = jnp.where(offset < 0, offset + last_idx, offset)
        is_first = (row_col == last_idx) | ((row_col != fixed) & (offset >= 1) & (offset <= width - 1))
        swap = (col_full == partner).astype(jnp.float32)
        on_diag = jnp.where(eye, gram, 0.0)
        diag_own = jnp.sum(on_diag, axis=1, keepdims=True)
        diag_row = jnp.sum(on_diag, axis=0, keepdims=True)
        diag_mate = jnp.sum(swap * diag_row, axis=1, keepdims=True)
        picked = gram * swap
        cross_second = jnp.sum(picked, axis=1, keepdims=True)
        cross_row = jnp.sum(picked, axis=0, keepdims=True)
        cross_first = jnp.sum(jnp.where(eye, cross_row, 0.0), axis=1, keepdims=True)
        cross_val = jnp.where(is_first, cross_first, cross_second)
        spread = jnp.where(is_first, diag_mate - diag_own, diag_own - diag_mate)
        hypot_val = jnp.sqrt(spread * spread + 4.0 * cross_val * cross_val)
        denom = jnp.sqrt(2.0 * hypot_val * (hypot_val + jnp.abs(spread)))
        sign_val = jnp.where(spread >= 0.0, 1.0, -1.0)
        cosine = (hypot_val + jnp.abs(spread)) / denom
        sine_val = 2.0 * cross_val * sign_val / denom
        signed = jnp.where(is_first, sine_val, -sine_val)
        diag_part = jnp.where(eye, cosine, 0.0)
        turn = diag_part + swap * signed
        turn_t = diag_part - swap * signed
        gram = jnp.dot(
            turn_t,
            jnp.dot(gram, turn, precision=highest, preferred_element_type=jnp.float32),
            precision=highest,
            preferred_element_type=jnp.float32,
        )
        rotation = turn if rotation is None else jnp.dot(
            rotation, turn, precision=highest, preferred_element_type=jnp.float32
        )
    rotation_ref[...] = rotation

def jacobi_pallas(gram):
    return pl.pallas_call(
        jacobi_kernel,
        out_shape=jax.ShapeDtypeStruct(gram.shape, jnp.float32),
        in_specs=[pl.BlockSpec(memory_space=pltpu.VMEM)],
        out_specs=pl.BlockSpec(memory_space=pltpu.VMEM),
    )(gram)


def gram_kernel(mine_ref, theirs_ref, out_ref, acc_ref):
    step = pl.program_id(0)

    @pl.when(step == 0)
    def _():
        acc_ref[...] = jnp.zeros_like(acc_ref)

    stacked = jnp.concatenate([mine_ref[...], theirs_ref[...]], 0)
    acc_ref[...] += lax.dot_general(
        stacked,
        stacked,
        (((1,), (1,)), ((), ())),
        precision=lax.Precision.HIGHEST,
        preferred_element_type=jnp.float32,
    )

    @pl.when(step == pl.num_programs(0) - 1)
    def _():
        width = mine_ref.shape[0]
        out_ref[0] = acc_ref[:width, :width]
        out_ref[1] = acc_ref[:width, width:]
        out_ref[2] = acc_ref[width:, width:]


def gram_store_kernel(mine_ref, theirs_ref, own_in, other_in, out_ref, own_ref, other_ref, acc_ref):
    del own_in, other_in
    gram_kernel(mine_ref, theirs_ref, out_ref, acc_ref)
    own_ref[...] = mine_ref[...]
    other_ref[...] = theirs_ref[...]


def pair_terms_stored(mine, theirs, own_full, other_full, chunk):
    width, piece = mine.shape
    cell_spec = pl.BlockSpec((width, piece), lambda step: (0, 0))
    full_spec = pl.BlockSpec((width, piece), lambda step: (0, chunk))
    return pl.pallas_call(
        gram_store_kernel,
        out_shape=[
            jax.ShapeDtypeStruct((3, width, width), jnp.float32),
            jax.ShapeDtypeStruct(own_full.shape, own_full.dtype),
            jax.ShapeDtypeStruct(other_full.shape, other_full.dtype),
        ],
        grid=(1,),
        in_specs=[cell_spec, cell_spec, pl.BlockSpec(memory_space=pl.ANY), pl.BlockSpec(memory_space=pl.ANY)],
        out_specs=[pl.BlockSpec((3, width, width), lambda step: (0, 0, 0)), full_spec, full_spec],
        scratch_shapes=[pltpu.VMEM((2 * width, 2 * width), jnp.float32)],
        input_output_aliases={2: 1, 3: 2},
        cost_estimate=pl.CostEstimate(
            flops=8 * width * width * piece, transcendentals=0, bytes_accessed=16 * width * piece
        ),
    )(mine, theirs, own_full, other_full)


def pair_terms(mine, theirs):
    width, cells = mine.shape
    tile = min(cells, 2048)
    cell_spec = pl.BlockSpec((width, tile), lambda step: (0, step))
    return pl.pallas_call(
        gram_kernel,
        out_shape=jax.ShapeDtypeStruct((3, width, width), jnp.float32),
        grid=(cells // tile,),
        in_specs=[cell_spec, cell_spec],
        out_specs=pl.BlockSpec((3, width, width), lambda step: (0, 0, 0)),
        scratch_shapes=[pltpu.VMEM((2 * width, 2 * width), jnp.float32)],
        cost_estimate=pl.CostEstimate(
            flops=8 * width * width * cells, transcendentals=0, bytes_accessed=8 * width * cells
        ),
    )(mine, theirs)


def row_total(part):
    count = lax.axis_size("rows")
    bit = 1
    while bit < count:
        pairs = [(source, source ^ bit) for source in range(count)]
        part = part + lax.ppermute(part, "rows", pairs)
        bit *= 2
    return part


CHUNKS = 4


def lay_kernel(source_ref, *out_refs):
    piece = out_refs[0].shape[-1]
    for chunk, out_ref in enumerate(out_refs):
        out_ref[...] = source_ref[:, chunk * piece : (chunk + 1) * piece]


def lay_out(snapshots, rows_n, chunks):
    local_rows, cells = snapshots.shape
    width = cells // rows_n
    piece = width // chunks
    out_spec = pl.BlockSpec((None, local_rows, piece), lambda dest: (dest, 0, 0))
    return pl.pallas_call(
        lay_kernel,
        out_shape=[jax.ShapeDtypeStruct((rows_n, local_rows, piece), snapshots.dtype)] * chunks,
        grid=(rows_n,),
        in_specs=[pl.BlockSpec((local_rows, width), lambda dest: (0, dest))],
        out_specs=[out_spec] * chunks,
        cost_estimate=pl.CostEstimate(flops=0, transcendentals=0, bytes_accessed=8 * local_rows * cells),
    )(snapshots)


def exchange(bit_pos, snapshots):
    chunks = 1 if bit_pos == 0 else CHUNKS
    rows_n = lax.axis_size("rows")
    local_rows, cells = snapshots.shape
    width = cells // rows_n
    piece = width // chunks

    sends = lay_out(snapshots, rows_n, chunks)

    def laid(chunk):
        return sends[chunk]

    def spread(sent):
        got = lax.all_to_all(sent, "rows", split_axis=0, concat_axis=0)
        return got.reshape(rows_n * local_rows, piece)

    own_parts = [spread(laid(0))]
    other_parts = []
    for chunk in range(1, chunks):
        held = (own_parts[-1], laid(chunk)) + tuple(other_parts[-1:])
        held = lax.optimization_barrier(held)
        own_parts[-1] = held[0]
        if other_parts:
            other_parts[-1] = held[2]
        other_parts.append(partner_2(held[0], "cols", bit_pos))
        own_parts.append(spread(held[1]))
    other_parts.append(partner_2(own_parts[-1], "cols", bit_pos))
    if chunks == 1:
        return own_parts[0], other_parts[0], pair_terms(own_parts[0], other_parts[0])
    own_full = jnp.zeros((rows_n * local_rows, width), snapshots.dtype)
    other_full = jnp.zeros((rows_n * local_rows, width), snapshots.dtype)
    terms = None
    for chunk, (mine, theirs) in enumerate(zip(own_parts, other_parts)):
        part, own_full, other_full = pair_terms_stored(mine, theirs, own_full, other_full, chunk)
        terms = part if terms is None else terms + part
    return own_full, other_full, terms


def assemble(terms, own_low):
    gram_mine, gram_mixed, gram_theirs = terms[0], terms[1], terms[2]
    upper_left = jnp.where(own_low, gram_mine, gram_theirs)
    lower_right = jnp.where(own_low, gram_theirs, gram_mine)
    upper_right = jnp.where(own_low, gram_mixed, gram_mixed.T)
    top_rows = jnp.concatenate([upper_left, upper_right], 1)
    bottom_rows = jnp.concatenate([upper_right.T, lower_right], 1)
    return jnp.concatenate([top_rows, bottom_rows], 0)


def rotate_kernel(coef_ref, mine_ref, theirs_ref, out_ref):
    stacked = jnp.concatenate([mine_ref[...], theirs_ref[...]], 0)
    out_ref[...] = jnp.dot(
        coef_ref[...], stacked, precision=lax.Precision.HIGHEST, preferred_element_type=jnp.float32
    )


def rotate_part(columns_sel, own_low, mine, theirs):
    width, cells = mine.shape
    coef_mine = jnp.where(own_low, columns_sel[:width], columns_sel[width:])
    coef_theirs = jnp.where(own_low, columns_sel[width:], columns_sel[:width])
    coef = jnp.concatenate([coef_mine, coef_theirs], 0).T
    tile = min(cells, 2048)
    coef_spec = pl.BlockSpec((width, 2 * width), lambda step: (0, 0))
    cell_spec = pl.BlockSpec((width, tile), lambda step: (0, step))
    return pl.pallas_call(
        rotate_kernel,
        out_shape=jax.ShapeDtypeStruct((width, cells), jnp.float32),
        grid=(cells // tile,),
        in_specs=[coef_spec, cell_spec, cell_spec],
        out_specs=cell_spec,
        cost_estimate=pl.CostEstimate(
            flops=4 * width * width * cells, transcendentals=0, bytes_accessed=12 * width * cells
        ),
    )(coef, mine, theirs)


def shards(snapshots, pair_table):
    bit_count = lax.axis_size("cols").bit_length() - 1
    column = lax.axis_index("cols")
    mask_val = pair_table[0]
    bit_index = jnp.int32(0)
    for bit_pos in range(bit_count):
        bit_index = bit_index + (mask_val >> bit_pos & 1) * bit_pos
    partner = jnp.bitwise_xor(column, mask_val)
    own_low = column < partner
    branches = [functools.partial(exchange, bit_pos) for bit_pos in range(bit_count)]
    own_parts, other_parts, terms = lax.switch(bit_index, branches, snapshots)
    gram_full = assemble(row_total(terms), own_low)
    rotation = jacobi_pallas(gram_full)
    width = own_parts.shape[0]
    own_columns = jnp.where(own_low, rotation[:, :width], rotation[:, width:])
    return rotate_part(own_columns, own_low, own_parts, other_parts)


def solution(mesh):
    in_specs = (P(("cols", "rows"), None), P())
    out_specs = P("cols", "rows")
    return jax.shard_map(shards, mesh=mesh, in_specs=in_specs, out_specs=out_specs, check_vma=False)
```

```python
import functools

import jax
import jax.numpy as jnp
import numpy as np
from jax import lax
from jax.experimental import pallas as pl
from jax.experimental.pallas import tpu as pltpu
from jax.sharding import PartitionSpec as P

ROUNDS = 8


def partner_2(value, axis, bit):
    mask = 2**bit
    pairs = [(source, source ^ mask) for source in range(lax.axis_size(axis))]
    return lax.ppermute(value, axis, pairs)


def jacobi_kernel(gram_ref, rotation_ref):
    highest = lax.Precision.HIGHEST
    order_dim = gram_ref.shape[0]
    last_idx = order_dim - 1
    width = order_dim // 2
    gram = gram_ref[...]
    row_col = lax.broadcasted_iota(jnp.int32, (order_dim, 1), 0)
    row_full = lax.broadcasted_iota(jnp.int32, (order_dim, order_dim), 0)
    col_full = lax.broadcasted_iota(jnp.int32, (order_dim, order_dim), 1)
    eye = row_full == col_full
    rotation = None
    for round_idx in range(ROUNDS):
        fixed = round_idx % last_idx
        mirror = 2 * fixed - row_col
        mirror = jnp.where(mirror < 0, mirror + last_idx, mirror)
        partner = jnp.where(row_col == fixed, last_idx, jnp.where(row_col == last_idx, fixed, mirror))
        offset = row_col - fixed
        offset = jnp.where(offset < 0, offset + last_idx, offset)
        is_first = (row_col == last_idx) | ((row_col != fixed) & (offset >= 1) & (offset <= width - 1))
        swap = (col_full == partner).astype(jnp.float32)
        on_diag = jnp.where(eye, gram, 0.0)
        diag_own = jnp.sum(on_diag, axis=1, keepdims=True)
        diag_row = jnp.sum(on_diag, axis=0, keepdims=True)
        diag_mate = jnp.sum(swap * diag_row, axis=1, keepdims=True)
        picked = gram * swap
        cross_second = jnp.sum(picked, axis=1, keepdims=True)
        cross_row = jnp.sum(picked, axis=0, keepdims=True)
        cross_first = jnp.sum(jnp.where(eye, cross_row, 0.0), axis=1, keepdims=True)
        cross_val = jnp.where(is_first, cross_first, cross_second)
        spread = jnp.where(is_first, diag_mate - diag_own, diag_own - diag_mate)
        hypot_val = jnp.sqrt(spread * spread + 4.0 * cross_val * cross_val)
        denom = jnp.sqrt(2.0 * hypot_val * (hypot_val + jnp.abs(spread)))
        sign_val = jnp.where(spread >= 0.0, 1.0, -1.0)
        cosine = (hypot_val + jnp.abs(spread)) / denom
        sine_val = 2.0 * cross_val * sign_val / denom
        signed = jnp.where(is_first, sine_val, -sine_val)
        diag_part = jnp.where(eye, cosine, 0.0)
        turn = diag_part + swap * signed
        turn_t = diag_part - swap * signed
        gram = jnp.dot(
            turn_t,
            jnp.dot(gram, turn, precision=highest, preferred_element_type=jnp.float32),
            precision=highest,
            preferred_element_type=jnp.float32,
        )
        rotation = turn if rotation is None else jnp.dot(
            rotation, turn, precision=highest, preferred_element_type=jnp.float32
        )
    rotation_ref[...] = rotation

def jacobi_pallas(gram):
    return pl.pallas_call(
        jacobi_kernel,
        out_shape=jax.ShapeDtypeStruct(gram.shape, jnp.float32),
        in_specs=[pl.BlockSpec(memory_space=pltpu.VMEM)],
        out_specs=pl.BlockSpec(memory_space=pltpu.VMEM),
    )(gram)


def gram_kernel(mine_ref, theirs_ref, out_ref, acc_ref):
    step = pl.program_id(0)

    @pl.when(step == 0)
    def _():
        acc_ref[...] = jnp.zeros_like(acc_ref)

    stacked = jnp.concatenate([mine_ref[...], theirs_ref[...]], 0)
    acc_ref[...] += lax.dot_general(
        stacked,
        stacked,
        (((1,), (1,)), ((), ())),
        precision=lax.Precision.HIGHEST,
        preferred_element_type=jnp.float32,
    )

    @pl.when(step == pl.num_programs(0) - 1)
    def _():
        width = mine_ref.shape[0]
        out_ref[0] = acc_ref[:width, :width]
        out_ref[1] = acc_ref[:width, width:]
        out_ref[2] = acc_ref[width:, width:]


def gram_store_kernel(mine_ref, theirs_ref, own_in, other_in, out_ref, own_ref, other_ref, acc_ref):
    del own_in, other_in
    gram_kernel(mine_ref, theirs_ref, out_ref, acc_ref)
    own_ref[...] = mine_ref[...]
    other_ref[...] = theirs_ref[...]


def pair_terms_stored(mine, theirs, own_full, other_full, chunk):
    width, piece = mine.shape
    cell_spec = pl.BlockSpec((width, piece), lambda step: (0, 0))
    full_spec = pl.BlockSpec((width, piece), lambda step: (0, chunk))
    return pl.pallas_call(
        gram_store_kernel,
        out_shape=[
            jax.ShapeDtypeStruct((3, width, width), jnp.float32),
            jax.ShapeDtypeStruct(own_full.shape, own_full.dtype),
            jax.ShapeDtypeStruct(other_full.shape, other_full.dtype),
        ],
        grid=(1,),
        in_specs=[cell_spec, cell_spec, pl.BlockSpec(memory_space=pl.ANY), pl.BlockSpec(memory_space=pl.ANY)],
        out_specs=[pl.BlockSpec((3, width, width), lambda step: (0, 0, 0)), full_spec, full_spec],
        scratch_shapes=[pltpu.VMEM((2 * width, 2 * width), jnp.float32)],
        input_output_aliases={2: 1, 3: 2},
        cost_estimate=pl.CostEstimate(
            flops=8 * width * width * piece, transcendentals=0, bytes_accessed=16 * width * piece
        ),
    )(mine, theirs, own_full, other_full)


def pair_terms(mine, theirs):
    width, cells = mine.shape
    tile = min(cells, 2048)
    cell_spec = pl.BlockSpec((width, tile), lambda step: (0, step))
    return pl.pallas_call(
        gram_kernel,
        out_shape=jax.ShapeDtypeStruct((3, width, width), jnp.float32),
        grid=(cells // tile,),
        in_specs=[cell_spec, cell_spec],
        out_specs=pl.BlockSpec((3, width, width), lambda step: (0, 0, 0)),
        scratch_shapes=[pltpu.VMEM((2 * width, 2 * width), jnp.float32)],
        cost_estimate=pl.CostEstimate(
            flops=8 * width * width * cells, transcendentals=0, bytes_accessed=8 * width * cells
        ),
    )(mine, theirs)


def row_total(part):
    count = lax.axis_size("rows")
    bit = 1
    while bit < count:
        pairs = [(source, source ^ bit) for source in range(count)]
        part = part + lax.ppermute(part, "rows", pairs)
        bit *= 2
    return part


CHUNKS = 4


def lay_kernel(source_ref, *out_refs):
    piece = out_refs[0].shape[-1]
    for chunk, out_ref in enumerate(out_refs):
        out_ref[...] = source_ref[:, chunk * piece : (chunk + 1) * piece]


def lay_out(snapshots, rows_n, chunks):
    local_rows, cells = snapshots.shape
    width = cells // rows_n
    piece = width // chunks
    out_spec = pl.BlockSpec((None, local_rows, piece), lambda dest: (dest, 0, 0))
    return pl.pallas_call(
        lay_kernel,
        out_shape=[jax.ShapeDtypeStruct((rows_n, local_rows, piece), snapshots.dtype)] * chunks,
        grid=(rows_n,),
        in_specs=[pl.BlockSpec((local_rows, width), lambda dest: (0, dest))],
        out_specs=[out_spec] * chunks,
        cost_estimate=pl.CostEstimate(flops=0, transcendentals=0, bytes_accessed=8 * local_rows * cells),
    )(snapshots)


def exchange(bit_pos, snapshots):
    chunks = 1 if bit_pos == 0 else CHUNKS
    rows_n = lax.axis_size("rows")
    local_rows, cells = snapshots.shape
    width = cells // rows_n
    piece = width // chunks

    sends = lay_out(snapshots, rows_n, chunks)

    def laid(chunk):
        return sends[chunk]

    def spread(sent):
        got = lax.all_to_all(sent, "rows", split_axis=0, concat_axis=0)
        return got.reshape(rows_n * local_rows, piece)

    own_parts = [spread(laid(0))]
    other_parts = []
    for chunk in range(1, chunks):
        held = (own_parts[-1], laid(chunk)) + tuple(other_parts[-1:])
        held = lax.optimization_barrier(held)
        own_parts[-1] = held[0]
        if other_parts:
            other_parts[-1] = held[2]
        other_parts.append(partner_2(held[0], "cols", bit_pos))
        own_parts.append(spread(held[1]))
    other_parts.append(partner_2(own_parts[-1], "cols", bit_pos))
    if chunks == 1:
        return own_parts[0], other_parts[0], pair_terms(own_parts[0], other_parts[0])
    own_full = jnp.zeros((rows_n * local_rows, width), snapshots.dtype)
    other_full = jnp.zeros((rows_n * local_rows, width), snapshots.dtype)
    terms = None
    for chunk, (mine, theirs) in enumerate(zip(own_parts, other_parts)):
        part, own_full, other_full = pair_terms_stored(mine, theirs, own_full, other_full, chunk)
        terms = part if terms is None else terms + part
    return own_full, other_full, terms


def pack_terms(terms):
    width = terms.shape[1]
    row = lax.broadcasted_iota(jnp.int32, (width, width), 0)
    col = lax.broadcasted_iota(jnp.int32, (width, width), 1)
    shared = jnp.where(row <= col, terms[0], terms[2])
    diag_theirs = jnp.sum(jnp.where(row == col, terms[2], 0.0), axis=0, keepdims=True)
    return jnp.concatenate([shared, terms[1], jnp.broadcast_to(diag_theirs, (8, width))], 0)


def unpack_terms(packed, width):
    row = lax.broadcasted_iota(jnp.int32, (width, width), 0)
    col = lax.broadcasted_iota(jnp.int32, (width, width), 1)
    shared = packed[:width]
    gram_mixed = packed[width : 2 * width]
    diag_theirs = packed[2 * width : 2 * width + 1]
    gram_mine = jnp.where(row <= col, shared, shared.T)
    gram_theirs = jnp.where(row > col, shared, jnp.where(row < col, shared.T, diag_theirs))
    return gram_mine, gram_mixed, gram_theirs


def assemble(terms, own_low):
    gram_mine, gram_mixed, gram_theirs = unpack_terms(row_total(pack_terms(terms)), terms.shape[1])
    upper_left = jnp.where(own_low, gram_mine, gram_theirs)
    lower_right = jnp.where(own_low, gram_theirs, gram_mine)
    upper_right = jnp.where(own_low, gram_mixed, gram_mixed.T)
    top_rows = jnp.concatenate([upper_left, upper_right], 1)
    bottom_rows = jnp.concatenate([upper_right.T, lower_right], 1)
    return jnp.concatenate([top_rows, bottom_rows], 0)


def rotate_kernel(coef_ref, mine_ref, theirs_ref, out_ref):
    stacked = jnp.concatenate([mine_ref[...], theirs_ref[...]], 0)
    out_ref[...] = jnp.dot(
        coef_ref[...], stacked, precision=lax.Precision.HIGHEST, preferred_element_type=jnp.float32
    )


def rotate_part(columns_sel, own_low, mine, theirs):
    width, cells = mine.shape
    coef_mine = jnp.where(own_low, columns_sel[:width], columns_sel[width:])
    coef_theirs = jnp.where(own_low, columns_sel[width:], columns_sel[:width])
    coef = jnp.concatenate([coef_mine, coef_theirs], 0).T
    tile = min(cells, 2048)
    coef_spec = pl.BlockSpec((width, 2 * width), lambda step: (0, 0))
    cell_spec = pl.BlockSpec((width, tile), lambda step: (0, step))
    return pl.pallas_call(
        rotate_kernel,
        out_shape=jax.ShapeDtypeStruct((width, cells), jnp.float32),
        grid=(cells // tile,),
        in_specs=[coef_spec, cell_spec, cell_spec],
        out_specs=cell_spec,
        cost_estimate=pl.CostEstimate(
            flops=4 * width * width * cells, transcendentals=0, bytes_accessed=12 * width * cells
        ),
    )(coef, mine, theirs)


def shards(snapshots, pair_table):
    bit_count = lax.axis_size("cols").bit_length() - 1
    column = lax.axis_index("cols")
    mask_val = pair_table[0]
    bit_index = jnp.int32(0)
    for bit_pos in range(bit_count):
        bit_index = bit_index + (mask_val >> bit_pos & 1) * bit_pos
    partner = jnp.bitwise_xor(column, mask_val)
    own_low = column < partner
    branches = [functools.partial(exchange, bit_pos) for bit_pos in range(bit_count)]
    own_parts, other_parts, terms = lax.switch(bit_index, branches, snapshots)
    gram_full = assemble(terms, own_low)
    rotation = jacobi_pallas(gram_full)
    width = own_parts.shape[0]
    own_columns = jnp.where(own_low, rotation[:, :width], rotation[:, width:])
    return rotate_part(own_columns, own_low, own_parts, other_parts)


def solution(mesh):
    in_specs = (P(("cols", "rows"), None), P())
    out_specs = P("cols", "rows")
    return jax.shard_map(shards, mesh=mesh, in_specs=in_specs, out_specs=out_specs, check_vma=False)
```

```python
import functools

import jax
import jax.numpy as jnp
import numpy as np
from jax import lax
from jax.experimental import pallas as pl
from jax.experimental.pallas import tpu as pltpu
from jax.sharding import PartitionSpec as P

ROUNDS = 8


def partner_2(value, axis, bit):
    mask = 2**bit
    pairs = [(source, source ^ mask) for source in range(lax.axis_size(axis))]
    return lax.ppermute(value, axis, pairs)


def jacobi_kernel(gram_ref, rotation_ref):
    highest = lax.Precision.HIGHEST
    order_dim = gram_ref.shape[0]
    last_idx = order_dim - 1
    width = order_dim // 2
    gram = gram_ref[...]
    row_col = lax.broadcasted_iota(jnp.int32, (order_dim, 1), 0)
    row_full = lax.broadcasted_iota(jnp.int32, (order_dim, order_dim), 0)
    col_full = lax.broadcasted_iota(jnp.int32, (order_dim, order_dim), 1)
    eye = row_full == col_full
    rotation = None
    for round_idx in range(ROUNDS):
        fixed = round_idx % last_idx
        mirror = 2 * fixed - row_col
        mirror = jnp.where(mirror < 0, mirror + last_idx, mirror)
        partner = jnp.where(row_col == fixed, last_idx, jnp.where(row_col == last_idx, fixed, mirror))
        offset = row_col - fixed
        offset = jnp.where(offset < 0, offset + last_idx, offset)
        is_first = (row_col == last_idx) | ((row_col != fixed) & (offset >= 1) & (offset <= width - 1))
        swap = (col_full == partner).astype(jnp.float32)
        on_diag = jnp.where(eye, gram, 0.0)
        diag_own = jnp.sum(on_diag, axis=1, keepdims=True)
        diag_row = jnp.sum(on_diag, axis=0, keepdims=True)
        diag_mate = jnp.sum(swap * diag_row, axis=1, keepdims=True)
        picked = gram * swap
        cross_second = jnp.sum(picked, axis=1, keepdims=True)
        cross_row = jnp.sum(picked, axis=0, keepdims=True)
        cross_first = jnp.sum(jnp.where(eye, cross_row, 0.0), axis=1, keepdims=True)
        cross_val = jnp.where(is_first, cross_first, cross_second)
        spread = jnp.where(is_first, diag_mate - diag_own, diag_own - diag_mate)
        hypot_val = jnp.sqrt(spread * spread + 4.0 * cross_val * cross_val)
        denom = jnp.sqrt(2.0 * hypot_val * (hypot_val + jnp.abs(spread)))
        sign_val = jnp.where(spread >= 0.0, 1.0, -1.0)
        cosine = (hypot_val + jnp.abs(spread)) / denom
        sine_val = 2.0 * cross_val * sign_val / denom
        signed = jnp.where(is_first, sine_val, -sine_val)
        diag_part = jnp.where(eye, cosine, 0.0)
        turn = diag_part + swap * signed
        turn_t = diag_part - swap * signed
        gram = jnp.dot(
            turn_t,
            jnp.dot(gram, turn, precision=highest, preferred_element_type=jnp.float32),
            precision=highest,
            preferred_element_type=jnp.float32,
        )
        rotation = turn if rotation is None else jnp.dot(
            rotation, turn, precision=highest, preferred_element_type=jnp.float32
        )
    rotation_ref[...] = rotation

def jacobi_pallas(gram):
    return pl.pallas_call(
        jacobi_kernel,
        out_shape=jax.ShapeDtypeStruct(gram.shape, jnp.float32),
        in_specs=[pl.BlockSpec(memory_space=pltpu.VMEM)],
        out_specs=pl.BlockSpec(memory_space=pltpu.VMEM),
    )(gram)


def gram_kernel(mine_ref, theirs_ref, out_ref, acc_ref):
    step = pl.program_id(0)

    @pl.when(step == 0)
    def _():
        acc_ref[...] = jnp.zeros_like(acc_ref)

    stacked = jnp.concatenate([mine_ref[...], theirs_ref[...]], 0)
    acc_ref[...] += lax.dot_general(
        stacked,
        stacked,
        (((1,), (1,)), ((), ())),
        precision=lax.Precision.HIGHEST,
        preferred_element_type=jnp.float32,
    )

    @pl.when(step == pl.num_programs(0) - 1)
    def _():
        width = mine_ref.shape[0]
        row = lax.broadcasted_iota(jnp.int32, (width, width), 0)
        col = lax.broadcasted_iota(jnp.int32, (width, width), 1)
        gram_theirs = acc_ref[width:, width:]
        out_ref[:width, :] = jnp.where(row <= col, acc_ref[:width, :width], gram_theirs)
        out_ref[width : 2 * width, :] = acc_ref[:width, width:]
        diag_theirs = jnp.sum(jnp.where(row == col, gram_theirs, 0.0), axis=0, keepdims=True)
        out_ref[2 * width :, :] = jnp.broadcast_to(diag_theirs, (8, width))


def gram_store_kernel(mine_ref, theirs_ref, own_in, other_in, out_ref, own_ref, other_ref, acc_ref):
    del own_in, other_in
    gram_kernel(mine_ref, theirs_ref, out_ref, acc_ref)
    own_ref[...] = mine_ref[...]
    other_ref[...] = theirs_ref[...]


def pair_terms_stored(mine, theirs, own_full, other_full, chunk):
    width, piece = mine.shape
    cell_spec = pl.BlockSpec((width, piece), lambda step: (0, 0))
    full_spec = pl.BlockSpec((width, piece), lambda step: (0, chunk))
    return pl.pallas_call(
        gram_store_kernel,
        out_shape=[
            jax.ShapeDtypeStruct((2 * width + 8, width), jnp.float32),
            jax.ShapeDtypeStruct(own_full.shape, own_full.dtype),
            jax.ShapeDtypeStruct(other_full.shape, other_full.dtype),
        ],
        grid=(1,),
        in_specs=[cell_spec, cell_spec, pl.BlockSpec(memory_space=pl.ANY), pl.BlockSpec(memory_space=pl.ANY)],
        out_specs=[pl.BlockSpec((2 * width + 8, width), lambda step: (0, 0)), full_spec, full_spec],
        scratch_shapes=[pltpu.VMEM((2 * width, 2 * width), jnp.float32)],
        input_output_aliases={2: 1, 3: 2},
        cost_estimate=pl.CostEstimate(
            flops=8 * width * width * piece, transcendentals=0, bytes_accessed=16 * width * piece
        ),
    )(mine, theirs, own_full, other_full)


def pair_terms(mine, theirs):
    width, cells = mine.shape
    tile = min(cells, 2048)
    cell_spec = pl.BlockSpec((width, tile), lambda step: (0, step))
    return pl.pallas_call(
        gram_kernel,
        out_shape=jax.ShapeDtypeStruct((2 * width + 8, width), jnp.float32),
        grid=(cells // tile,),
        in_specs=[cell_spec, cell_spec],
        out_specs=pl.BlockSpec((2 * width + 8, width), lambda step: (0, 0)),
        scratch_shapes=[pltpu.VMEM((2 * width, 2 * width), jnp.float32)],
        cost_estimate=pl.CostEstimate(
            flops=8 * width * width * cells, transcendentals=0, bytes_accessed=8 * width * cells
        ),
    )(mine, theirs)


def row_total(part):
    count = lax.axis_size("rows")
    bit = 1
    while bit < count:
        pairs = [(source, source ^ bit) for source in range(count)]
        part = part + lax.ppermute(part, "rows", pairs)
        bit *= 2
    return part


CHUNKS = 4


def lay_kernel(source_ref, *out_refs):
    piece = out_refs[0].shape[-1]
    for chunk, out_ref in enumerate(out_refs):
        out_ref[...] = source_ref[:, chunk * piece : (chunk + 1) * piece]


def lay_out(snapshots, rows_n, chunks):
    local_rows, cells = snapshots.shape
    width = cells // rows_n
    piece = width // chunks
    out_spec = pl.BlockSpec((None, local_rows, piece), lambda dest: (dest, 0, 0))
    return pl.pallas_call(
        lay_kernel,
        out_shape=[jax.ShapeDtypeStruct((rows_n, local_rows, piece), snapshots.dtype)] * chunks,
        grid=(rows_n,),
        in_specs=[pl.BlockSpec((local_rows, width), lambda dest: (0, dest))],
        out_specs=[out_spec] * chunks,
        cost_estimate=pl.CostEstimate(flops=0, transcendentals=0, bytes_accessed=8 * local_rows * cells),
    )(snapshots)


def exchange(bit_pos, snapshots):
    chunks = 1 if bit_pos == 0 else CHUNKS
    rows_n = lax.axis_size("rows")
    local_rows, cells = snapshots.shape
    width = cells // rows_n
    piece = width // chunks

    sends = lay_out(snapshots, rows_n, chunks)

    def laid(chunk):
        return sends[chunk]

    def spread(sent):
        got = lax.all_to_all(sent, "rows", split_axis=0, concat_axis=0)
        return got.reshape(rows_n * local_rows, piece)

    own_parts = [spread(laid(0))]
    other_parts = []
    for chunk in range(1, chunks):
        held = (own_parts[-1], laid(chunk)) + tuple(other_parts[-1:])
        held = lax.optimization_barrier(held)
        own_parts[-1] = held[0]
        if other_parts:
            other_parts[-1] = held[2]
        other_parts.append(partner_2(held[0], "cols", bit_pos))
        own_parts.append(spread(held[1]))
    other_parts.append(partner_2(own_parts[-1], "cols", bit_pos))
    if chunks == 1:
        return own_parts[0], other_parts[0], pair_terms(own_parts[0], other_parts[0])
    own_full = jnp.zeros((rows_n * local_rows, width), snapshots.dtype)
    other_full = jnp.zeros((rows_n * local_rows, width), snapshots.dtype)
    terms = None
    for chunk, (mine, theirs) in enumerate(zip(own_parts, other_parts)):
        part, own_full, other_full = pair_terms_stored(mine, theirs, own_full, other_full, chunk)
        terms = part if terms is None else terms + part
    return own_full, other_full, terms


def unpack_terms(packed, width):
    row = lax.broadcasted_iota(jnp.int32, (width, width), 0)
    col = lax.broadcasted_iota(jnp.int32, (width, width), 1)
    shared = packed[:width]
    gram_mixed = packed[width : 2 * width]
    diag_theirs = packed[2 * width : 2 * width + 1]
    gram_mine = jnp.where(row <= col, shared, shared.T)
    gram_theirs = jnp.where(row > col, shared, jnp.where(row < col, shared.T, diag_theirs))
    return gram_mine, gram_mixed, gram_theirs


def assemble(terms, own_low):
    gram_mine, gram_mixed, gram_theirs = unpack_terms(row_total(terms), terms.shape[1])
    upper_left = jnp.where(own_low, gram_mine, gram_theirs)
    lower_right = jnp.where(own_low, gram_theirs, gram_mine)
    upper_right = jnp.where(own_low, gram_mixed, gram_mixed.T)
    top_rows = jnp.concatenate([upper_left, upper_right], 1)
    bottom_rows = jnp.concatenate([upper_right.T, lower_right], 1)
    return jnp.concatenate([top_rows, bottom_rows], 0)


def rotate_kernel(coef_ref, mine_ref, theirs_ref, out_ref):
    stacked = jnp.concatenate([mine_ref[...], theirs_ref[...]], 0)
    out_ref[...] = jnp.dot(
        coef_ref[...], stacked, precision=lax.Precision.HIGHEST, preferred_element_type=jnp.float32
    )


def rotate_part(columns_sel, own_low, mine, theirs):
    width, cells = mine.shape
    coef_mine = jnp.where(own_low, columns_sel[:width], columns_sel[width:])
    coef_theirs = jnp.where(own_low, columns_sel[width:], columns_sel[:width])
    coef = jnp.concatenate([coef_mine, coef_theirs], 0).T
    tile = min(cells, 2048)
    coef_spec = pl.BlockSpec((width, 2 * width), lambda step: (0, 0))
    cell_spec = pl.BlockSpec((width, tile), lambda step: (0, step))
    return pl.pallas_call(
        rotate_kernel,
        out_shape=jax.ShapeDtypeStruct((width, cells), jnp.float32),
        grid=(cells // tile,),
        in_specs=[coef_spec, cell_spec, cell_spec],
        out_specs=cell_spec,
        cost_estimate=pl.CostEstimate(
            flops=4 * width * width * cells, transcendentals=0, bytes_accessed=12 * width * cells
        ),
    )(coef, mine, theirs)


def shards(snapshots, pair_table):
    bit_count = lax.axis_size("cols").bit_length() - 1
    column = lax.axis_index("cols")
    mask_val = pair_table[0]
    bit_index = jnp.int32(0)
    for bit_pos in range(bit_count):
        bit_index = bit_index + (mask_val >> bit_pos & 1) * bit_pos
    partner = jnp.bitwise_xor(column, mask_val)
    own_low = column < partner
    branches = [functools.partial(exchange, bit_pos) for bit_pos in range(bit_count)]
    own_parts, other_parts, terms = lax.switch(bit_index, branches, snapshots)
    gram_full = assemble(terms, own_low)
    rotation = jacobi_pallas(gram_full)
    width = own_parts.shape[0]
    own_columns = jnp.where(own_low, rotation[:, :width], rotation[:, width:])
    return rotate_part(own_columns, own_low, own_parts, other_parts)


def solution(mesh):
    in_specs = (P(("cols", "rows"), None), P())
    out_specs = P("cols", "rows")
    return jax.shard_map(shards, mesh=mesh, in_specs=in_specs, out_specs=out_specs, check_vma=False)
```

```python
import functools

import jax
import jax.numpy as jnp
import numpy as np
from jax import lax
from jax.experimental import pallas as pl
from jax.experimental.pallas import tpu as pltpu
from jax.sharding import PartitionSpec as P

ROUNDS = 8


def partner_2(value, axis, bit):
    mask = 2**bit
    pairs = [(source, source ^ mask) for source in range(lax.axis_size(axis))]
    return lax.ppermute(value, axis, pairs)


def jacobi_kernel(gram_ref, rotation_ref):
    highest = lax.Precision.HIGHEST
    order_dim = gram_ref.shape[0]
    last_idx = order_dim - 1
    width = order_dim // 2
    gram = gram_ref[...]
    row_col = lax.broadcasted_iota(jnp.int32, (order_dim, 1), 0)
    row_full = lax.broadcasted_iota(jnp.int32, (order_dim, order_dim), 0)
    col_full = lax.broadcasted_iota(jnp.int32, (order_dim, order_dim), 1)
    eye = row_full == col_full
    rotation = None
    for round_idx in range(ROUNDS):
        fixed = round_idx % last_idx
        mirror = 2 * fixed - row_col
        mirror = jnp.where(mirror < 0, mirror + last_idx, mirror)
        partner = jnp.where(row_col == fixed, last_idx, jnp.where(row_col == last_idx, fixed, mirror))
        offset = row_col - fixed
        offset = jnp.where(offset < 0, offset + last_idx, offset)
        is_first = (row_col == last_idx) | ((row_col != fixed) & (offset >= 1) & (offset <= width - 1))
        swap = (col_full == partner).astype(jnp.float32)
        on_diag = jnp.where(eye, gram, 0.0)
        diag_own = jnp.sum(on_diag, axis=1, keepdims=True)
        diag_row = jnp.sum(on_diag, axis=0, keepdims=True)
        diag_mate = jnp.sum(swap * diag_row, axis=1, keepdims=True)
        picked = gram * swap
        cross_second = jnp.sum(picked, axis=1, keepdims=True)
        cross_row = jnp.sum(picked, axis=0, keepdims=True)
        cross_first = jnp.sum(jnp.where(eye, cross_row, 0.0), axis=1, keepdims=True)
        cross_val = jnp.where(is_first, cross_first, cross_second)
        spread = jnp.where(is_first, diag_mate - diag_own, diag_own - diag_mate)
        hypot_val = jnp.sqrt(spread * spread + 4.0 * cross_val * cross_val)
        denom = jnp.sqrt(2.0 * hypot_val * (hypot_val + jnp.abs(spread)))
        sign_val = jnp.where(spread >= 0.0, 1.0, -1.0)
        cosine = (hypot_val + jnp.abs(spread)) / denom
        sine_val = 2.0 * cross_val * sign_val / denom
        signed = jnp.where(is_first, sine_val, -sine_val)
        diag_part = jnp.where(eye, cosine, 0.0)
        turn = diag_part + swap * signed
        turn_t = diag_part - swap * signed
        gram = jnp.dot(
            turn_t,
            jnp.dot(gram, turn, precision=highest, preferred_element_type=jnp.float32),
            precision=highest,
            preferred_element_type=jnp.float32,
        )
        rotation = turn if rotation is None else jnp.dot(
            rotation, turn, precision=lax.Precision.HIGH, preferred_element_type=jnp.float32
        )
    rotation_ref[...] = rotation

def jacobi_pallas(gram):
    return pl.pallas_call(
        jacobi_kernel,
        out_shape=jax.ShapeDtypeStruct(gram.shape, jnp.float32),
        in_specs=[pl.BlockSpec(memory_space=pltpu.VMEM)],
        out_specs=pl.BlockSpec(memory_space=pltpu.VMEM),
    )(gram)


def gram_kernel(mine_ref, theirs_ref, out_ref, acc_ref):
    step = pl.program_id(0)

    @pl.when(step == 0)
    def _():
        acc_ref[...] = jnp.zeros_like(acc_ref)

    stacked = jnp.concatenate([mine_ref[...], theirs_ref[...]], 0)
    acc_ref[...] += lax.dot_general(
        stacked,
        stacked,
        (((1,), (1,)), ((), ())),
        precision=lax.Precision.HIGHEST,
        preferred_element_type=jnp.float32,
    )

    @pl.when(step == pl.num_programs(0) - 1)
    def _():
        width = mine_ref.shape[0]
        row = lax.broadcasted_iota(jnp.int32, (width, width), 0)
        col = lax.broadcasted_iota(jnp.int32, (width, width), 1)
        gram_theirs = acc_ref[width:, width:]
        out_ref[:width, :] = jnp.where(row <= col, acc_ref[:width, :width], gram_theirs)
        out_ref[width : 2 * width, :] = acc_ref[:width, width:]
        diag_theirs = jnp.sum(jnp.where(row == col, gram_theirs, 0.0), axis=0, keepdims=True)
        out_ref[2 * width :, :] = jnp.broadcast_to(diag_theirs, (8, width))


def gram_store_kernel(mine_ref, theirs_ref, own_in, other_in, out_ref, own_ref, other_ref, acc_ref):
    del own_in, other_in
    gram_kernel(mine_ref, theirs_ref, out_ref, acc_ref)
    own_ref[...] = mine_ref[...]
    other_ref[...] = theirs_ref[...]


def pair_terms_stored(mine, theirs, own_full, other_full, chunk):
    width, piece = mine.shape
    cell_spec = pl.BlockSpec((width, piece), lambda step: (0, 0))
    full_spec = pl.BlockSpec((width, piece), lambda step: (0, chunk))
    return pl.pallas_call(
        gram_store_kernel,
        out_shape=[
            jax.ShapeDtypeStruct((2 * width + 8, width), jnp.float32),
            jax.ShapeDtypeStruct(own_full.shape, own_full.dtype),
            jax.ShapeDtypeStruct(other_full.shape, other_full.dtype),
        ],
        grid=(1,),
        in_specs=[cell_spec, cell_spec, pl.BlockSpec(memory_space=pl.ANY), pl.BlockSpec(memory_space=pl.ANY)],
        out_specs=[pl.BlockSpec((2 * width + 8, width), lambda step: (0, 0)), full_spec, full_spec],
        scratch_shapes=[pltpu.VMEM((2 * width, 2 * width), jnp.float32)],
        input_output_aliases={2: 1, 3: 2},
        cost_estimate=pl.CostEstimate(
            flops=8 * width * width * piece, transcendentals=0, bytes_accessed=16 * width * piece
        ),
    )(mine, theirs, own_full, other_full)


def pair_terms(mine, theirs):
    width, cells = mine.shape
    tile = min(cells, 2048)
    cell_spec = pl.BlockSpec((width, tile), lambda step: (0, step))
    return pl.pallas_call(
        gram_kernel,
        out_shape=jax.ShapeDtypeStruct((2 * width + 8, width), jnp.float32),
        grid=(cells // tile,),
        in_specs=[cell_spec, cell_spec],
        out_specs=pl.BlockSpec((2 * width + 8, width), lambda step: (0, 0)),
        scratch_shapes=[pltpu.VMEM((2 * width, 2 * width), jnp.float32)],
        cost_estimate=pl.CostEstimate(
            flops=8 * width * width * cells, transcendentals=0, bytes_accessed=8 * width * cells
        ),
    )(mine, theirs)


def row_total(part):
    count = lax.axis_size("rows")
    bit = 1
    while bit < count:
        pairs = [(source, source ^ bit) for source in range(count)]
        part = part + lax.ppermute(part, "rows", pairs)
        bit *= 2
    return part


CHUNKS = 4


def lay_kernel(source_ref, *out_refs):
    piece = out_refs[0].shape[-1]
    for chunk, out_ref in enumerate(out_refs):
        out_ref[...] = source_ref[:, chunk * piece : (chunk + 1) * piece]


def lay_out(snapshots, rows_n, chunks):
    local_rows, cells = snapshots.shape
    width = cells // rows_n
    piece = width // chunks
    out_spec = pl.BlockSpec((None, local_rows, piece), lambda dest: (dest, 0, 0))
    return pl.pallas_call(
        lay_kernel,
        out_shape=[jax.ShapeDtypeStruct((rows_n, local_rows, piece), snapshots.dtype)] * chunks,
        grid=(rows_n,),
        in_specs=[pl.BlockSpec((local_rows, width), lambda dest: (0, dest))],
        out_specs=[out_spec] * chunks,
        cost_estimate=pl.CostEstimate(flops=0, transcendentals=0, bytes_accessed=8 * local_rows * cells),
    )(snapshots)


def exchange(bit_pos, snapshots):
    chunks = 1 if bit_pos == 0 else CHUNKS
    rows_n = lax.axis_size("rows")
    local_rows, cells = snapshots.shape
    width = cells // rows_n
    piece = width // chunks

    sends = lay_out(snapshots, rows_n, chunks)

    def laid(chunk):
        return sends[chunk]

    def spread(sent):
        got = lax.all_to_all(sent, "rows", split_axis=0, concat_axis=0)
        return got.reshape(rows_n * local_rows, piece)

    own_parts = [spread(laid(0))]
    other_parts = []
    for chunk in range(1, chunks):
        held = (own_parts[-1], laid(chunk)) + tuple(other_parts[-1:])
        held = lax.optimization_barrier(held)
        own_parts[-1] = held[0]
        if other_parts:
            other_parts[-1] = held[2]
        other_parts.append(partner_2(held[0], "cols", bit_pos))
        own_parts.append(spread(held[1]))
    other_parts.append(partner_2(own_parts[-1], "cols", bit_pos))
    if chunks == 1:
        return own_parts[0], other_parts[0], pair_terms(own_parts[0], other_parts[0])
    own_full = jnp.zeros((rows_n * local_rows, width), snapshots.dtype)
    other_full = jnp.zeros((rows_n * local_rows, width), snapshots.dtype)
    terms = None
    for chunk, (mine, theirs) in enumerate(zip(own_parts, other_parts)):
        part, own_full, other_full = pair_terms_stored(mine, theirs, own_full, other_full, chunk)
        terms = part if terms is None else terms + part
    return own_full, other_full, terms


def unpack_terms(packed, width):
    row = lax.broadcasted_iota(jnp.int32, (width, width), 0)
    col = lax.broadcasted_iota(jnp.int32, (width, width), 1)
    shared = packed[:width]
    gram_mixed = packed[width : 2 * width]
    diag_theirs = packed[2 * width : 2 * width + 1]
    gram_mine = jnp.where(row <= col, shared, shared.T)
    gram_theirs = jnp.where(row > col, shared, jnp.where(row < col, shared.T, diag_theirs))
    return gram_mine, gram_mixed, gram_theirs


def assemble(terms, own_low):
    gram_mine, gram_mixed, gram_theirs = unpack_terms(row_total(terms), terms.shape[1])
    upper_left = jnp.where(own_low, gram_mine, gram_theirs)
    lower_right = jnp.where(own_low, gram_theirs, gram_mine)
    upper_right = jnp.where(own_low, gram_mixed, gram_mixed.T)
    top_rows = jnp.concatenate([upper_left, upper_right], 1)
    bottom_rows = jnp.concatenate([upper_right.T, lower_right], 1)
    return jnp.concatenate([top_rows, bottom_rows], 0)


def rotate_kernel(coef_ref, mine_ref, theirs_ref, out_ref):
    stacked = jnp.concatenate([mine_ref[...], theirs_ref[...]], 0)
    out_ref[...] = jnp.dot(
        coef_ref[...], stacked, precision=lax.Precision.HIGH, preferred_element_type=jnp.float32
    )


def rotate_part(columns_sel, own_low, mine, theirs):
    width, cells = mine.shape
    coef_mine = jnp.where(own_low, columns_sel[:width], columns_sel[width:])
    coef_theirs = jnp.where(own_low, columns_sel[width:], columns_sel[:width])
    coef = jnp.concatenate([coef_mine, coef_theirs], 0).T
    tile = min(cells, 2048)
    coef_spec = pl.BlockSpec((width, 2 * width), lambda step: (0, 0))
    cell_spec = pl.BlockSpec((width, tile), lambda step: (0, step))
    return pl.pallas_call(
        rotate_kernel,
        out_shape=jax.ShapeDtypeStruct((width, cells), jnp.float32),
        grid=(cells // tile,),
        in_specs=[coef_spec, cell_spec, cell_spec],
        out_specs=cell_spec,
        cost_estimate=pl.CostEstimate(
            flops=4 * width * width * cells, transcendentals=0, bytes_accessed=12 * width * cells
        ),
    )(coef, mine, theirs)


def shards(snapshots, pair_table):
    bit_count = lax.axis_size("cols").bit_length() - 1
    column = lax.axis_index("cols")
    mask_val = pair_table[0]
    bit_index = jnp.int32(0)
    for bit_pos in range(bit_count):
        bit_index = bit_index + (mask_val >> bit_pos & 1) * bit_pos
    partner = jnp.bitwise_xor(column, mask_val)
    own_low = column < partner
    branches = [functools.partial(exchange, bit_pos) for bit_pos in range(bit_count)]
    own_parts, other_parts, terms = lax.switch(bit_index, branches, snapshots)
    gram_full = assemble(terms, own_low)
    rotation = jacobi_pallas(gram_full)
    width = own_parts.shape[0]
    own_columns = jnp.where(own_low, rotation[:, :width], rotation[:, width:])
    return rotate_part(own_columns, own_low, own_parts, other_parts)


def solution(mesh):
    in_specs = (P(("cols", "rows"), None), P())
    out_specs = P("cols", "rows")
    return jax.shard_map(shards, mesh=mesh, in_specs=in_specs, out_specs=out_specs, check_vma=False)
```

```python
import functools

import jax
import jax.numpy as jnp
import numpy as np
from jax import lax
from jax.experimental import pallas as pl
from jax.experimental.pallas import tpu as pltpu
from jax.sharding import PartitionSpec as P

ROUNDS = 8


def partner_2(value, axis, bit):
    mask = 2**bit
    pairs = [(source, source ^ mask) for source in range(lax.axis_size(axis))]
    return lax.ppermute(value, axis, pairs)


def jacobi_kernel(gram_ref, rotation_ref):
    highest = lax.Precision.HIGHEST
    order_dim = gram_ref.shape[0]
    last_idx = order_dim - 1
    width = order_dim // 2
    gram = gram_ref[...]
    row_col = lax.broadcasted_iota(jnp.int32, (order_dim, 1), 0)
    row_full = lax.broadcasted_iota(jnp.int32, (order_dim, order_dim), 0)
    col_full = lax.broadcasted_iota(jnp.int32, (order_dim, order_dim), 1)
    eye = row_full == col_full
    rotation = None
    for round_idx in range(ROUNDS):
        fixed = round_idx % last_idx
        mirror = 2 * fixed - row_col
        mirror = jnp.where(mirror < 0, mirror + last_idx, mirror)
        partner = jnp.where(row_col == fixed, last_idx, jnp.where(row_col == last_idx, fixed, mirror))
        offset = row_col - fixed
        offset = jnp.where(offset < 0, offset + last_idx, offset)
        is_first = (row_col == last_idx) | ((row_col != fixed) & (offset >= 1) & (offset <= width - 1))
        swap = (col_full == partner).astype(jnp.float32)
        on_diag = jnp.where(eye, gram, 0.0)
        diag_own = jnp.sum(on_diag, axis=1, keepdims=True)
        diag_row = jnp.sum(on_diag, axis=0, keepdims=True)
        diag_mate = jnp.sum(swap * diag_row, axis=1, keepdims=True)
        picked = gram * swap
        cross_second = jnp.sum(picked, axis=1, keepdims=True)
        cross_row = jnp.sum(picked, axis=0, keepdims=True)
        cross_first = jnp.sum(jnp.where(eye, cross_row, 0.0), axis=1, keepdims=True)
        cross_val = jnp.where(is_first, cross_first, cross_second)
        spread = jnp.where(is_first, diag_mate - diag_own, diag_own - diag_mate)
        hypot_val = jnp.sqrt(spread * spread + 4.0 * cross_val * cross_val)
        denom = jnp.sqrt(2.0 * hypot_val * (hypot_val + jnp.abs(spread)))
        sign_val = jnp.where(spread >= 0.0, 1.0, -1.0)
        cosine = (hypot_val + jnp.abs(spread)) / denom
        sine_val = 2.0 * cross_val * sign_val / denom
        signed = jnp.where(is_first, sine_val, -sine_val)
        diag_part = jnp.where(eye, cosine, 0.0)
        turn = diag_part + swap * signed
        turn_t = diag_part - swap * signed
        gram = jnp.dot(
            turn_t,
            jnp.dot(gram, turn, precision=highest, preferred_element_type=jnp.float32),
            precision=highest,
            preferred_element_type=jnp.float32,
        )
        rotation = turn if rotation is None else jnp.dot(
            rotation, turn, precision=highest, preferred_element_type=jnp.float32
        )
    rotation_ref[...] = rotation

def jacobi_pallas(gram):
    return pl.pallas_call(
        jacobi_kernel,
        out_shape=jax.ShapeDtypeStruct(gram.shape, jnp.float32),
        in_specs=[pl.BlockSpec(memory_space=pltpu.VMEM)],
        out_specs=pl.BlockSpec(memory_space=pltpu.VMEM),
    )(gram)


def gram_kernel(mine_ref, theirs_ref, out_ref, acc_ref):
    step = pl.program_id(0)

    @pl.when(step == 0)
    def _():
        acc_ref[...] = jnp.zeros_like(acc_ref)

    stacked = jnp.concatenate([mine_ref[...], theirs_ref[...]], 0)
    acc_ref[...] += lax.dot_general(
        stacked,
        stacked,
        (((1,), (1,)), ((), ())),
        precision=lax.Precision.HIGHEST,
        preferred_element_type=jnp.float32,
    )

    @pl.when(step == pl.num_programs(0) - 1)
    def _():
        width = mine_ref.shape[0]
        row = lax.broadcasted_iota(jnp.int32, (width, width), 0)
        col = lax.broadcasted_iota(jnp.int32, (width, width), 1)
        gram_theirs = acc_ref[width:, width:]
        out_ref[:width, :] = jnp.where(row <= col, acc_ref[:width, :width], gram_theirs)
        out_ref[width : 2 * width, :] = acc_ref[:width, width:]
        diag_theirs = jnp.sum(jnp.where(row == col, gram_theirs, 0.0), axis=0, keepdims=True)
        out_ref[2 * width :, :] = jnp.broadcast_to(diag_theirs, (8, width))


def gram_store_kernel(mine_ref, theirs_ref, own_in, other_in, out_ref, own_ref, other_ref, acc_ref):
    del own_in, other_in
    gram_kernel(mine_ref, theirs_ref, out_ref, acc_ref)
    own_ref[...] = mine_ref[...]
    other_ref[...] = theirs_ref[...]


def pair_terms_stored(mine, theirs, own_full, other_full, chunk):
    width, piece = mine.shape
    cell_spec = pl.BlockSpec((width, piece), lambda step: (0, 0))
    full_spec = pl.BlockSpec((width, piece), lambda step: (0, chunk))
    return pl.pallas_call(
        gram_store_kernel,
        out_shape=[
            jax.ShapeDtypeStruct((2 * width + 8, width), jnp.float32),
            jax.ShapeDtypeStruct(own_full.shape, own_full.dtype),
            jax.ShapeDtypeStruct(other_full.shape, other_full.dtype),
        ],
        grid=(1,),
        in_specs=[cell_spec, cell_spec, pl.BlockSpec(memory_space=pl.ANY), pl.BlockSpec(memory_space=pl.ANY)],
        out_specs=[pl.BlockSpec((2 * width + 8, width), lambda step: (0, 0)), full_spec, full_spec],
        scratch_shapes=[pltpu.VMEM((2 * width, 2 * width), jnp.float32)],
        input_output_aliases={2: 1, 3: 2},
        cost_estimate=pl.CostEstimate(
            flops=8 * width * width * piece, transcendentals=0, bytes_accessed=16 * width * piece
        ),
    )(mine, theirs, own_full, other_full)


def pair_terms(mine, theirs):
    width, cells = mine.shape
    tile = min(cells, 2048)
    cell_spec = pl.BlockSpec((width, tile), lambda step: (0, step))
    return pl.pallas_call(
        gram_kernel,
        out_shape=jax.ShapeDtypeStruct((2 * width + 8, width), jnp.float32),
        grid=(cells // tile,),
        in_specs=[cell_spec, cell_spec],
        out_specs=pl.BlockSpec((2 * width + 8, width), lambda step: (0, 0)),
        scratch_shapes=[pltpu.VMEM((2 * width, 2 * width), jnp.float32)],
        cost_estimate=pl.CostEstimate(
            flops=8 * width * width * cells, transcendentals=0, bytes_accessed=8 * width * cells
        ),
    )(mine, theirs)


def row_total(part):
    count = lax.axis_size("rows")
    bit = 1
    while bit < count:
        pairs = [(source, source ^ bit) for source in range(count)]
        part = part + lax.ppermute(part, "rows", pairs)
        bit *= 2
    return part


CHUNKS = 4


def lay_kernel(chunk_ids, piece, source_ref, *out_refs):
    for chunk, out_ref in zip(chunk_ids, out_refs):
        out_ref[...] = source_ref[:, chunk * piece : (chunk + 1) * piece]


def lay_out(snapshots, rows_n, chunks, chunk_ids):
    local_rows, cells = snapshots.shape
    width = cells // rows_n
    piece = width // chunks
    out_spec = pl.BlockSpec((None, local_rows, piece), lambda dest: (dest, 0, 0))
    return pl.pallas_call(
        functools.partial(lay_kernel, tuple(chunk_ids), piece),
        out_shape=[jax.ShapeDtypeStruct((rows_n, local_rows, piece), snapshots.dtype)] * len(chunk_ids),
        grid=(rows_n,),
        in_specs=[pl.BlockSpec((local_rows, width), lambda dest: (0, dest))],
        out_specs=[out_spec] * len(chunk_ids),
        cost_estimate=pl.CostEstimate(
            flops=0, transcendentals=0, bytes_accessed=8 * local_rows * piece * rows_n * len(chunk_ids)
        ),
    )(snapshots)


def exchange(bit_pos, snapshots):
    chunks = 1 if bit_pos == 0 else CHUNKS
    rows_n = lax.axis_size("rows")
    local_rows, cells = snapshots.shape
    width = cells // rows_n
    piece = width // chunks

    if chunks == 1:
        mine = lax.all_to_all(snapshots, "rows", split_axis=1, concat_axis=0, tiled=True)
        theirs = partner_2(mine, "cols", bit_pos)
        return mine, theirs, pair_terms(mine, theirs)

    sends = lay_out(snapshots, rows_n, chunks, [0]) + lay_out(snapshots, rows_n, chunks, range(1, chunks))

    def laid(chunk):
        return sends[chunk]

    def spread(sent):
        got = lax.all_to_all(sent, "rows", split_axis=0, concat_axis=0)
        return got.reshape(rows_n * local_rows, piece)

    own_parts = [spread(laid(0))]
    other_parts = []
    for chunk in range(1, chunks):
        held = (own_parts[-1], laid(chunk)) + tuple(other_parts[-1:])
        held = lax.optimization_barrier(held)
        own_parts[-1] = held[0]
        if other_parts:
            other_parts[-1] = held[2]
        other_parts.append(partner_2(held[0], "cols", bit_pos))
        own_parts.append(spread(held[1]))
    other_parts.append(partner_2(own_parts[-1], "cols", bit_pos))
    own_full = jnp.zeros((rows_n * local_rows, width), snapshots.dtype)
    other_full = jnp.zeros((rows_n * local_rows, width), snapshots.dtype)
    terms = None
    for chunk, (mine, theirs) in enumerate(zip(own_parts, other_parts)):
        part, own_full, other_full = pair_terms_stored(mine, theirs, own_full, other_full, chunk)
        terms = part if terms is None else terms + part
    return own_full, other_full, terms


def unpack_terms(packed, width):
    row = lax.broadcasted_iota(jnp.int32, (width, width), 0)
    col = lax.broadcasted_iota(jnp.int32, (width, width), 1)
    shared = packed[:width]
    gram_mixed = packed[width : 2 * width]
    diag_theirs = packed[2 * width : 2 * width + 1]
    gram_mine = jnp.where(row <= col, shared, shared.T)
    gram_theirs = jnp.where(row > col, shared, jnp.where(row < col, shared.T, diag_theirs))
    return gram_mine, gram_mixed, gram_theirs


def assemble(terms, own_low):
    gram_mine, gram_mixed, gram_theirs = unpack_terms(row_total(terms), terms.shape[1])
    upper_left = jnp.where(own_low, gram_mine, gram_theirs)
    lower_right = jnp.where(own_low, gram_theirs, gram_mine)
    upper_right = jnp.where(own_low, gram_mixed, gram_mixed.T)
    top_rows = jnp.concatenate([upper_left, upper_right], 1)
    bottom_rows = jnp.concatenate([upper_right.T, lower_right], 1)
    return jnp.concatenate([top_rows, bottom_rows], 0)


def rotate_kernel(coef_ref, mine_ref, theirs_ref, out_ref):
    stacked = jnp.concatenate([mine_ref[...], theirs_ref[...]], 0)
    out_ref[...] = jnp.dot(
        coef_ref[...], stacked, precision=lax.Precision.HIGHEST, preferred_element_type=jnp.float32
    )


def rotate_part(columns_sel, own_low, mine, theirs):
    width, cells = mine.shape
    coef_mine = jnp.where(own_low, columns_sel[:width], columns_sel[width:])
    coef_theirs = jnp.where(own_low, columns_sel[width:], columns_sel[:width])
    coef = jnp.concatenate([coef_mine, coef_theirs], 0).T
    tile = min(cells, 2048)
    coef_spec = pl.BlockSpec((width, 2 * width), lambda step: (0, 0))
    cell_spec = pl.BlockSpec((width, tile), lambda step: (0, step))
    return pl.pallas_call(
        rotate_kernel,
        out_shape=jax.ShapeDtypeStruct((width, cells), jnp.float32),
        grid=(cells // tile,),
        in_specs=[coef_spec, cell_spec, cell_spec],
        out_specs=cell_spec,
        cost_estimate=pl.CostEstimate(
            flops=4 * width * width * cells, transcendentals=0, bytes_accessed=12 * width * cells
        ),
    )(coef, mine, theirs)


def shards(snapshots, pair_table):
    bit_count = lax.axis_size("cols").bit_length() - 1
    column = lax.axis_index("cols")
    mask_val = pair_table[0]
    bit_index = jnp.int32(0)
    for bit_pos in range(bit_count):
        bit_index = bit_index + (mask_val >> bit_pos & 1) * bit_pos
    partner = jnp.bitwise_xor(column, mask_val)
    own_low = column < partner
    branches = [functools.partial(exchange, bit_pos) for bit_pos in range(bit_count)]
    own_parts, other_parts, terms = lax.switch(bit_index, branches, snapshots)
    gram_full = assemble(terms, own_low)
    rotation = jacobi_pallas(gram_full)
    width = own_parts.shape[0]
    own_columns = jnp.where(own_low, rotation[:, :width], rotation[:, width:])
    return rotate_part(own_columns, own_low, own_parts, other_parts)


def solution(mesh):
    in_specs = (P(("cols", "rows"), None), P())
    out_specs = P("cols", "rows")
    return jax.shard_map(shards, mesh=mesh, in_specs=in_specs, out_specs=out_specs, check_vma=False)
```

```python
import functools

import jax
import jax.numpy as jnp
import numpy as np
from jax import lax
from jax.experimental import pallas as pl
from jax.experimental.pallas import tpu as pltpu
from jax.sharding import PartitionSpec as P

ROUNDS = 8


def partner_2(value, axis, bit):
    mask = 2**bit
    pairs = [(source, source ^ mask) for source in range(lax.axis_size(axis))]
    return lax.ppermute(value, axis, pairs)


def jacobi_kernel(gram_ref, rotation_ref):
    highest = lax.Precision.HIGHEST
    order_dim = gram_ref.shape[0]
    last_idx = order_dim - 1
    width = order_dim // 2
    gram = gram_ref[...]
    row_col = lax.broadcasted_iota(jnp.int32, (order_dim, 1), 0)
    row_full = lax.broadcasted_iota(jnp.int32, (order_dim, order_dim), 0)
    col_full = lax.broadcasted_iota(jnp.int32, (order_dim, order_dim), 1)
    eye = row_full == col_full
    rotation = None
    for round_idx in range(ROUNDS):
        fixed = round_idx % last_idx
        mirror = 2 * fixed - row_col
        mirror = jnp.where(mirror < 0, mirror + last_idx, mirror)
        partner = jnp.where(row_col == fixed, last_idx, jnp.where(row_col == last_idx, fixed, mirror))
        offset = row_col - fixed
        offset = jnp.where(offset < 0, offset + last_idx, offset)
        is_first = (row_col == last_idx) | ((row_col != fixed) & (offset >= 1) & (offset <= width - 1))
        swap = (col_full == partner).astype(jnp.float32)
        on_diag = jnp.where(eye, gram, 0.0)
        diag_own = jnp.sum(on_diag, axis=1, keepdims=True)
        diag_row = jnp.sum(on_diag, axis=0, keepdims=True)
        diag_mate = jnp.sum(swap * diag_row, axis=1, keepdims=True)
        picked = gram * swap
        cross_second = jnp.sum(picked, axis=1, keepdims=True)
        cross_row = jnp.sum(picked, axis=0, keepdims=True)
        cross_first = jnp.sum(jnp.where(eye, cross_row, 0.0), axis=1, keepdims=True)
        cross_val = jnp.where(is_first, cross_first, cross_second)
        spread = jnp.where(is_first, diag_mate - diag_own, diag_own - diag_mate)
        hypot_val = jnp.sqrt(spread * spread + 4.0 * cross_val * cross_val)
        denom = jnp.sqrt(2.0 * hypot_val * (hypot_val + jnp.abs(spread)))
        sign_val = jnp.where(spread >= 0.0, 1.0, -1.0)
        cosine = (hypot_val + jnp.abs(spread)) / denom
        sine_val = 2.0 * cross_val * sign_val / denom
        signed = jnp.where(is_first, sine_val, -sine_val)
        diag_part = jnp.where(eye, cosine, 0.0)
        turn = diag_part + swap * signed
        turn_t = diag_part - swap * signed
        gram = jnp.dot(
            turn_t,
            jnp.dot(gram, turn, precision=highest, preferred_element_type=jnp.float32),
            precision=highest,
            preferred_element_type=jnp.float32,
        )
        rotation = turn if rotation is None else jnp.dot(
            rotation, turn, precision=highest, preferred_element_type=jnp.float32
        )
    rotation_ref[...] = rotation

def jacobi_pallas(gram):
    return pl.pallas_call(
        jacobi_kernel,
        out_shape=jax.ShapeDtypeStruct(gram.shape, jnp.float32),
        in_specs=[pl.BlockSpec(memory_space=pltpu.VMEM)],
        out_specs=pl.BlockSpec(memory_space=pltpu.VMEM),
    )(gram)


def gram_kernel(mine_ref, theirs_ref, out_ref, acc_ref):
    step = pl.program_id(0)

    @pl.when(step == 0)
    def _():
        acc_ref[...] = jnp.zeros_like(acc_ref)

    stacked = jnp.concatenate([mine_ref[...], theirs_ref[...]], 0)
    acc_ref[...] += lax.dot_general(
        stacked,
        stacked,
        (((1,), (1,)), ((), ())),
        precision=lax.Precision.HIGHEST,
        preferred_element_type=jnp.float32,
    )

    @pl.when(step == pl.num_programs(0) - 1)
    def _():
        width = mine_ref.shape[0]
        row = lax.broadcasted_iota(jnp.int32, (width, width), 0)
        col = lax.broadcasted_iota(jnp.int32, (width, width), 1)
        gram_theirs = acc_ref[width:, width:]
        out_ref[:width, :] = jnp.where(row <= col, acc_ref[:width, :width], gram_theirs)
        out_ref[width : 2 * width, :] = acc_ref[:width, width:]
        diag_theirs = jnp.sum(jnp.where(row == col, gram_theirs, 0.0), axis=0, keepdims=True)
        out_ref[2 * width :, :] = jnp.broadcast_to(diag_theirs, (8, width))


def gram_store_kernel(mine_ref, theirs_ref, own_in, other_in, out_ref, own_ref, other_ref, acc_ref):
    del own_in, other_in
    gram_kernel(mine_ref, theirs_ref, out_ref, acc_ref)
    own_ref[...] = mine_ref[...]
    other_ref[...] = theirs_ref[...]


def pair_terms_stored(mine, theirs, own_full, other_full, chunk):
    width, piece = mine.shape
    cell_spec = pl.BlockSpec((width, piece), lambda step: (0, 0))
    full_spec = pl.BlockSpec((width, piece), lambda step: (0, chunk))
    return pl.pallas_call(
        gram_store_kernel,
        out_shape=[
            jax.ShapeDtypeStruct((2 * width + 8, width), jnp.float32),
            jax.ShapeDtypeStruct(own_full.shape, own_full.dtype),
            jax.ShapeDtypeStruct(other_full.shape, other_full.dtype),
        ],
        grid=(1,),
        in_specs=[cell_spec, cell_spec, pl.BlockSpec(memory_space=pl.ANY), pl.BlockSpec(memory_space=pl.ANY)],
        out_specs=[pl.BlockSpec((2 * width + 8, width), lambda step: (0, 0)), full_spec, full_spec],
        scratch_shapes=[pltpu.VMEM((2 * width, 2 * width), jnp.float32)],
        input_output_aliases={2: 1, 3: 2},
        cost_estimate=pl.CostEstimate(
            flops=8 * width * width * piece, transcendentals=0, bytes_accessed=16 * width * piece
        ),
    )(mine, theirs, own_full, other_full)


def pair_terms(mine, theirs):
    width, cells = mine.shape
    tile = min(cells, 2048)
    cell_spec = pl.BlockSpec((width, tile), lambda step: (0, step))
    return pl.pallas_call(
        gram_kernel,
        out_shape=jax.ShapeDtypeStruct((2 * width + 8, width), jnp.float32),
        grid=(cells // tile,),
        in_specs=[cell_spec, cell_spec],
        out_specs=pl.BlockSpec((2 * width + 8, width), lambda step: (0, 0)),
        scratch_shapes=[pltpu.VMEM((2 * width, 2 * width), jnp.float32)],
        cost_estimate=pl.CostEstimate(
            flops=8 * width * width * cells, transcendentals=0, bytes_accessed=8 * width * cells
        ),
    )(mine, theirs)


def row_total(part):
    count = lax.axis_size("rows")
    bit = 1
    while bit < count:
        pairs = [(source, source ^ bit) for source in range(count)]
        part = part + lax.ppermute(part, "rows", pairs)
        bit *= 2
    return part


CHUNKS = 4


def lay_kernel(chunk_ids, piece, source_ref, *out_refs):
    if len(chunk_ids) == 1:
        out_refs[0][...] = source_ref[...]
        return
    for chunk, out_ref in zip(chunk_ids, out_refs):
        out_ref[...] = source_ref[:, chunk * piece : (chunk + 1) * piece]


def lay_out(snapshots, rows_n, chunks, chunk_ids):
    local_rows, cells = snapshots.shape
    width = cells // rows_n
    piece = width // chunks
    out_spec = pl.BlockSpec((None, local_rows, piece), lambda dest: (dest, 0, 0))
    return pl.pallas_call(
        functools.partial(lay_kernel, tuple(chunk_ids), piece),
        out_shape=[jax.ShapeDtypeStruct((rows_n, local_rows, piece), snapshots.dtype)] * len(chunk_ids),
        grid=(rows_n,),
        in_specs=[
            pl.BlockSpec((local_rows, piece), lambda dest: (0, dest * chunks + chunk_ids[0]))
            if len(chunk_ids) == 1
            else pl.BlockSpec((local_rows, width), lambda dest: (0, dest))
        ],
        out_specs=[out_spec] * len(chunk_ids),
        cost_estimate=pl.CostEstimate(
            flops=0, transcendentals=0, bytes_accessed=8 * local_rows * piece * rows_n * len(chunk_ids)
        ),
    )(snapshots)


def exchange(bit_pos, snapshots):
    chunks = 1 if bit_pos == 0 else CHUNKS
    rows_n = lax.axis_size("rows")
    local_rows, cells = snapshots.shape
    width = cells // rows_n
    piece = width // chunks

    if chunks == 1:
        mine = lax.all_to_all(snapshots, "rows", split_axis=1, concat_axis=0, tiled=True)
        theirs = partner_2(mine, "cols", bit_pos)
        return mine, theirs, pair_terms(mine, theirs)

    sends = lay_out(snapshots, rows_n, chunks, [0]) + lay_out(snapshots, rows_n, chunks, list(range(1, chunks)))

    def laid(chunk):
        return sends[chunk]

    def spread(sent):
        got = lax.all_to_all(sent, "rows", split_axis=0, concat_axis=0)
        return got.reshape(rows_n * local_rows, piece)

    own_parts = [spread(laid(0))]
    other_parts = []
    for chunk in range(1, chunks):
        held = (own_parts[-1], laid(chunk)) + tuple(other_parts[-1:])
        held = lax.optimization_barrier(held)
        own_parts[-1] = held[0]
        if other_parts:
            other_parts[-1] = held[2]
        other_parts.append(partner_2(held[0], "cols", bit_pos))
        own_parts.append(spread(held[1]))
    other_parts.append(partner_2(own_parts[-1], "cols", bit_pos))
    own_full = jnp.zeros((rows_n * local_rows, width), snapshots.dtype)
    other_full = jnp.zeros((rows_n * local_rows, width), snapshots.dtype)
    terms = None
    for chunk, (mine, theirs) in enumerate(zip(own_parts, other_parts)):
        part, own_full, other_full = pair_terms_stored(mine, theirs, own_full, other_full, chunk)
        terms = part if terms is None else terms + part
    return own_full, other_full, terms


def unpack_terms(packed, width):
    row = lax.broadcasted_iota(jnp.int32, (width, width), 0)
    col = lax.broadcasted_iota(jnp.int32, (width, width), 1)
    shared = packed[:width]
    gram_mixed = packed[width : 2 * width]
    diag_theirs = packed[2 * width : 2 * width + 1]
    gram_mine = jnp.where(row <= col, shared, shared.T)
    gram_theirs = jnp.where(row > col, shared, jnp.where(row < col, shared.T, diag_theirs))
    return gram_mine, gram_mixed, gram_theirs


def assemble(terms, own_low):
    gram_mine, gram_mixed, gram_theirs = unpack_terms(row_total(terms), terms.shape[1])
    upper_left = jnp.where(own_low, gram_mine, gram_theirs)
    lower_right = jnp.where(own_low, gram_theirs, gram_mine)
    upper_right = jnp.where(own_low, gram_mixed, gram_mixed.T)
    top_rows = jnp.concatenate([upper_left, upper_right], 1)
    bottom_rows = jnp.concatenate([upper_right.T, lower_right], 1)
    return jnp.concatenate([top_rows, bottom_rows], 0)


def rotate_kernel(coef_ref, mine_ref, theirs_ref, out_ref):
    stacked = jnp.concatenate([mine_ref[...], theirs_ref[...]], 0)
    out_ref[...] = jnp.dot(
        coef_ref[...], stacked, precision=lax.Precision.HIGHEST, preferred_element_type=jnp.float32
    )


def rotate_part(columns_sel, own_low, mine, theirs):
    width, cells = mine.shape
    coef_mine = jnp.where(own_low, columns_sel[:width], columns_sel[width:])
    coef_theirs = jnp.where(own_low, columns_sel[width:], columns_sel[:width])
    coef = jnp.concatenate([coef_mine, coef_theirs], 0).T
    tile = min(cells, 2048)
    coef_spec = pl.BlockSpec((width, 2 * width), lambda step: (0, 0))
    cell_spec = pl.BlockSpec((width, tile), lambda step: (0, step))
    return pl.pallas_call(
        rotate_kernel,
        out_shape=jax.ShapeDtypeStruct((width, cells), jnp.float32),
        grid=(cells // tile,),
        in_specs=[coef_spec, cell_spec, cell_spec],
        out_specs=cell_spec,
        cost_estimate=pl.CostEstimate(
            flops=4 * width * width * cells, transcendentals=0, bytes_accessed=12 * width * cells
        ),
    )(coef, mine, theirs)


def shards(snapshots, pair_table):
    bit_count = lax.axis_size("cols").bit_length() - 1
    column = lax.axis_index("cols")
    mask_val = pair_table[0]
    bit_index = jnp.int32(0)
    for bit_pos in range(bit_count):
        bit_index = bit_index + (mask_val >> bit_pos & 1) * bit_pos
    partner = jnp.bitwise_xor(column, mask_val)
    own_low = column < partner
    branches = [functools.partial(exchange, bit_pos) for bit_pos in range(bit_count)]
    own_parts, other_parts, terms = lax.switch(bit_index, branches, snapshots)
    gram_full = assemble(terms, own_low)
    rotation = jacobi_pallas(gram_full)
    width = own_parts.shape[0]
    own_columns = jnp.where(own_low, rotation[:, :width], rotation[:, width:])
    return rotate_part(own_columns, own_low, own_parts, other_parts)


def solution(mesh):
    in_specs = (P(("cols", "rows"), None), P())
    out_specs = P("cols", "rows")
    return jax.shard_map(shards, mesh=mesh, in_specs=in_specs, out_specs=out_specs, check_vma=False)
```

```python
import functools

import jax
import jax.numpy as jnp
import numpy as np
from jax import lax
from jax.experimental import pallas as pl
from jax.experimental.pallas import tpu as pltpu
from jax.sharding import PartitionSpec as P

ROUNDS = 8


def partner_2(value, axis, bit):
    mask = 2**bit
    pairs = [(source, source ^ mask) for source in range(lax.axis_size(axis))]
    return lax.ppermute(value, axis, pairs)


def jacobi_kernel(gram_ref, rotation_ref):
    highest = lax.Precision.HIGHEST
    order_dim = gram_ref.shape[0]
    last_idx = order_dim - 1
    width = order_dim // 2
    gram = gram_ref[...]
    row_col = lax.broadcasted_iota(jnp.int32, (order_dim, 1), 0)
    row_full = lax.broadcasted_iota(jnp.int32, (order_dim, order_dim), 0)
    col_full = lax.broadcasted_iota(jnp.int32, (order_dim, order_dim), 1)
    eye = row_full == col_full
    rotation = None
    for round_idx in range(ROUNDS):
        fixed = round_idx % last_idx
        mirror = 2 * fixed - row_col
        mirror = jnp.where(mirror < 0, mirror + last_idx, mirror)
        partner = jnp.where(row_col == fixed, last_idx, jnp.where(row_col == last_idx, fixed, mirror))
        offset = row_col - fixed
        offset = jnp.where(offset < 0, offset + last_idx, offset)
        is_first = (row_col == last_idx) | ((row_col != fixed) & (offset >= 1) & (offset <= width - 1))
        swap = (col_full == partner).astype(jnp.float32)
        on_diag = jnp.where(eye, gram, 0.0)
        diag_own = jnp.sum(on_diag, axis=1, keepdims=True)
        diag_row = jnp.sum(on_diag, axis=0, keepdims=True)
        diag_mate = jnp.sum(swap * diag_row, axis=1, keepdims=True)
        picked = gram * swap
        cross_second = jnp.sum(picked, axis=1, keepdims=True)
        cross_row = jnp.sum(picked, axis=0, keepdims=True)
        cross_first = jnp.sum(jnp.where(eye, cross_row, 0.0), axis=1, keepdims=True)
        cross_val = jnp.where(is_first, cross_first, cross_second)
        spread = jnp.where(is_first, diag_mate - diag_own, diag_own - diag_mate)
        hypot_val = jnp.sqrt(spread * spread + 4.0 * cross_val * cross_val)
        denom = jnp.sqrt(2.0 * hypot_val * (hypot_val + jnp.abs(spread)))
        sign_val = jnp.where(spread >= 0.0, 1.0, -1.0)
        cosine = (hypot_val + jnp.abs(spread)) / denom
        sine_val = 2.0 * cross_val * sign_val / denom
        signed = jnp.where(is_first, sine_val, -sine_val)
        diag_part = jnp.where(eye, cosine, 0.0)
        turn = diag_part + swap * signed
        turn_t = diag_part - swap * signed
        gram = jnp.dot(
            turn_t,
            jnp.dot(gram, turn, precision=highest, preferred_element_type=jnp.float32),
            precision=highest,
            preferred_element_type=jnp.float32,
        )
        rotation = turn if rotation is None else jnp.dot(
            rotation, turn, precision=highest, preferred_element_type=jnp.float32
        )
    rotation_ref[...] = rotation

def jacobi_pallas(gram):
    return pl.pallas_call(
        jacobi_kernel,
        out_shape=jax.ShapeDtypeStruct(gram.shape, jnp.float32),
        in_specs=[pl.BlockSpec(memory_space=pltpu.VMEM)],
        out_specs=pl.BlockSpec(memory_space=pltpu.VMEM),
    )(gram)


def gram_kernel(mine_ref, theirs_ref, out_ref, acc_ref):
    step = pl.program_id(0)

    @pl.when(step == 0)
    def _():
        acc_ref[...] = jnp.zeros_like(acc_ref)

    stacked = jnp.concatenate([mine_ref[...], theirs_ref[...]], 0)
    acc_ref[...] += lax.dot_general(
        stacked,
        stacked,
        (((1,), (1,)), ((), ())),
        precision=lax.Precision.HIGHEST,
        preferred_element_type=jnp.float32,
    )

    @pl.when(step == pl.num_programs(0) - 1)
    def _():
        width = mine_ref.shape[0]
        row = lax.broadcasted_iota(jnp.int32, (width, width), 0)
        col = lax.broadcasted_iota(jnp.int32, (width, width), 1)
        gram_theirs = acc_ref[width:, width:]
        out_ref[:width, :] = jnp.where(row <= col, acc_ref[:width, :width], gram_theirs)
        out_ref[width : 2 * width, :] = acc_ref[:width, width:]
        diag_theirs = jnp.sum(jnp.where(row == col, gram_theirs, 0.0), axis=0, keepdims=True)
        out_ref[2 * width :, :] = jnp.broadcast_to(diag_theirs, (8, width))


def gram_store_kernel(mine_ref, theirs_ref, own_in, other_in, out_ref, own_ref, other_ref, acc_ref):
    del own_in, other_in
    gram_kernel(mine_ref, theirs_ref, out_ref, acc_ref)
    own_ref[...] = mine_ref[...]
    other_ref[...] = theirs_ref[...]


def pair_terms_stored(mine, theirs, own_full, other_full, chunk):
    width, piece = mine.shape
    cell_spec = pl.BlockSpec((width, piece), lambda step: (0, 0))
    full_spec = pl.BlockSpec((width, piece), lambda step: (0, chunk))
    return pl.pallas_call(
        gram_store_kernel,
        out_shape=[
            jax.ShapeDtypeStruct((2 * width + 8, width), jnp.float32),
            jax.ShapeDtypeStruct(own_full.shape, own_full.dtype),
            jax.ShapeDtypeStruct(other_full.shape, other_full.dtype),
        ],
        grid=(1,),
        in_specs=[cell_spec, cell_spec, pl.BlockSpec(memory_space=pl.ANY), pl.BlockSpec(memory_space=pl.ANY)],
        out_specs=[pl.BlockSpec((2 * width + 8, width), lambda step: (0, 0)), full_spec, full_spec],
        scratch_shapes=[pltpu.VMEM((2 * width, 2 * width), jnp.float32)],
        input_output_aliases={2: 1, 3: 2},
        cost_estimate=pl.CostEstimate(
            flops=8 * width * width * piece, transcendentals=0, bytes_accessed=16 * width * piece
        ),
    )(mine, theirs, own_full, other_full)


def gram_other_kernel(mine_ref, theirs_ref, other_in, out_ref, other_ref, acc_ref):
    del other_in
    gram_kernel(mine_ref, theirs_ref, out_ref, acc_ref)
    other_ref[...] = theirs_ref[...]


def pair_terms_half(mine_full, theirs, other_full, chunk):
    width, piece = theirs.shape
    part_spec = pl.BlockSpec((width, piece), lambda step: (0, chunk))
    return pl.pallas_call(
        gram_other_kernel,
        out_shape=[
            jax.ShapeDtypeStruct((2 * width + 8, width), jnp.float32),
            jax.ShapeDtypeStruct(other_full.shape, other_full.dtype),
        ],
        grid=(1,),
        in_specs=[part_spec, pl.BlockSpec((width, piece), lambda step: (0, 0)), pl.BlockSpec(memory_space=pl.ANY)],
        out_specs=[pl.BlockSpec((2 * width + 8, width), lambda step: (0, 0)), part_spec],
        scratch_shapes=[pltpu.VMEM((2 * width, 2 * width), jnp.float32)],
        input_output_aliases={2: 1},
        cost_estimate=pl.CostEstimate(
            flops=8 * width * width * piece, transcendentals=0, bytes_accessed=12 * width * piece
        ),
    )(mine_full, theirs, other_full)


def pair_terms(mine, theirs):
    width, cells = mine.shape
    tile = min(cells, 2048)
    cell_spec = pl.BlockSpec((width, tile), lambda step: (0, step))
    return pl.pallas_call(
        gram_kernel,
        out_shape=jax.ShapeDtypeStruct((2 * width + 8, width), jnp.float32),
        grid=(cells // tile,),
        in_specs=[cell_spec, cell_spec],
        out_specs=pl.BlockSpec((2 * width + 8, width), lambda step: (0, 0)),
        scratch_shapes=[pltpu.VMEM((2 * width, 2 * width), jnp.float32)],
        cost_estimate=pl.CostEstimate(
            flops=8 * width * width * cells, transcendentals=0, bytes_accessed=8 * width * cells
        ),
    )(mine, theirs)


def row_total(part):
    count = lax.axis_size("rows")
    bit = 1
    while bit < count:
        pairs = [(source, source ^ bit) for source in range(count)]
        part = part + lax.ppermute(part, "rows", pairs)
        bit *= 2
    return part


CHUNKS = 4


def lay_kernel(chunk_ids, piece, source_ref, *out_refs):
    if len(chunk_ids) == 1:
        out_refs[0][...] = source_ref[...]
        return
    for chunk, out_ref in zip(chunk_ids, out_refs):
        out_ref[...] = source_ref[:, chunk * piece : (chunk + 1) * piece]


def lay_out(snapshots, rows_n, chunks, chunk_ids):
    local_rows, cells = snapshots.shape
    width = cells // rows_n
    piece = width // chunks
    out_spec = pl.BlockSpec((None, local_rows, piece), lambda dest: (dest, 0, 0))
    return pl.pallas_call(
        functools.partial(lay_kernel, tuple(chunk_ids), piece),
        out_shape=[jax.ShapeDtypeStruct((rows_n, local_rows, piece), snapshots.dtype)] * len(chunk_ids),
        grid=(rows_n,),
        in_specs=[
            pl.BlockSpec((local_rows, piece), lambda dest: (0, dest * chunks + chunk_ids[0]))
            if len(chunk_ids) == 1
            else pl.BlockSpec((local_rows, width), lambda dest: (0, dest))
        ],
        out_specs=[out_spec] * len(chunk_ids),
        cost_estimate=pl.CostEstimate(
            flops=0, transcendentals=0, bytes_accessed=8 * local_rows * piece * rows_n * len(chunk_ids)
        ),
    )(snapshots)


def exchange(bit_pos, snapshots):
    chunks = 1 if bit_pos == 0 else CHUNKS
    rows_n = lax.axis_size("rows")
    local_rows, cells = snapshots.shape
    width = cells // rows_n
    piece = width // chunks

    if chunks == 1:
        mine = lax.all_to_all(snapshots, "rows", split_axis=1, concat_axis=0, tiled=True)
        half = width // 2
        other_full = jnp.zeros_like(mine)
        terms = None
        for part in range(2):
            theirs = partner_2(mine[:, part * half : (part + 1) * half], "cols", bit_pos)
            got, other_full = pair_terms_half(mine, theirs, other_full, part)
            terms = got if terms is None else terms + got
        return mine, other_full, terms

    sends = lay_out(snapshots, rows_n, chunks, [0]) + lay_out(snapshots, rows_n, chunks, list(range(1, chunks)))

    def laid(chunk):
        return sends[chunk]

    def spread(sent):
        got = lax.all_to_all(sent, "rows", split_axis=0, concat_axis=0)
        return got.reshape(rows_n * local_rows, piece)

    own_parts = [spread(laid(0))]
    other_parts = []
    for chunk in range(1, chunks):
        held = (own_parts[-1], laid(chunk)) + tuple(other_parts[-1:])
        held = lax.optimization_barrier(held)
        own_parts[-1] = held[0]
        if other_parts:
            other_parts[-1] = held[2]
        other_parts.append(partner_2(held[0], "cols", bit_pos))
        own_parts.append(spread(held[1]))
    other_parts.append(partner_2(own_parts[-1], "cols", bit_pos))
    own_full = jnp.zeros((rows_n * local_rows, width), snapshots.dtype)
    other_full = jnp.zeros((rows_n * local_rows, width), snapshots.dtype)
    terms = None
    for chunk, (mine, theirs) in enumerate(zip(own_parts, other_parts)):
        part, own_full, other_full = pair_terms_stored(mine, theirs, own_full, other_full, chunk)
        terms = part if terms is None else terms + part
    return own_full, other_full, terms


def unpack_terms(packed, width):
    row = lax.broadcasted_iota(jnp.int32, (width, width), 0)
    col = lax.broadcasted_iota(jnp.int32, (width, width), 1)
    shared = packed[:width]
    gram_mixed = packed[width : 2 * width]
    diag_theirs = packed[2 * width : 2 * width + 1]
    gram_mine = jnp.where(row <= col, shared, shared.T)
    gram_theirs = jnp.where(row > col, shared, jnp.where(row < col, shared.T, diag_theirs))
    return gram_mine, gram_mixed, gram_theirs


def assemble(terms, own_low):
    gram_mine, gram_mixed, gram_theirs = unpack_terms(row_total(terms), terms.shape[1])
    upper_left = jnp.where(own_low, gram_mine, gram_theirs)
    lower_right = jnp.where(own_low, gram_theirs, gram_mine)
    upper_right = jnp.where(own_low, gram_mixed, gram_mixed.T)
    top_rows = jnp.concatenate([upper_left, upper_right], 1)
    bottom_rows = jnp.concatenate([upper_right.T, lower_right], 1)
    return jnp.concatenate([top_rows, bottom_rows], 0)


def rotate_kernel(coef_ref, mine_ref, theirs_ref, out_ref):
    stacked = jnp.concatenate([mine_ref[...], theirs_ref[...]], 0)
    out_ref[...] = jnp.dot(
        coef_ref[...], stacked, precision=lax.Precision.HIGHEST, preferred_element_type=jnp.float32
    )


def rotate_part(columns_sel, own_low, mine, theirs):
    width, cells = mine.shape
    coef_mine = jnp.where(own_low, columns_sel[:width], columns_sel[width:])
    coef_theirs = jnp.where(own_low, columns_sel[width:], columns_sel[:width])
    coef = jnp.concatenate([coef_mine, coef_theirs], 0).T
    tile = min(cells, 2048)
    coef_spec = pl.BlockSpec((width, 2 * width), lambda step: (0, 0))
    cell_spec = pl.BlockSpec((width, tile), lambda step: (0, step))
    return pl.pallas_call(
        rotate_kernel,
        out_shape=jax.ShapeDtypeStruct((width, cells), jnp.float32),
        grid=(cells // tile,),
        in_specs=[coef_spec, cell_spec, cell_spec],
        out_specs=cell_spec,
        cost_estimate=pl.CostEstimate(
            flops=4 * width * width * cells, transcendentals=0, bytes_accessed=12 * width * cells
        ),
    )(coef, mine, theirs)


def shards(snapshots, pair_table):
    bit_count = lax.axis_size("cols").bit_length() - 1
    column = lax.axis_index("cols")
    mask_val = pair_table[0]
    bit_index = jnp.int32(0)
    for bit_pos in range(bit_count):
        bit_index = bit_index + (mask_val >> bit_pos & 1) * bit_pos
    partner = jnp.bitwise_xor(column, mask_val)
    own_low = column < partner
    branches = [functools.partial(exchange, bit_pos) for bit_pos in range(bit_count)]
    own_parts, other_parts, terms = lax.switch(bit_index, branches, snapshots)
    gram_full = assemble(terms, own_low)
    rotation = jacobi_pallas(gram_full)
    width = own_parts.shape[0]
    own_columns = jnp.where(own_low, rotation[:, :width], rotation[:, width:])
    return rotate_part(own_columns, own_low, own_parts, other_parts)


def solution(mesh):
    in_specs = (P(("cols", "rows"), None), P())
    out_specs = P("cols", "rows")
    return jax.shard_map(shards, mesh=mesh, in_specs=in_specs, out_specs=out_specs, check_vma=False)
```

```python
import functools

import jax
import jax.numpy as jnp
import numpy as np
from jax import lax
from jax.experimental import pallas as pl
from jax.experimental.pallas import tpu as pltpu
from jax.sharding import PartitionSpec as P

ROUNDS = 8


def partner_2(value, axis, bit):
    mask = 2**bit
    pairs = [(source, source ^ mask) for source in range(lax.axis_size(axis))]
    return lax.ppermute(value, axis, pairs)


def jacobi_kernel(gram_ref, rotation_ref):
    highest = lax.Precision.HIGHEST
    order_dim = gram_ref.shape[0]
    last_idx = order_dim - 1
    width = order_dim // 2
    gram = gram_ref[...]
    row_col = lax.broadcasted_iota(jnp.int32, (order_dim, 1), 0)
    row_full = lax.broadcasted_iota(jnp.int32, (order_dim, order_dim), 0)
    col_full = lax.broadcasted_iota(jnp.int32, (order_dim, order_dim), 1)
    eye = row_full == col_full
    rotation = None
    for round_idx in range(ROUNDS):
        fixed = round_idx % last_idx
        mirror = 2 * fixed - row_col
        mirror = jnp.where(mirror < 0, mirror + last_idx, mirror)
        partner = jnp.where(row_col == fixed, last_idx, jnp.where(row_col == last_idx, fixed, mirror))
        offset = row_col - fixed
        offset = jnp.where(offset < 0, offset + last_idx, offset)
        is_first = (row_col == last_idx) | ((row_col != fixed) & (offset >= 1) & (offset <= width - 1))
        swap = (col_full == partner).astype(jnp.float32)
        on_diag = jnp.where(eye, gram, 0.0)
        diag_own = jnp.sum(on_diag, axis=1, keepdims=True)
        diag_row = jnp.sum(on_diag, axis=0, keepdims=True)
        diag_mate = jnp.sum(swap * diag_row, axis=1, keepdims=True)
        picked = gram * swap
        cross_second = jnp.sum(picked, axis=1, keepdims=True)
        cross_row = jnp.sum(picked, axis=0, keepdims=True)
        cross_first = jnp.sum(jnp.where(eye, cross_row, 0.0), axis=1, keepdims=True)
        cross_val = jnp.where(is_first, cross_first, cross_second)
        spread = jnp.where(is_first, diag_mate - diag_own, diag_own - diag_mate)
        hypot_val = jnp.sqrt(spread * spread + 4.0 * cross_val * cross_val)
        denom = jnp.sqrt(2.0 * hypot_val * (hypot_val + jnp.abs(spread)))
        sign_val = jnp.where(spread >= 0.0, 1.0, -1.0)
        cosine = (hypot_val + jnp.abs(spread)) / denom
        sine_val = 2.0 * cross_val * sign_val / denom
        signed = jnp.where(is_first, sine_val, -sine_val)
        diag_part = jnp.where(eye, cosine, 0.0)
        turn = diag_part + swap * signed
        turn_t = diag_part - swap * signed
        gram = jnp.dot(
            turn_t,
            jnp.dot(gram, turn, precision=highest, preferred_element_type=jnp.float32),
            precision=highest,
            preferred_element_type=jnp.float32,
        )
        rotation = turn if rotation is None else jnp.dot(
            rotation, turn, precision=highest, preferred_element_type=jnp.float32
        )
    rotation_ref[...] = rotation

def jacobi_pallas(gram):
    return pl.pallas_call(
        jacobi_kernel,
        out_shape=jax.ShapeDtypeStruct(gram.shape, jnp.float32),
        in_specs=[pl.BlockSpec(memory_space=pltpu.VMEM)],
        out_specs=pl.BlockSpec(memory_space=pltpu.VMEM),
    )(gram)


def gram_kernel(mine_ref, theirs_ref, out_ref, acc_ref):
    step = pl.program_id(0)

    @pl.when(step == 0)
    def _():
        acc_ref[...] = jnp.zeros_like(acc_ref)

    stacked = jnp.concatenate([mine_ref[...], theirs_ref[...]], 0)
    acc_ref[...] += lax.dot_general(
        stacked,
        stacked,
        (((1,), (1,)), ((), ())),
        precision=lax.Precision.HIGHEST,
        preferred_element_type=jnp.float32,
    )

    @pl.when(step == pl.num_programs(0) - 1)
    def _():
        width = mine_ref.shape[0]
        row = lax.broadcasted_iota(jnp.int32, (width, width), 0)
        col = lax.broadcasted_iota(jnp.int32, (width, width), 1)
        gram_theirs = acc_ref[width:, width:]
        out_ref[:width, :] = jnp.where(row <= col, acc_ref[:width, :width], gram_theirs)
        out_ref[width : 2 * width, :] = acc_ref[:width, width:]
        diag_theirs = jnp.sum(jnp.where(row == col, gram_theirs, 0.0), axis=0, keepdims=True)
        out_ref[2 * width :, :] = jnp.broadcast_to(diag_theirs, (8, width))


def gram_store_kernel(mine_ref, theirs_ref, own_in, other_in, out_ref, own_ref, other_ref, acc_ref):
    del own_in, other_in
    gram_kernel(mine_ref, theirs_ref, out_ref, acc_ref)
    own_ref[...] = mine_ref[...]
    other_ref[...] = theirs_ref[...]


def pair_terms_stored(mine, theirs, own_full, other_full, chunk):
    width, piece = mine.shape
    cell_spec = pl.BlockSpec((width, piece), lambda step: (0, 0))
    full_spec = pl.BlockSpec((width, piece), lambda step: (0, chunk))
    return pl.pallas_call(
        gram_store_kernel,
        out_shape=[
            jax.ShapeDtypeStruct((2 * width + 8, width), jnp.float32),
            jax.ShapeDtypeStruct(own_full.shape, own_full.dtype),
            jax.ShapeDtypeStruct(other_full.shape, other_full.dtype),
        ],
        grid=(1,),
        in_specs=[cell_spec, cell_spec, pl.BlockSpec(memory_space=pl.ANY), pl.BlockSpec(memory_space=pl.ANY)],
        out_specs=[pl.BlockSpec((2 * width + 8, width), lambda step: (0, 0)), full_spec, full_spec],
        scratch_shapes=[pltpu.VMEM((2 * width, 2 * width), jnp.float32)],
        input_output_aliases={2: 1, 3: 2},
        cost_estimate=pl.CostEstimate(
            flops=8 * width * width * piece, transcendentals=0, bytes_accessed=16 * width * piece
        ),
    )(mine, theirs, own_full, other_full)


def mine_kernel(mine_ref, out_ref, acc_ref):
    step = pl.program_id(0)

    @pl.when(step == 0)
    def _():
        acc_ref[...] = jnp.zeros_like(acc_ref)

    acc_ref[...] += lax.dot_general(
        mine_ref[...],
        mine_ref[...],
        (((1,), (1,)), ((), ())),
        precision=lax.Precision.HIGHEST,
        preferred_element_type=jnp.float32,
    )

    @pl.when(step == pl.num_programs(0) - 1)
    def _():
        width = mine_ref.shape[0]
        row = lax.broadcasted_iota(jnp.int32, (width, width), 0)
        col = lax.broadcasted_iota(jnp.int32, (width, width), 1)
        out_ref[:width, :] = jnp.where(row <= col, acc_ref[...], 0.0)
        out_ref[width:, :] = jnp.zeros((width + 8, width), jnp.float32)


def rest_kernel(mine_ref, theirs_ref, out_ref, acc_ref):
    step = pl.program_id(0)

    @pl.when(step == 0)
    def _():
        acc_ref[...] = jnp.zeros_like(acc_ref)

    stacked = jnp.concatenate([mine_ref[...], theirs_ref[...]], 0)
    acc_ref[...] += lax.dot_general(
        stacked,
        theirs_ref[...],
        (((1,), (1,)), ((), ())),
        precision=lax.Precision.HIGHEST,
        preferred_element_type=jnp.float32,
    )

    @pl.when(step == pl.num_programs(0) - 1)
    def _():
        width = mine_ref.shape[0]
        row = lax.broadcasted_iota(jnp.int32, (width, width), 0)
        col = lax.broadcasted_iota(jnp.int32, (width, width), 1)
        gram_theirs = acc_ref[width:, :]
        out_ref[:width, :] = jnp.where(row > col, gram_theirs, 0.0)
        out_ref[width : 2 * width, :] = acc_ref[:width, :]
        diag_theirs = jnp.sum(jnp.where(row == col, gram_theirs, 0.0), axis=0, keepdims=True)
        out_ref[2 * width :, :] = jnp.broadcast_to(diag_theirs, (8, width))


def split_terms(kernel, operands, acc_rows):
    width, cells = operands[0].shape
    tile = min(cells, 2048)
    cell_spec = pl.BlockSpec((width, tile), lambda step: (0, step))
    return pl.pallas_call(
        kernel,
        out_shape=jax.ShapeDtypeStruct((2 * width + 8, width), jnp.float32),
        grid=(cells // tile,),
        in_specs=[cell_spec] * len(operands),
        out_specs=pl.BlockSpec((2 * width + 8, width), lambda step: (0, 0)),
        scratch_shapes=[pltpu.VMEM((acc_rows, width), jnp.float32)],
        cost_estimate=pl.CostEstimate(
            flops=2 * acc_rows * width * cells,
            transcendentals=0,
            bytes_accessed=4 * width * cells * len(operands),
        ),
    )(*operands)


def pair_terms(mine, theirs):
    width, cells = mine.shape
    tile = min(cells, 2048)
    cell_spec = pl.BlockSpec((width, tile), lambda step: (0, step))
    return pl.pallas_call(
        gram_kernel,
        out_shape=jax.ShapeDtypeStruct((2 * width + 8, width), jnp.float32),
        grid=(cells // tile,),
        in_specs=[cell_spec, cell_spec],
        out_specs=pl.BlockSpec((2 * width + 8, width), lambda step: (0, 0)),
        scratch_shapes=[pltpu.VMEM((2 * width, 2 * width), jnp.float32)],
        cost_estimate=pl.CostEstimate(
            flops=8 * width * width * cells, transcendentals=0, bytes_accessed=8 * width * cells
        ),
    )(mine, theirs)


def row_total(part):
    count = lax.axis_size("rows")
    bit = 1
    while bit < count:
        pairs = [(source, source ^ bit) for source in range(count)]
        part = part + lax.ppermute(part, "rows", pairs)
        bit *= 2
    return part


CHUNKS = 4


def lay_kernel(chunk_ids, piece, source_ref, *out_refs):
    if len(chunk_ids) == 1:
        out_refs[0][...] = source_ref[...]
        return
    for chunk, out_ref in zip(chunk_ids, out_refs):
        out_ref[...] = source_ref[:, chunk * piece : (chunk + 1) * piece]


def lay_out(snapshots, rows_n, chunks, chunk_ids):
    local_rows, cells = snapshots.shape
    width = cells // rows_n
    piece = width // chunks
    out_spec = pl.BlockSpec((None, local_rows, piece), lambda dest: (dest, 0, 0))
    return pl.pallas_call(
        functools.partial(lay_kernel, tuple(chunk_ids), piece),
        out_shape=[jax.ShapeDtypeStruct((rows_n, local_rows, piece), snapshots.dtype)] * len(chunk_ids),
        grid=(rows_n,),
        in_specs=[
            pl.BlockSpec((local_rows, piece), lambda dest: (0, dest * chunks + chunk_ids[0]))
            if len(chunk_ids) == 1
            else pl.BlockSpec((local_rows, width), lambda dest: (0, dest))
        ],
        out_specs=[out_spec] * len(chunk_ids),
        cost_estimate=pl.CostEstimate(
            flops=0, transcendentals=0, bytes_accessed=8 * local_rows * piece * rows_n * len(chunk_ids)
        ),
    )(snapshots)


def exchange(bit_pos, snapshots):
    chunks = 1 if bit_pos == 0 else CHUNKS
    rows_n = lax.axis_size("rows")
    local_rows, cells = snapshots.shape
    width = cells // rows_n
    piece = width // chunks

    if chunks == 1:
        mine = lax.all_to_all(snapshots, "rows", split_axis=1, concat_axis=0, tiled=True)
        block_rows = mine.shape[0]
        own_terms = split_terms(mine_kernel, (mine,), block_rows)
        theirs = partner_2(mine, "cols", bit_pos)
        return mine, theirs, own_terms + split_terms(rest_kernel, (mine, theirs), 2 * block_rows)

    sends = lay_out(snapshots, rows_n, chunks, [0]) + lay_out(snapshots, rows_n, chunks, list(range(1, chunks)))

    def laid(chunk):
        return sends[chunk]

    def spread(sent):
        got = lax.all_to_all(sent, "rows", split_axis=0, concat_axis=0)
        return got.reshape(rows_n * local_rows, piece)

    own_parts = [spread(laid(0))]
    other_parts = []
    for chunk in range(1, chunks):
        held = (own_parts[-1], laid(chunk)) + tuple(other_parts[-1:])
        held = lax.optimization_barrier(held)
        own_parts[-1] = held[0]
        if other_parts:
            other_parts[-1] = held[2]
        other_parts.append(partner_2(held[0], "cols", bit_pos))
        own_parts.append(spread(held[1]))
    other_parts.append(partner_2(own_parts[-1], "cols", bit_pos))
    own_full = jnp.zeros((rows_n * local_rows, width), snapshots.dtype)
    other_full = jnp.zeros((rows_n * local_rows, width), snapshots.dtype)
    terms = None
    for chunk, (mine, theirs) in enumerate(zip(own_parts, other_parts)):
        part, own_full, other_full = pair_terms_stored(mine, theirs, own_full, other_full, chunk)
        terms = part if terms is None else terms + part
    return own_full, other_full, terms


def unpack_terms(packed, width):
    row = lax.broadcasted_iota(jnp.int32, (width, width), 0)
    col = lax.broadcasted_iota(jnp.int32, (width, width), 1)
    shared = packed[:width]
    gram_mixed = packed[width : 2 * width]
    diag_theirs = packed[2 * width : 2 * width + 1]
    gram_mine = jnp.where(row <= col, shared, shared.T)
    gram_theirs = jnp.where(row > col, shared, jnp.where(row < col, shared.T, diag_theirs))
    return gram_mine, gram_mixed, gram_theirs


def assemble(terms, own_low):
    gram_mine, gram_mixed, gram_theirs = unpack_terms(row_total(terms), terms.shape[1])
    upper_left = jnp.where(own_low, gram_mine, gram_theirs)
    lower_right = jnp.where(own_low, gram_theirs, gram_mine)
    upper_right = jnp.where(own_low, gram_mixed, gram_mixed.T)
    top_rows = jnp.concatenate([upper_left, upper_right], 1)
    bottom_rows = jnp.concatenate([upper_right.T, lower_right], 1)
    return jnp.concatenate([top_rows, bottom_rows], 0)


def rotate_kernel(coef_ref, mine_ref, theirs_ref, out_ref):
    stacked = jnp.concatenate([mine_ref[...], theirs_ref[...]], 0)
    out_ref[...] = jnp.dot(
        coef_ref[...], stacked, precision=lax.Precision.HIGHEST, preferred_element_type=jnp.float32
    )


def rotate_part(columns_sel, own_low, mine, theirs):
    width, cells = mine.shape
    coef_mine = jnp.where(own_low, columns_sel[:width], columns_sel[width:])
    coef_theirs = jnp.where(own_low, columns_sel[width:], columns_sel[:width])
    coef = jnp.concatenate([coef_mine, coef_theirs], 0).T
    tile = min(cells, 2048)
    coef_spec = pl.BlockSpec((width, 2 * width), lambda step: (0, 0))
    cell_spec = pl.BlockSpec((width, tile), lambda step: (0, step))
    return pl.pallas_call(
        rotate_kernel,
        out_shape=jax.ShapeDtypeStruct((width, cells), jnp.float32),
        grid=(cells // tile,),
        in_specs=[coef_spec, cell_spec, cell_spec],
        out_specs=cell_spec,
        cost_estimate=pl.CostEstimate(
            flops=4 * width * width * cells, transcendentals=0, bytes_accessed=12 * width * cells
        ),
    )(coef, mine, theirs)


def shards(snapshots, pair_table):
    bit_count = lax.axis_size("cols").bit_length() - 1
    column = lax.axis_index("cols")
    mask_val = pair_table[0]
    bit_index = jnp.int32(0)
    for bit_pos in range(bit_count):
        bit_index = bit_index + (mask_val >> bit_pos & 1) * bit_pos
    partner = jnp.bitwise_xor(column, mask_val)
    own_low = column < partner
    branches = [functools.partial(exchange, bit_pos) for bit_pos in range(bit_count)]
    own_parts, other_parts, terms = lax.switch(bit_index, branches, snapshots)
    gram_full = assemble(terms, own_low)
    rotation = jacobi_pallas(gram_full)
    width = own_parts.shape[0]
    own_columns = jnp.where(own_low, rotation[:, :width], rotation[:, width:])
    return rotate_part(own_columns, own_low, own_parts, other_parts)


def solution(mesh):
    in_specs = (P(("cols", "rows"), None), P())
    out_specs = P("cols", "rows")
    return jax.shard_map(shards, mesh=mesh, in_specs=in_specs, out_specs=out_specs, check_vma=False)
```

```python
import functools

import jax
import jax.numpy as jnp
import numpy as np
from jax import lax
from jax.experimental import pallas as pl
from jax.experimental.pallas import tpu as pltpu
from jax.sharding import PartitionSpec as P

ROUNDS = 8


def partner_2(value, axis, bit):
    mask = 2**bit
    pairs = [(source, source ^ mask) for source in range(lax.axis_size(axis))]
    return lax.ppermute(value, axis, pairs)


def jacobi_kernel(gram_ref, rotation_ref):
    highest = lax.Precision.HIGHEST
    order_dim = gram_ref.shape[0]
    last_idx = order_dim - 1
    width = order_dim // 2
    gram = gram_ref[...]
    row_col = lax.broadcasted_iota(jnp.int32, (order_dim, 1), 0)
    row_full = lax.broadcasted_iota(jnp.int32, (order_dim, order_dim), 0)
    col_full = lax.broadcasted_iota(jnp.int32, (order_dim, order_dim), 1)
    eye = row_full == col_full
    rotation = None
    for round_idx in range(ROUNDS):
        fixed = round_idx % last_idx
        mirror = 2 * fixed - row_col
        mirror = jnp.where(mirror < 0, mirror + last_idx, mirror)
        partner = jnp.where(row_col == fixed, last_idx, jnp.where(row_col == last_idx, fixed, mirror))
        offset = row_col - fixed
        offset = jnp.where(offset < 0, offset + last_idx, offset)
        is_first = (row_col == last_idx) | ((row_col != fixed) & (offset >= 1) & (offset <= width - 1))
        swap = (col_full == partner).astype(jnp.float32)
        on_diag = jnp.where(eye, gram, 0.0)
        diag_own = jnp.sum(on_diag, axis=1, keepdims=True)
        diag_row = jnp.sum(on_diag, axis=0, keepdims=True)
        diag_mate = jnp.sum(swap * diag_row, axis=1, keepdims=True)
        picked = gram * swap
        cross_second = jnp.sum(picked, axis=1, keepdims=True)
        cross_row = jnp.sum(picked, axis=0, keepdims=True)
        cross_first = jnp.sum(jnp.where(eye, cross_row, 0.0), axis=1, keepdims=True)
        cross_val = jnp.where(is_first, cross_first, cross_second)
        spread = jnp.where(is_first, diag_mate - diag_own, diag_own - diag_mate)
        hypot_val = jnp.sqrt(spread * spread + 4.0 * cross_val * cross_val)
        denom = jnp.sqrt(2.0 * hypot_val * (hypot_val + jnp.abs(spread)))
        sign_val = jnp.where(spread >= 0.0, 1.0, -1.0)
        cosine = (hypot_val + jnp.abs(spread)) / denom
        sine_val = 2.0 * cross_val * sign_val / denom
        signed = jnp.where(is_first, sine_val, -sine_val)
        diag_part = jnp.where(eye, cosine, 0.0)
        turn = diag_part + swap * signed
        turn_t = diag_part - swap * signed
        gram = jnp.dot(
            turn_t,
            jnp.dot(gram, turn, precision=highest, preferred_element_type=jnp.float32),
            precision=highest,
            preferred_element_type=jnp.float32,
        )
        rotation = turn if rotation is None else jnp.dot(
            rotation, turn, precision=highest, preferred_element_type=jnp.float32
        )
    rotation_ref[...] = rotation

def jacobi_pallas(gram):
    return pl.pallas_call(
        jacobi_kernel,
        out_shape=jax.ShapeDtypeStruct(gram.shape, jnp.float32),
        in_specs=[pl.BlockSpec(memory_space=pltpu.VMEM)],
        out_specs=pl.BlockSpec(memory_space=pltpu.VMEM),
    )(gram)


def gram_kernel(mine_ref, theirs_ref, out_ref, acc_ref):
    step = pl.program_id(0)

    @pl.when(step == 0)
    def _():
        acc_ref[...] = jnp.zeros_like(acc_ref)

    stacked = jnp.concatenate([mine_ref[...], theirs_ref[...]], 0)
    acc_ref[...] += lax.dot_general(
        stacked,
        stacked,
        (((1,), (1,)), ((), ())),
        precision=lax.Precision.HIGHEST,
        preferred_element_type=jnp.float32,
    )

    @pl.when(step == pl.num_programs(0) - 1)
    def _():
        width = mine_ref.shape[0]
        row = lax.broadcasted_iota(jnp.int32, (width, width), 0)
        col = lax.broadcasted_iota(jnp.int32, (width, width), 1)
        gram_theirs = acc_ref[width:, width:]
        out_ref[:width, :] = jnp.where(row <= col, acc_ref[:width, :width], gram_theirs)
        out_ref[width : 2 * width, :] = acc_ref[:width, width:]
        diag_theirs = jnp.sum(jnp.where(row == col, gram_theirs, 0.0), axis=0, keepdims=True)
        out_ref[2 * width :, :] = jnp.broadcast_to(diag_theirs, (8, width))


def gram_store_kernel(mine_ref, theirs_ref, own_in, other_in, out_ref, own_ref, other_ref, acc_ref):
    del own_in, other_in
    gram_kernel(mine_ref, theirs_ref, out_ref, acc_ref)
    own_ref[...] = mine_ref[...]
    other_ref[...] = theirs_ref[...]


def pair_terms_stored(mine, theirs, own_full, other_full, chunk):
    width, piece = mine.shape
    cell_spec = pl.BlockSpec((width, piece), lambda step: (0, 0))
    full_spec = pl.BlockSpec((width, piece), lambda step: (0, chunk))
    return pl.pallas_call(
        gram_store_kernel,
        out_shape=[
            jax.ShapeDtypeStruct((2 * width + 8, width), jnp.float32),
            jax.ShapeDtypeStruct(own_full.shape, own_full.dtype),
            jax.ShapeDtypeStruct(other_full.shape, other_full.dtype),
        ],
        grid=(1,),
        in_specs=[cell_spec, cell_spec, pl.BlockSpec(memory_space=pl.ANY), pl.BlockSpec(memory_space=pl.ANY)],
        out_specs=[pl.BlockSpec((2 * width + 8, width), lambda step: (0, 0)), full_spec, full_spec],
        scratch_shapes=[pltpu.VMEM((2 * width, 2 * width), jnp.float32)],
        input_output_aliases={2: 1, 3: 2},
        cost_estimate=pl.CostEstimate(
            flops=8 * width * width * piece, transcendentals=0, bytes_accessed=16 * width * piece
        ),
    )(mine, theirs, own_full, other_full)


def mine_kernel(mine_ref, out_ref, acc_ref):
    step = pl.program_id(0)

    @pl.when(step == 0)
    def _():
        acc_ref[...] = jnp.zeros_like(acc_ref)

    acc_ref[...] += lax.dot_general(
        mine_ref[...],
        mine_ref[...],
        (((1,), (1,)), ((), ())),
        precision=lax.Precision.HIGHEST,
        preferred_element_type=jnp.float32,
    )

    @pl.when(step == pl.num_programs(0) - 1)
    def _():
        width = mine_ref.shape[0]
        row = lax.broadcasted_iota(jnp.int32, (width, width), 0)
        col = lax.broadcasted_iota(jnp.int32, (width, width), 1)
        out_ref[:width, :] = jnp.where(row <= col, acc_ref[...], 0.0)
        out_ref[width:, :] = jnp.zeros((width + 8, width), jnp.float32)


def rest_kernel(mine_ref, theirs_ref, out_ref, acc_ref):
    step = pl.program_id(0)

    @pl.when(step == 0)
    def _():
        acc_ref[...] = jnp.zeros_like(acc_ref)

    stacked = jnp.concatenate([mine_ref[...], theirs_ref[...]], 0)
    acc_ref[...] += lax.dot_general(
        theirs_ref[...],
        stacked,
        (((1,), (1,)), ((), ())),
        precision=lax.Precision.HIGHEST,
        preferred_element_type=jnp.float32,
    )

    @pl.when(step == pl.num_programs(0) - 1)
    def _():
        width = mine_ref.shape[0]
        row = lax.broadcasted_iota(jnp.int32, (width, width), 0)
        col = lax.broadcasted_iota(jnp.int32, (width, width), 1)
        gram_theirs = acc_ref[:, width:]
        out_ref[:width, :] = jnp.where(row > col, gram_theirs, 0.0)
        out_ref[width : 2 * width, :] = acc_ref[:, :width].T
        diag_theirs = jnp.sum(jnp.where(row == col, gram_theirs, 0.0), axis=0, keepdims=True)
        out_ref[2 * width :, :] = jnp.broadcast_to(diag_theirs, (8, width))


def split_terms(kernel, operands, acc_cols):
    width, cells = operands[0].shape
    tile = min(cells, 2048)
    cell_spec = pl.BlockSpec((width, tile), lambda step: (0, step))
    return pl.pallas_call(
        kernel,
        out_shape=jax.ShapeDtypeStruct((2 * width + 8, width), jnp.float32),
        grid=(cells // tile,),
        in_specs=[cell_spec] * len(operands),
        out_specs=pl.BlockSpec((2 * width + 8, width), lambda step: (0, 0)),
        scratch_shapes=[pltpu.VMEM((width, acc_cols), jnp.float32)],
        cost_estimate=pl.CostEstimate(
            flops=2 * acc_cols * width * cells,
            transcendentals=0,
            bytes_accessed=4 * width * cells * len(operands),
        ),
    )(*operands)


def pair_terms(mine, theirs):
    width, cells = mine.shape
    tile = min(cells, 2048)
    cell_spec = pl.BlockSpec((width, tile), lambda step: (0, step))
    return pl.pallas_call(
        gram_kernel,
        out_shape=jax.ShapeDtypeStruct((2 * width + 8, width), jnp.float32),
        grid=(cells // tile,),
        in_specs=[cell_spec, cell_spec],
        out_specs=pl.BlockSpec((2 * width + 8, width), lambda step: (0, 0)),
        scratch_shapes=[pltpu.VMEM((2 * width, 2 * width), jnp.float32)],
        cost_estimate=pl.CostEstimate(
            flops=8 * width * width * cells, transcendentals=0, bytes_accessed=8 * width * cells
        ),
    )(mine, theirs)


def row_total(part):
    count = lax.axis_size("rows")
    bit = 1
    while bit < count:
        pairs = [(source, source ^ bit) for source in range(count)]
        part = part + lax.ppermute(part, "rows", pairs)
        bit *= 2
    return part


CHUNKS = 4


def lay_kernel(chunk_ids, piece, source_ref, *out_refs):
    if len(chunk_ids) == 1:
        out_refs[0][...] = source_ref[...]
        return
    for chunk, out_ref in zip(chunk_ids, out_refs):
        out_ref[...] = source_ref[:, chunk * piece : (chunk + 1) * piece]


def lay_out(snapshots, rows_n, chunks, chunk_ids):
    local_rows, cells = snapshots.shape
    width = cells // rows_n
    piece = width // chunks
    out_spec = pl.BlockSpec((None, local_rows, piece), lambda dest: (dest, 0, 0))
    return pl.pallas_call(
        functools.partial(lay_kernel, tuple(chunk_ids), piece),
        out_shape=[jax.ShapeDtypeStruct((rows_n, local_rows, piece), snapshots.dtype)] * len(chunk_ids),
        grid=(rows_n,),
        in_specs=[
            pl.BlockSpec((local_rows, piece), lambda dest: (0, dest * chunks + chunk_ids[0]))
            if len(chunk_ids) == 1
            else pl.BlockSpec((local_rows, width), lambda dest: (0, dest))
        ],
        out_specs=[out_spec] * len(chunk_ids),
        cost_estimate=pl.CostEstimate(
            flops=0, transcendentals=0, bytes_accessed=8 * local_rows * piece * rows_n * len(chunk_ids)
        ),
    )(snapshots)


def exchange(bit_pos, snapshots):
    chunks = 1 if bit_pos == 0 else CHUNKS
    rows_n = lax.axis_size("rows")
    local_rows, cells = snapshots.shape
    width = cells // rows_n
    piece = width // chunks

    if chunks == 1:
        mine = lax.all_to_all(snapshots, "rows", split_axis=1, concat_axis=0, tiled=True)
        block_rows = mine.shape[0]
        own_terms = split_terms(mine_kernel, (mine,), block_rows)
        theirs = partner_2(mine, "cols", bit_pos)
        return mine, theirs, own_terms + split_terms(rest_kernel, (mine, theirs), 2 * block_rows)

    sends = lay_out(snapshots, rows_n, chunks, [0]) + lay_out(snapshots, rows_n, chunks, list(range(1, chunks)))

    def laid(chunk):
        return sends[chunk]

    def spread(sent):
        got = lax.all_to_all(sent, "rows", split_axis=0, concat_axis=0)
        return got.reshape(rows_n * local_rows, piece)

    own_parts = [spread(laid(0))]
    other_parts = []
    for chunk in range(1, chunks):
        held = (own_parts[-1], laid(chunk)) + tuple(other_parts[-1:])
        held = lax.optimization_barrier(held)
        own_parts[-1] = held[0]
        if other_parts:
            other_parts[-1] = held[2]
        other_parts.append(partner_2(held[0], "cols", bit_pos))
        own_parts.append(spread(held[1]))
    other_parts.append(partner_2(own_parts[-1], "cols", bit_pos))
    own_full = jnp.zeros((rows_n * local_rows, width), snapshots.dtype)
    other_full = jnp.zeros((rows_n * local_rows, width), snapshots.dtype)
    terms = None
    for chunk, (mine, theirs) in enumerate(zip(own_parts, other_parts)):
        part, own_full, other_full = pair_terms_stored(mine, theirs, own_full, other_full, chunk)
        terms = part if terms is None else terms + part
    return own_full, other_full, terms


def unpack_terms(packed, width):
    row = lax.broadcasted_iota(jnp.int32, (width, width), 0)
    col = lax.broadcasted_iota(jnp.int32, (width, width), 1)
    shared = packed[:width]
    gram_mixed = packed[width : 2 * width]
    diag_theirs = packed[2 * width : 2 * width + 1]
    gram_mine = jnp.where(row <= col, shared, shared.T)
    gram_theirs = jnp.where(row > col, shared, jnp.where(row < col, shared.T, diag_theirs))
    return gram_mine, gram_mixed, gram_theirs


def assemble(terms, own_low):
    gram_mine, gram_mixed, gram_theirs = unpack_terms(row_total(terms), terms.shape[1])
    upper_left = jnp.where(own_low, gram_mine, gram_theirs)
    lower_right = jnp.where(own_low, gram_theirs, gram_mine)
    upper_right = jnp.where(own_low, gram_mixed, gram_mixed.T)
    top_rows = jnp.concatenate([upper_left, upper_right], 1)
    bottom_rows = jnp.concatenate([upper_right.T, lower_right], 1)
    return jnp.concatenate([top_rows, bottom_rows], 0)


def rotate_kernel(coef_ref, mine_ref, theirs_ref, out_ref):
    stacked = jnp.concatenate([mine_ref[...], theirs_ref[...]], 0)
    out_ref[...] = jnp.dot(
        coef_ref[...], stacked, precision=lax.Precision.HIGHEST, preferred_element_type=jnp.float32
    )


def rotate_part(columns_sel, own_low, mine, theirs):
    width, cells = mine.shape
    coef_mine = jnp.where(own_low, columns_sel[:width], columns_sel[width:])
    coef_theirs = jnp.where(own_low, columns_sel[width:], columns_sel[:width])
    coef = jnp.concatenate([coef_mine, coef_theirs], 0).T
    tile = min(cells, 2048)
    coef_spec = pl.BlockSpec((width, 2 * width), lambda step: (0, 0))
    cell_spec = pl.BlockSpec((width, tile), lambda step: (0, step))
    return pl.pallas_call(
        rotate_kernel,
        out_shape=jax.ShapeDtypeStruct((width, cells), jnp.float32),
        grid=(cells // tile,),
        in_specs=[coef_spec, cell_spec, cell_spec],
        out_specs=cell_spec,
        cost_estimate=pl.CostEstimate(
            flops=4 * width * width * cells, transcendentals=0, bytes_accessed=12 * width * cells
        ),
    )(coef, mine, theirs)


def shards(snapshots, pair_table):
    bit_count = lax.axis_size("cols").bit_length() - 1
    column = lax.axis_index("cols")
    mask_val = pair_table[0]
    bit_index = jnp.int32(0)
    for bit_pos in range(bit_count):
        bit_index = bit_index + (mask_val >> bit_pos & 1) * bit_pos
    partner = jnp.bitwise_xor(column, mask_val)
    own_low = column < partner
    branches = [functools.partial(exchange, bit_pos) for bit_pos in range(bit_count)]
    own_parts, other_parts, terms = lax.switch(bit_index, branches, snapshots)
    gram_full = assemble(terms, own_low)
    rotation = jacobi_pallas(gram_full)
    width = own_parts.shape[0]
    own_columns = jnp.where(own_low, rotation[:, :width], rotation[:, width:])
    return rotate_part(own_columns, own_low, own_parts, other_parts)


def solution(mesh):
    in_specs = (P(("cols", "rows"), None), P())
    out_specs = P("cols", "rows")
    return jax.shard_map(shards, mesh=mesh, in_specs=in_specs, out_specs=out_specs, check_vma=False)
```

```python
import functools

import jax
import jax.numpy as jnp
import numpy as np
from jax import lax
from jax.experimental import pallas as pl
from jax.experimental.pallas import tpu as pltpu
from jax.sharding import PartitionSpec as P

ROUNDS = 8


def partner_2(value, axis, bit):
    mask = 2**bit
    pairs = [(source, source ^ mask) for source in range(lax.axis_size(axis))]
    return lax.ppermute(value, axis, pairs)


def jacobi_kernel(gram_ref, rotation_ref):
    highest = lax.Precision.HIGHEST
    order_dim = gram_ref.shape[0]
    last_idx = order_dim - 1
    width = order_dim // 2
    gram = gram_ref[...]
    row_col = lax.broadcasted_iota(jnp.int32, (order_dim, 1), 0)
    row_full = lax.broadcasted_iota(jnp.int32, (order_dim, order_dim), 0)
    col_full = lax.broadcasted_iota(jnp.int32, (order_dim, order_dim), 1)
    eye = row_full == col_full
    rotation = None
    for round_idx in range(ROUNDS):
        fixed = round_idx % last_idx
        mirror = 2 * fixed - row_col
        mirror = jnp.where(mirror < 0, mirror + last_idx, mirror)
        partner = jnp.where(row_col == fixed, last_idx, jnp.where(row_col == last_idx, fixed, mirror))
        offset = row_col - fixed
        offset = jnp.where(offset < 0, offset + last_idx, offset)
        is_first = (row_col == last_idx) | ((row_col != fixed) & (offset >= 1) & (offset <= width - 1))
        swap = (col_full == partner).astype(jnp.float32)
        on_diag = jnp.where(eye, gram, 0.0)
        diag_own = jnp.sum(on_diag, axis=1, keepdims=True)
        diag_row = jnp.sum(on_diag, axis=0, keepdims=True)
        diag_mate = jnp.sum(swap * diag_row, axis=1, keepdims=True)
        picked = gram * swap
        cross_second = jnp.sum(picked, axis=1, keepdims=True)
        cross_row = jnp.sum(picked, axis=0, keepdims=True)
        cross_first = jnp.sum(jnp.where(eye, cross_row, 0.0), axis=1, keepdims=True)
        cross_val = jnp.where(is_first, cross_first, cross_second)
        spread = jnp.where(is_first, diag_mate - diag_own, diag_own - diag_mate)
        hypot_val = jnp.sqrt(spread * spread + 4.0 * cross_val * cross_val)
        denom = jnp.sqrt(2.0 * hypot_val * (hypot_val + jnp.abs(spread)))
        sign_val = jnp.where(spread >= 0.0, 1.0, -1.0)
        cosine = (hypot_val + jnp.abs(spread)) / denom
        sine_val = 2.0 * cross_val * sign_val / denom
        signed = jnp.where(is_first, sine_val, -sine_val)
        diag_part = jnp.where(eye, cosine, 0.0)
        turn = diag_part + swap * signed
        turn_t = diag_part - swap * signed
        gram = jnp.dot(
            turn_t,
            jnp.dot(gram, turn, precision=highest, preferred_element_type=jnp.float32),
            precision=highest,
            preferred_element_type=jnp.float32,
        )
        rotation = turn if rotation is None else jnp.dot(
            rotation, turn, precision=highest, preferred_element_type=jnp.float32
        )
    rotation_ref[...] = rotation

def jacobi_pallas(gram):
    return pl.pallas_call(
        jacobi_kernel,
        out_shape=jax.ShapeDtypeStruct(gram.shape, jnp.float32),
        in_specs=[pl.BlockSpec(memory_space=pltpu.VMEM)],
        out_specs=pl.BlockSpec(memory_space=pltpu.VMEM),
    )(gram)


def gram_kernel(mine_ref, theirs_ref, out_ref, acc_ref):
    step = pl.program_id(0)

    @pl.when(step == 0)
    def _():
        acc_ref[...] = jnp.zeros_like(acc_ref)

    stacked = jnp.concatenate([mine_ref[...], theirs_ref[...]], 0)
    acc_ref[...] += lax.dot_general(
        stacked,
        stacked,
        (((1,), (1,)), ((), ())),
        precision=lax.Precision.HIGHEST,
        preferred_element_type=jnp.float32,
    )

    @pl.when(step == pl.num_programs(0) - 1)
    def _():
        width = mine_ref.shape[0]
        row = lax.broadcasted_iota(jnp.int32, (width, width), 0)
        col = lax.broadcasted_iota(jnp.int32, (width, width), 1)
        gram_theirs = acc_ref[width:, width:]
        out_ref[:width, :] = jnp.where(row <= col, acc_ref[:width, :width], gram_theirs)
        out_ref[width : 2 * width, :] = acc_ref[:width, width:]
        diag_theirs = jnp.sum(jnp.where(row == col, gram_theirs, 0.0), axis=0, keepdims=True)
        out_ref[2 * width :, :] = jnp.broadcast_to(diag_theirs, (8, width))


def gram_store_kernel(mine_ref, theirs_ref, own_in, other_in, out_ref, own_ref, other_ref, acc_ref):
    del own_in, other_in
    gram_kernel(mine_ref, theirs_ref, out_ref, acc_ref)
    own_ref[...] = mine_ref[...]
    other_ref[...] = theirs_ref[...]


def rest_store_kernel(mine_ref, theirs_ref, own_in, other_in, out_ref, own_ref, other_ref, acc_ref):
    del own_in, other_in
    rest_kernel(mine_ref, theirs_ref, out_ref, acc_ref)
    own_ref[...] = mine_ref[...]
    other_ref[...] = theirs_ref[...]


def pair_terms_stored(mine, theirs, own_full, other_full, chunk, kernel=None, acc_rows=None):
    width, piece = mine.shape
    kernel = gram_store_kernel if kernel is None else kernel
    acc_shape = (2 * width, 2 * width) if acc_rows is None else (acc_rows, width)
    cell_spec = pl.BlockSpec((width, piece), lambda step: (0, 0))
    full_spec = pl.BlockSpec((width, piece), lambda step: (0, chunk))
    return pl.pallas_call(
        kernel,
        out_shape=[
            jax.ShapeDtypeStruct((2 * width + 8, width), jnp.float32),
            jax.ShapeDtypeStruct(own_full.shape, own_full.dtype),
            jax.ShapeDtypeStruct(other_full.shape, other_full.dtype),
        ],
        grid=(1,),
        in_specs=[cell_spec, cell_spec, pl.BlockSpec(memory_space=pl.ANY), pl.BlockSpec(memory_space=pl.ANY)],
        out_specs=[pl.BlockSpec((2 * width + 8, width), lambda step: (0, 0)), full_spec, full_spec],
        scratch_shapes=[pltpu.VMEM(acc_shape, jnp.float32)],
        input_output_aliases={2: 1, 3: 2},
        cost_estimate=pl.CostEstimate(
            flops=8 * width * width * piece, transcendentals=0, bytes_accessed=16 * width * piece
        ),
    )(mine, theirs, own_full, other_full)


def mine_kernel(mine_ref, out_ref, acc_ref):
    step = pl.program_id(0)

    @pl.when(step == 0)
    def _():
        acc_ref[...] = jnp.zeros_like(acc_ref)

    acc_ref[...] += lax.dot_general(
        mine_ref[...],
        mine_ref[...],
        (((1,), (1,)), ((), ())),
        precision=lax.Precision.HIGHEST,
        preferred_element_type=jnp.float32,
    )

    @pl.when(step == pl.num_programs(0) - 1)
    def _():
        width = mine_ref.shape[0]
        row = lax.broadcasted_iota(jnp.int32, (width, width), 0)
        col = lax.broadcasted_iota(jnp.int32, (width, width), 1)
        out_ref[:width, :] = jnp.where(row <= col, acc_ref[...], 0.0)
        out_ref[width:, :] = jnp.zeros((width + 8, width), jnp.float32)


def rest_kernel(mine_ref, theirs_ref, out_ref, acc_ref):
    step = pl.program_id(0)

    @pl.when(step == 0)
    def _():
        acc_ref[...] = jnp.zeros_like(acc_ref)

    stacked = jnp.concatenate([mine_ref[...], theirs_ref[...]], 0)
    acc_ref[...] += lax.dot_general(
        stacked,
        theirs_ref[...],
        (((1,), (1,)), ((), ())),
        precision=lax.Precision.HIGHEST,
        preferred_element_type=jnp.float32,
    )

    @pl.when(step == pl.num_programs(0) - 1)
    def _():
        width = mine_ref.shape[0]
        row = lax.broadcasted_iota(jnp.int32, (width, width), 0)
        col = lax.broadcasted_iota(jnp.int32, (width, width), 1)
        gram_theirs = acc_ref[width:, :]
        out_ref[:width, :] = jnp.where(row > col, gram_theirs, 0.0)
        out_ref[width : 2 * width, :] = acc_ref[:width, :]
        diag_theirs = jnp.sum(jnp.where(row == col, gram_theirs, 0.0), axis=0, keepdims=True)
        out_ref[2 * width :, :] = jnp.broadcast_to(diag_theirs, (8, width))


def split_terms(kernel, operands, acc_rows):
    width, cells = operands[0].shape
    tile = min(cells, 2048)
    cell_spec = pl.BlockSpec((width, tile), lambda step: (0, step))
    return pl.pallas_call(
        kernel,
        out_shape=jax.ShapeDtypeStruct((2 * width + 8, width), jnp.float32),
        grid=(cells // tile,),
        in_specs=[cell_spec] * len(operands),
        out_specs=pl.BlockSpec((2 * width + 8, width), lambda step: (0, 0)),
        scratch_shapes=[pltpu.VMEM((acc_rows, width), jnp.float32)],
        cost_estimate=pl.CostEstimate(
            flops=2 * acc_rows * width * cells,
            transcendentals=0,
            bytes_accessed=4 * width * cells * len(operands),
        ),
    )(*operands)


def pair_terms(mine, theirs):
    width, cells = mine.shape
    tile = min(cells, 2048)
    cell_spec = pl.BlockSpec((width, tile), lambda step: (0, step))
    return pl.pallas_call(
        gram_kernel,
        out_shape=jax.ShapeDtypeStruct((2 * width + 8, width), jnp.float32),
        grid=(cells // tile,),
        in_specs=[cell_spec, cell_spec],
        out_specs=pl.BlockSpec((2 * width + 8, width), lambda step: (0, 0)),
        scratch_shapes=[pltpu.VMEM((2 * width, 2 * width), jnp.float32)],
        cost_estimate=pl.CostEstimate(
            flops=8 * width * width * cells, transcendentals=0, bytes_accessed=8 * width * cells
        ),
    )(mine, theirs)


def row_total(part):
    count = lax.axis_size("rows")
    bit = 1
    while bit < count:
        pairs = [(source, source ^ bit) for source in range(count)]
        part = part + lax.ppermute(part, "rows", pairs)
        bit *= 2
    return part


CHUNKS = 4


def lay_kernel(chunk_ids, piece, source_ref, *out_refs):
    if len(chunk_ids) == 1:
        out_refs[0][...] = source_ref[...]
        return
    for chunk, out_ref in zip(chunk_ids, out_refs):
        out_ref[...] = source_ref[:, chunk * piece : (chunk + 1) * piece]


def lay_out(snapshots, rows_n, chunks, chunk_ids):
    local_rows, cells = snapshots.shape
    width = cells // rows_n
    piece = width // chunks
    out_spec = pl.BlockSpec((None, local_rows, piece), lambda dest: (dest, 0, 0))
    return pl.pallas_call(
        functools.partial(lay_kernel, tuple(chunk_ids), piece),
        out_shape=[jax.ShapeDtypeStruct((rows_n, local_rows, piece), snapshots.dtype)] * len(chunk_ids),
        grid=(rows_n,),
        in_specs=[
            pl.BlockSpec((local_rows, piece), lambda dest: (0, dest * chunks + chunk_ids[0]))
            if len(chunk_ids) == 1
            else pl.BlockSpec((local_rows, width), lambda dest: (0, dest))
        ],
        out_specs=[out_spec] * len(chunk_ids),
        cost_estimate=pl.CostEstimate(
            flops=0, transcendentals=0, bytes_accessed=8 * local_rows * piece * rows_n * len(chunk_ids)
        ),
    )(snapshots)


def exchange(bit_pos, snapshots):
    chunks = 1 if bit_pos == 0 else CHUNKS
    rows_n = lax.axis_size("rows")
    local_rows, cells = snapshots.shape
    width = cells // rows_n
    piece = width // chunks

    if chunks == 1:
        mine = lax.all_to_all(snapshots, "rows", split_axis=1, concat_axis=0, tiled=True)
        block_rows = mine.shape[0]
        own_terms = split_terms(mine_kernel, (mine,), block_rows)
        theirs = partner_2(mine, "cols", bit_pos)
        return mine, theirs, own_terms + split_terms(rest_kernel, (mine, theirs), 2 * block_rows)

    sends = lay_out(snapshots, rows_n, chunks, [0]) + lay_out(snapshots, rows_n, chunks, list(range(1, chunks)))

    def laid(chunk):
        return sends[chunk]

    def spread(sent):
        got = lax.all_to_all(sent, "rows", split_axis=0, concat_axis=0)
        return got.reshape(rows_n * local_rows, piece)

    own_parts = [spread(laid(0))]
    other_parts = []
    for chunk in range(1, chunks):
        held = (own_parts[-1], laid(chunk)) + tuple(other_parts[-1:])
        held = lax.optimization_barrier(held)
        own_parts[-1] = held[0]
        if other_parts:
            other_parts[-1] = held[2]
        other_parts.append(partner_2(held[0], "cols", bit_pos))
        own_parts.append(spread(held[1]))
    block_rows = rows_n * local_rows
    last_own = split_terms(mine_kernel, (own_parts[-1],), block_rows)
    other_parts.append(partner_2(own_parts[-1], "cols", bit_pos))
    own_full = jnp.zeros((block_rows, width), snapshots.dtype)
    other_full = jnp.zeros((block_rows, width), snapshots.dtype)
    terms = last_own
    for chunk, (mine, theirs) in enumerate(zip(own_parts, other_parts)):
        if chunk == chunks - 1:
            part, own_full, other_full = pair_terms_stored(
                mine, theirs, own_full, other_full, chunk, rest_store_kernel, 2 * block_rows
            )
        else:
            part, own_full, other_full = pair_terms_stored(mine, theirs, own_full, other_full, chunk)
        terms = terms + part
    return own_full, other_full, terms


def unpack_terms(packed, width):
    row = lax.broadcasted_iota(jnp.int32, (width, width), 0)
    col = lax.broadcasted_iota(jnp.int32, (width, width), 1)
    shared = packed[:width]
    gram_mixed = packed[width : 2 * width]
    diag_theirs = packed[2 * width : 2 * width + 1]
    gram_mine = jnp.where(row <= col, shared, shared.T)
    gram_theirs = jnp.where(row > col, shared, jnp.where(row < col, shared.T, diag_theirs))
    return gram_mine, gram_mixed, gram_theirs


def assemble(terms, own_low):
    gram_mine, gram_mixed, gram_theirs = unpack_terms(row_total(terms), terms.shape[1])
    upper_left = jnp.where(own_low, gram_mine, gram_theirs)
    lower_right = jnp.where(own_low, gram_theirs, gram_mine)
    upper_right = jnp.where(own_low, gram_mixed, gram_mixed.T)
    top_rows = jnp.concatenate([upper_left, upper_right], 1)
    bottom_rows = jnp.concatenate([upper_right.T, lower_right], 1)
    return jnp.concatenate([top_rows, bottom_rows], 0)


def rotate_kernel(coef_ref, mine_ref, theirs_ref, out_ref):
    stacked = jnp.concatenate([mine_ref[...], theirs_ref[...]], 0)
    out_ref[...] = jnp.dot(
        coef_ref[...], stacked, precision=lax.Precision.HIGHEST, preferred_element_type=jnp.float32
    )


def rotate_part(columns_sel, own_low, mine, theirs):
    width, cells = mine.shape
    coef_mine = jnp.where(own_low, columns_sel[:width], columns_sel[width:])
    coef_theirs = jnp.where(own_low, columns_sel[width:], columns_sel[:width])
    coef = jnp.concatenate([coef_mine, coef_theirs], 0).T
    tile = min(cells, 2048)
    coef_spec = pl.BlockSpec((width, 2 * width), lambda step: (0, 0))
    cell_spec = pl.BlockSpec((width, tile), lambda step: (0, step))
    return pl.pallas_call(
        rotate_kernel,
        out_shape=jax.ShapeDtypeStruct((width, cells), jnp.float32),
        grid=(cells // tile,),
        in_specs=[coef_spec, cell_spec, cell_spec],
        out_specs=cell_spec,
        cost_estimate=pl.CostEstimate(
            flops=4 * width * width * cells, transcendentals=0, bytes_accessed=12 * width * cells
        ),
    )(coef, mine, theirs)


def shards(snapshots, pair_table):
    bit_count = lax.axis_size("cols").bit_length() - 1
    column = lax.axis_index("cols")
    mask_val = pair_table[0]
    bit_index = jnp.int32(0)
    for bit_pos in range(bit_count):
        bit_index = bit_index + (mask_val >> bit_pos & 1) * bit_pos
    partner = jnp.bitwise_xor(column, mask_val)
    own_low = column < partner
    branches = [functools.partial(exchange, bit_pos) for bit_pos in range(bit_count)]
    own_parts, other_parts, terms = lax.switch(bit_index, branches, snapshots)
    gram_full = assemble(terms, own_low)
    rotation = jacobi_pallas(gram_full)
    width = own_parts.shape[0]
    own_columns = jnp.where(own_low, rotation[:, :width], rotation[:, width:])
    return rotate_part(own_columns, own_low, own_parts, other_parts)


def solution(mesh):
    in_specs = (P(("cols", "rows"), None), P())
    out_specs = P("cols", "rows")
    return jax.shard_map(shards, mesh=mesh, in_specs=in_specs, out_specs=out_specs, check_vma=False)
```

```python
import functools

import jax
import jax.numpy as jnp
import numpy as np
from jax import lax
from jax.experimental import pallas as pl
from jax.experimental.pallas import tpu as pltpu
from jax.sharding import PartitionSpec as P

ROUNDS = 8


def partner_2(value, axis, bit):
    mask = 2**bit
    pairs = [(source, source ^ mask) for source in range(lax.axis_size(axis))]
    return lax.ppermute(value, axis, pairs)


def jacobi_kernel(gram_ref, rotation_ref):
    highest = lax.Precision.HIGHEST
    order_dim = gram_ref.shape[0]
    last_idx = order_dim - 1
    width = order_dim // 2
    gram = gram_ref[...]
    row_col = lax.broadcasted_iota(jnp.int32, (order_dim, 1), 0)
    row_full = lax.broadcasted_iota(jnp.int32, (order_dim, order_dim), 0)
    col_full = lax.broadcasted_iota(jnp.int32, (order_dim, order_dim), 1)
    eye = row_full == col_full
    rotation = None
    for round_idx in range(ROUNDS):
        fixed = round_idx % last_idx
        mirror = 2 * fixed - row_col
        mirror = jnp.where(mirror < 0, mirror + last_idx, mirror)
        partner = jnp.where(row_col == fixed, last_idx, jnp.where(row_col == last_idx, fixed, mirror))
        offset = row_col - fixed
        offset = jnp.where(offset < 0, offset + last_idx, offset)
        is_first = (row_col == last_idx) | ((row_col != fixed) & (offset >= 1) & (offset <= width - 1))
        swap = (col_full == partner).astype(jnp.float32)
        on_diag = jnp.where(eye, gram, 0.0)
        diag_own = jnp.sum(on_diag, axis=1, keepdims=True)
        diag_row = jnp.sum(on_diag, axis=0, keepdims=True)
        diag_mate = jnp.sum(swap * diag_row, axis=1, keepdims=True)
        picked = gram * swap
        cross_second = jnp.sum(picked, axis=1, keepdims=True)
        cross_row = jnp.sum(picked, axis=0, keepdims=True)
        cross_first = jnp.sum(jnp.where(eye, cross_row, 0.0), axis=1, keepdims=True)
        cross_val = jnp.where(is_first, cross_first, cross_second)
        spread = jnp.where(is_first, diag_mate - diag_own, diag_own - diag_mate)
        hypot_val = jnp.sqrt(spread * spread + 4.0 * cross_val * cross_val)
        denom = jnp.sqrt(2.0 * hypot_val * (hypot_val + jnp.abs(spread)))
        sign_val = jnp.where(spread >= 0.0, 1.0, -1.0)
        cosine = (hypot_val + jnp.abs(spread)) / denom
        sine_val = 2.0 * cross_val * sign_val / denom
        signed = jnp.where(is_first, sine_val, -sine_val)
        diag_part = jnp.where(eye, cosine, 0.0)
        turn = diag_part + swap * signed
        turn_t = diag_part - swap * signed
        gram = jnp.dot(
            turn_t,
            jnp.dot(gram, turn, precision=highest, preferred_element_type=jnp.float32),
            precision=highest,
            preferred_element_type=jnp.float32,
        )
        rotation = turn if rotation is None else jnp.dot(
            rotation, turn, precision=highest, preferred_element_type=jnp.float32
        )
    rotation_ref[...] = rotation

def jacobi_pallas(gram):
    return pl.pallas_call(
        jacobi_kernel,
        out_shape=jax.ShapeDtypeStruct(gram.shape, jnp.float32),
        in_specs=[pl.BlockSpec(memory_space=pltpu.VMEM)],
        out_specs=pl.BlockSpec(memory_space=pltpu.VMEM),
    )(gram)


def gram_kernel(mine_ref, theirs_ref, out_ref, acc_ref):
    step = pl.program_id(0)

    @pl.when(step == 0)
    def _():
        acc_ref[...] = jnp.zeros_like(acc_ref)

    stacked = jnp.concatenate([mine_ref[...], theirs_ref[...]], 0)
    acc_ref[...] += lax.dot_general(
        stacked,
        stacked,
        (((1,), (1,)), ((), ())),
        precision=lax.Precision.HIGHEST,
        preferred_element_type=jnp.float32,
    )

    @pl.when(step == pl.num_programs(0) - 1)
    def _():
        width = mine_ref.shape[0]
        row = lax.broadcasted_iota(jnp.int32, (width, width), 0)
        col = lax.broadcasted_iota(jnp.int32, (width, width), 1)
        gram_theirs = acc_ref[width:, width:]
        out_ref[:width, :] = jnp.where(row <= col, acc_ref[:width, :width], gram_theirs)
        out_ref[width : 2 * width, :] = acc_ref[:width, width:]
        diag_theirs = jnp.sum(jnp.where(row == col, gram_theirs, 0.0), axis=0, keepdims=True)
        out_ref[2 * width :, :] = jnp.broadcast_to(diag_theirs, (8, width))


def gram_store_kernel(mine_ref, theirs_ref, own_in, other_in, out_ref, own_ref, other_ref, acc_ref):
    del own_in, other_in
    gram_kernel(mine_ref, theirs_ref, out_ref, acc_ref)
    own_ref[...] = mine_ref[...]
    other_ref[...] = theirs_ref[...]


def pair_terms_stored(mine, theirs, own_full, other_full, chunk):
    width, piece = mine.shape
    cell_spec = pl.BlockSpec((width, piece), lambda step: (0, 0))
    full_spec = pl.BlockSpec((width, piece), lambda step: (0, chunk))
    return pl.pallas_call(
        gram_store_kernel,
        out_shape=[
            jax.ShapeDtypeStruct((2 * width + 8, width), jnp.float32),
            jax.ShapeDtypeStruct(own_full.shape, own_full.dtype),
            jax.ShapeDtypeStruct(other_full.shape, other_full.dtype),
        ],
        grid=(1,),
        in_specs=[cell_spec, cell_spec, pl.BlockSpec(memory_space=pl.ANY), pl.BlockSpec(memory_space=pl.ANY)],
        out_specs=[pl.BlockSpec((2 * width + 8, width), lambda step: (0, 0)), full_spec, full_spec],
        scratch_shapes=[pltpu.VMEM((2 * width, 2 * width), jnp.float32)],
        input_output_aliases={2: 1, 3: 2},
        cost_estimate=pl.CostEstimate(
            flops=8 * width * width * piece, transcendentals=0, bytes_accessed=16 * width * piece
        ),
    )(mine, theirs, own_full, other_full)


def mine_kernel(mine_ref, out_ref, acc_ref):
    step = pl.program_id(0)

    @pl.when(step == 0)
    def _():
        acc_ref[...] = jnp.zeros_like(acc_ref)

    acc_ref[...] += lax.dot_general(
        mine_ref[...],
        mine_ref[...],
        (((1,), (1,)), ((), ())),
        precision=lax.Precision.HIGHEST,
        preferred_element_type=jnp.float32,
    )

    @pl.when(step == pl.num_programs(0) - 1)
    def _():
        width = mine_ref.shape[0]
        row = lax.broadcasted_iota(jnp.int32, (width, width), 0)
        col = lax.broadcasted_iota(jnp.int32, (width, width), 1)
        out_ref[:width, :] = jnp.where(row <= col, acc_ref[...], 0.0)
        out_ref[width:, :] = jnp.zeros((width + 8, width), jnp.float32)


def rest_kernel(mine_ref, theirs_ref, out_ref, acc_ref):
    step = pl.program_id(0)

    @pl.when(step == 0)
    def _():
        acc_ref[...] = jnp.zeros_like(acc_ref)

    stacked = jnp.concatenate([mine_ref[...], theirs_ref[...]], 0)
    acc_ref[...] += lax.dot_general(
        stacked,
        theirs_ref[...],
        (((1,), (1,)), ((), ())),
        precision=lax.Precision.HIGHEST,
        preferred_element_type=jnp.float32,
    )

    @pl.when(step == pl.num_programs(0) - 1)
    def _():
        width = mine_ref.shape[0]
        row = lax.broadcasted_iota(jnp.int32, (width, width), 0)
        col = lax.broadcasted_iota(jnp.int32, (width, width), 1)
        gram_theirs = acc_ref[width:, :]
        out_ref[:width, :] = jnp.where(row > col, gram_theirs, 0.0)
        out_ref[width : 2 * width, :] = acc_ref[:width, :]
        diag_theirs = jnp.sum(jnp.where(row == col, gram_theirs, 0.0), axis=0, keepdims=True)
        out_ref[2 * width :, :] = jnp.broadcast_to(diag_theirs, (8, width))


def split_terms(kernel, operands, acc_rows):
    width, cells = operands[0].shape
    tile = min(cells, 4096)
    cell_spec = pl.BlockSpec((width, tile), lambda step: (0, step))
    return pl.pallas_call(
        kernel,
        out_shape=jax.ShapeDtypeStruct((2 * width + 8, width), jnp.float32),
        grid=(cells // tile,),
        in_specs=[cell_spec] * len(operands),
        out_specs=pl.BlockSpec((2 * width + 8, width), lambda step: (0, 0)),
        scratch_shapes=[pltpu.VMEM((acc_rows, width), jnp.float32)],
        cost_estimate=pl.CostEstimate(
            flops=2 * acc_rows * width * cells,
            transcendentals=0,
            bytes_accessed=4 * width * cells * len(operands),
        ),
    )(*operands)


def pair_terms(mine, theirs):
    width, cells = mine.shape
    tile = min(cells, 4096)
    cell_spec = pl.BlockSpec((width, tile), lambda step: (0, step))
    return pl.pallas_call(
        gram_kernel,
        out_shape=jax.ShapeDtypeStruct((2 * width + 8, width), jnp.float32),
        grid=(cells // tile,),
        in_specs=[cell_spec, cell_spec],
        out_specs=pl.BlockSpec((2 * width + 8, width), lambda step: (0, 0)),
        scratch_shapes=[pltpu.VMEM((2 * width, 2 * width), jnp.float32)],
        cost_estimate=pl.CostEstimate(
            flops=8 * width * width * cells, transcendentals=0, bytes_accessed=8 * width * cells
        ),
    )(mine, theirs)


def row_total(part):
    count = lax.axis_size("rows")
    bit = 1
    while bit < count:
        pairs = [(source, source ^ bit) for source in range(count)]
        part = part + lax.ppermute(part, "rows", pairs)
        bit *= 2
    return part


CHUNKS = 4


def lay_kernel(chunk_ids, piece, source_ref, *out_refs):
    if len(chunk_ids) == 1:
        out_refs[0][...] = source_ref[...]
        return
    for chunk, out_ref in zip(chunk_ids, out_refs):
        out_ref[...] = source_ref[:, chunk * piece : (chunk + 1) * piece]


def lay_out(snapshots, rows_n, chunks, chunk_ids):
    local_rows, cells = snapshots.shape
    width = cells // rows_n
    piece = width // chunks
    out_spec = pl.BlockSpec((None, local_rows, piece), lambda dest: (dest, 0, 0))
    return pl.pallas_call(
        functools.partial(lay_kernel, tuple(chunk_ids), piece),
        out_shape=[jax.ShapeDtypeStruct((rows_n, local_rows, piece), snapshots.dtype)] * len(chunk_ids),
        grid=(rows_n,),
        in_specs=[
            pl.BlockSpec((local_rows, piece), lambda dest: (0, dest * chunks + chunk_ids[0]))
            if len(chunk_ids) == 1
            else pl.BlockSpec((local_rows, width), lambda dest: (0, dest))
        ],
        out_specs=[out_spec] * len(chunk_ids),
        cost_estimate=pl.CostEstimate(
            flops=0, transcendentals=0, bytes_accessed=8 * local_rows * piece * rows_n * len(chunk_ids)
        ),
    )(snapshots)


def exchange(bit_pos, snapshots):
    chunks = 1 if bit_pos == 0 else CHUNKS
    rows_n = lax.axis_size("rows")
    local_rows, cells = snapshots.shape
    width = cells // rows_n
    piece = width // chunks

    if chunks == 1:
        mine = lax.all_to_all(snapshots, "rows", split_axis=1, concat_axis=0, tiled=True)
        block_rows = mine.shape[0]
        own_terms = split_terms(mine_kernel, (mine,), block_rows)
        theirs = partner_2(mine, "cols", bit_pos)
        return mine, theirs, own_terms + split_terms(rest_kernel, (mine, theirs), 2 * block_rows)

    sends = lay_out(snapshots, rows_n, chunks, [0]) + lay_out(snapshots, rows_n, chunks, list(range(1, chunks)))

    def laid(chunk):
        return sends[chunk]

    def spread(sent):
        got = lax.all_to_all(sent, "rows", split_axis=0, concat_axis=0)
        return got.reshape(rows_n * local_rows, piece)

    own_parts = [spread(laid(0))]
    other_parts = []
    for chunk in range(1, chunks):
        held = (own_parts[-1], laid(chunk)) + tuple(other_parts[-1:])
        held = lax.optimization_barrier(held)
        own_parts[-1] = held[0]
        if other_parts:
            other_parts[-1] = held[2]
        other_parts.append(partner_2(held[0], "cols", bit_pos))
        own_parts.append(spread(held[1]))
    other_parts.append(partner_2(own_parts[-1], "cols", bit_pos))
    own_full = jnp.zeros((rows_n * local_rows, width), snapshots.dtype)
    other_full = jnp.zeros((rows_n * local_rows, width), snapshots.dtype)
    terms = None
    for chunk, (mine, theirs) in enumerate(zip(own_parts, other_parts)):
        part, own_full, other_full = pair_terms_stored(mine, theirs, own_full, other_full, chunk)
        terms = part if terms is None else terms + part
    return own_full, other_full, terms


def unpack_terms(packed, width):
    row = lax.broadcasted_iota(jnp.int32, (width, width), 0)
    col = lax.broadcasted_iota(jnp.int32, (width, width), 1)
    shared = packed[:width]
    gram_mixed = packed[width : 2 * width]
    diag_theirs = packed[2 * width : 2 * width + 1]
    gram_mine = jnp.where(row <= col, shared, shared.T)
    gram_theirs = jnp.where(row > col, shared, jnp.where(row < col, shared.T, diag_theirs))
    return gram_mine, gram_mixed, gram_theirs


def assemble(terms, own_low):
    gram_mine, gram_mixed, gram_theirs = unpack_terms(row_total(terms), terms.shape[1])
    upper_left = jnp.where(own_low, gram_mine, gram_theirs)
    lower_right = jnp.where(own_low, gram_theirs, gram_mine)
    upper_right = jnp.where(own_low, gram_mixed, gram_mixed.T)
    top_rows = jnp.concatenate([upper_left, upper_right], 1)
    bottom_rows = jnp.concatenate([upper_right.T, lower_right], 1)
    return jnp.concatenate([top_rows, bottom_rows], 0)


def rotate_kernel(coef_ref, mine_ref, theirs_ref, out_ref):
    stacked = jnp.concatenate([mine_ref[...], theirs_ref[...]], 0)
    out_ref[...] = jnp.dot(
        coef_ref[...], stacked, precision=lax.Precision.HIGHEST, preferred_element_type=jnp.float32
    )


def rotate_part(columns_sel, own_low, mine, theirs):
    width, cells = mine.shape
    coef_mine = jnp.where(own_low, columns_sel[:width], columns_sel[width:])
    coef_theirs = jnp.where(own_low, columns_sel[width:], columns_sel[:width])
    coef = jnp.concatenate([coef_mine, coef_theirs], 0).T
    tile = min(cells, 4096)
    coef_spec = pl.BlockSpec((width, 2 * width), lambda step: (0, 0))
    cell_spec = pl.BlockSpec((width, tile), lambda step: (0, step))
    return pl.pallas_call(
        rotate_kernel,
        out_shape=jax.ShapeDtypeStruct((width, cells), jnp.float32),
        grid=(cells // tile,),
        in_specs=[coef_spec, cell_spec, cell_spec],
        out_specs=cell_spec,
        cost_estimate=pl.CostEstimate(
            flops=4 * width * width * cells, transcendentals=0, bytes_accessed=12 * width * cells
        ),
    )(coef, mine, theirs)


def shards(snapshots, pair_table):
    bit_count = lax.axis_size("cols").bit_length() - 1
    column = lax.axis_index("cols")
    mask_val = pair_table[0]
    bit_index = jnp.int32(0)
    for bit_pos in range(bit_count):
        bit_index = bit_index + (mask_val >> bit_pos & 1) * bit_pos
    partner = jnp.bitwise_xor(column, mask_val)
    own_low = column < partner
    branches = [functools.partial(exchange, bit_pos) for bit_pos in range(bit_count)]
    own_parts, other_parts, terms = lax.switch(bit_index, branches, snapshots)
    gram_full = assemble(terms, own_low)
    rotation = jacobi_pallas(gram_full)
    width = own_parts.shape[0]
    own_columns = jnp.where(own_low, rotation[:, :width], rotation[:, width:])
    return rotate_part(own_columns, own_low, own_parts, other_parts)


def solution(mesh):
    in_specs = (P(("cols", "rows"), None), P())
    out_specs = P("cols", "rows")
    return jax.shard_map(shards, mesh=mesh, in_specs=in_specs, out_specs=out_specs, check_vma=False)
```

```python
import functools

import jax
import jax.numpy as jnp
import numpy as np
from jax import lax
from jax.experimental import pallas as pl
from jax.experimental.pallas import tpu as pltpu
from jax.sharding import PartitionSpec as P

ROUNDS = 8


def partner_2(value, axis, bit):
    mask = 2**bit
    pairs = [(source, source ^ mask) for source in range(lax.axis_size(axis))]
    return lax.ppermute(value, axis, pairs)


def packed_gram(low, packed):
    width = packed.shape[1]
    row = lax.broadcasted_iota(jnp.int32, (width, width), 0)
    col = lax.broadcasted_iota(jnp.int32, (width, width), 1)
    shared = packed[:width]
    shared_t = shared.T
    gram_mixed = packed[width : 2 * width]
    diag_theirs = packed[2 * width : 2 * width + 1]
    gram_mine = jnp.where(row <= col, shared, shared_t)
    gram_theirs = jnp.where(row > col, shared, jnp.where(row < col, shared_t, diag_theirs))
    upper_left = jnp.where(low, gram_mine, gram_theirs)
    lower_right = jnp.where(low, gram_theirs, gram_mine)
    upper_right = jnp.where(low, gram_mixed, gram_mixed.T)
    top_rows = jnp.concatenate([upper_left, upper_right], 1)
    bottom_rows = jnp.concatenate([upper_right.T, lower_right], 1)
    return jnp.concatenate([top_rows, bottom_rows], 0)


def jacobi_kernel(low_ref, packed_ref, rotation_ref):
    highest = lax.Precision.HIGHEST
    gram = packed_gram(low_ref[0] != 0, packed_ref[...])
    order_dim = gram.shape[0]
    last_idx = order_dim - 1
    width = order_dim // 2
    row_col = lax.broadcasted_iota(jnp.int32, (order_dim, 1), 0)
    row_full = lax.broadcasted_iota(jnp.int32, (order_dim, order_dim), 0)
    col_full = lax.broadcasted_iota(jnp.int32, (order_dim, order_dim), 1)
    eye = row_full == col_full
    rotation = None
    for round_idx in range(ROUNDS):
        fixed = round_idx % last_idx
        mirror = 2 * fixed - row_col
        mirror = jnp.where(mirror < 0, mirror + last_idx, mirror)
        partner = jnp.where(row_col == fixed, last_idx, jnp.where(row_col == last_idx, fixed, mirror))
        offset = row_col - fixed
        offset = jnp.where(offset < 0, offset + last_idx, offset)
        is_first = (row_col == last_idx) | ((row_col != fixed) & (offset >= 1) & (offset <= width - 1))
        swap = (col_full == partner).astype(jnp.float32)
        on_diag = jnp.where(eye, gram, 0.0)
        diag_own = jnp.sum(on_diag, axis=1, keepdims=True)
        diag_row = jnp.sum(on_diag, axis=0, keepdims=True)
        diag_mate = jnp.sum(swap * diag_row, axis=1, keepdims=True)
        picked = gram * swap
        cross_second = jnp.sum(picked, axis=1, keepdims=True)
        cross_row = jnp.sum(picked, axis=0, keepdims=True)
        cross_first = jnp.sum(jnp.where(eye, cross_row, 0.0), axis=1, keepdims=True)
        cross_val = jnp.where(is_first, cross_first, cross_second)
        spread = jnp.where(is_first, diag_mate - diag_own, diag_own - diag_mate)
        hypot_val = jnp.sqrt(spread * spread + 4.0 * cross_val * cross_val)
        denom = jnp.sqrt(2.0 * hypot_val * (hypot_val + jnp.abs(spread)))
        sign_val = jnp.where(spread >= 0.0, 1.0, -1.0)
        cosine = (hypot_val + jnp.abs(spread)) / denom
        sine_val = 2.0 * cross_val * sign_val / denom
        signed = jnp.where(is_first, sine_val, -sine_val)
        diag_part = jnp.where(eye, cosine, 0.0)
        turn = diag_part + swap * signed
        turn_t = diag_part - swap * signed
        gram = jnp.dot(
            turn_t,
            jnp.dot(gram, turn, precision=highest, preferred_element_type=jnp.float32),
            precision=highest,
            preferred_element_type=jnp.float32,
        )
        rotation = turn if rotation is None else jnp.dot(
            rotation, turn, precision=highest, preferred_element_type=jnp.float32
        )
    rotation_ref[...] = rotation

def jacobi_pallas(low, packed):
    order_dim = 2 * packed.shape[1]
    return pl.pallas_call(
        jacobi_kernel,
        out_shape=jax.ShapeDtypeStruct((order_dim, order_dim), jnp.float32),
        in_specs=[pl.BlockSpec(memory_space=pltpu.SMEM), pl.BlockSpec(memory_space=pltpu.VMEM)],
        out_specs=pl.BlockSpec(memory_space=pltpu.VMEM),
    )(low, packed)


def gram_kernel(mine_ref, theirs_ref, out_ref, acc_ref):
    step = pl.program_id(0)

    @pl.when(step == 0)
    def _():
        acc_ref[...] = jnp.zeros_like(acc_ref)

    stacked = jnp.concatenate([mine_ref[...], theirs_ref[...]], 0)
    acc_ref[...] += lax.dot_general(
        stacked,
        stacked,
        (((1,), (1,)), ((), ())),
        precision=lax.Precision.HIGHEST,
        preferred_element_type=jnp.float32,
    )

    @pl.when(step == pl.num_programs(0) - 1)
    def _():
        width = mine_ref.shape[0]
        row = lax.broadcasted_iota(jnp.int32, (width, width), 0)
        col = lax.broadcasted_iota(jnp.int32, (width, width), 1)
        gram_theirs = acc_ref[width:, width:]
        out_ref[:width, :] = jnp.where(row <= col, acc_ref[:width, :width], gram_theirs)
        out_ref[width : 2 * width, :] = acc_ref[:width, width:]
        diag_theirs = jnp.sum(jnp.where(row == col, gram_theirs, 0.0), axis=0, keepdims=True)
        out_ref[2 * width :, :] = jnp.broadcast_to(diag_theirs, (8, width))


def gram_store_kernel(mine_ref, theirs_ref, own_in, other_in, out_ref, own_ref, other_ref, acc_ref):
    del own_in, other_in
    gram_kernel(mine_ref, theirs_ref, out_ref, acc_ref)
    own_ref[...] = mine_ref[...]
    other_ref[...] = theirs_ref[...]


def pair_terms_stored(mine, theirs, own_full, other_full, chunk):
    width, piece = mine.shape
    cell_spec = pl.BlockSpec((width, piece), lambda step: (0, 0))
    full_spec = pl.BlockSpec((width, piece), lambda step: (0, chunk))
    return pl.pallas_call(
        gram_store_kernel,
        out_shape=[
            jax.ShapeDtypeStruct((2 * width + 8, width), jnp.float32),
            jax.ShapeDtypeStruct(own_full.shape, own_full.dtype),
            jax.ShapeDtypeStruct(other_full.shape, other_full.dtype),
        ],
        grid=(1,),
        in_specs=[cell_spec, cell_spec, pl.BlockSpec(memory_space=pl.ANY), pl.BlockSpec(memory_space=pl.ANY)],
        out_specs=[pl.BlockSpec((2 * width + 8, width), lambda step: (0, 0)), full_spec, full_spec],
        scratch_shapes=[pltpu.VMEM((2 * width, 2 * width), jnp.float32)],
        input_output_aliases={2: 1, 3: 2},
        cost_estimate=pl.CostEstimate(
            flops=8 * width * width * piece, transcendentals=0, bytes_accessed=16 * width * piece
        ),
    )(mine, theirs, own_full, other_full)


def mine_kernel(mine_ref, out_ref, acc_ref):
    step = pl.program_id(0)

    @pl.when(step == 0)
    def _():
        acc_ref[...] = jnp.zeros_like(acc_ref)

    acc_ref[...] += lax.dot_general(
        mine_ref[...],
        mine_ref[...],
        (((1,), (1,)), ((), ())),
        precision=lax.Precision.HIGHEST,
        preferred_element_type=jnp.float32,
    )

    @pl.when(step == pl.num_programs(0) - 1)
    def _():
        width = mine_ref.shape[0]
        row = lax.broadcasted_iota(jnp.int32, (width, width), 0)
        col = lax.broadcasted_iota(jnp.int32, (width, width), 1)
        out_ref[:width, :] = jnp.where(row <= col, acc_ref[...], 0.0)
        out_ref[width:, :] = jnp.zeros((width + 8, width), jnp.float32)


def rest_kernel(mine_ref, theirs_ref, out_ref, acc_ref):
    step = pl.program_id(0)

    @pl.when(step == 0)
    def _():
        acc_ref[...] = jnp.zeros_like(acc_ref)

    stacked = jnp.concatenate([mine_ref[...], theirs_ref[...]], 0)
    acc_ref[...] += lax.dot_general(
        stacked,
        theirs_ref[...],
        (((1,), (1,)), ((), ())),
        precision=lax.Precision.HIGHEST,
        preferred_element_type=jnp.float32,
    )

    @pl.when(step == pl.num_programs(0) - 1)
    def _():
        width = mine_ref.shape[0]
        row = lax.broadcasted_iota(jnp.int32, (width, width), 0)
        col = lax.broadcasted_iota(jnp.int32, (width, width), 1)
        gram_theirs = acc_ref[width:, :]
        out_ref[:width, :] = jnp.where(row > col, gram_theirs, 0.0)
        out_ref[width : 2 * width, :] = acc_ref[:width, :]
        diag_theirs = jnp.sum(jnp.where(row == col, gram_theirs, 0.0), axis=0, keepdims=True)
        out_ref[2 * width :, :] = jnp.broadcast_to(diag_theirs, (8, width))


def split_terms(kernel, operands, acc_rows):
    width, cells = operands[0].shape
    tile = min(cells, 2048)
    cell_spec = pl.BlockSpec((width, tile), lambda step: (0, step))
    return pl.pallas_call(
        kernel,
        out_shape=jax.ShapeDtypeStruct((2 * width + 8, width), jnp.float32),
        grid=(cells // tile,),
        in_specs=[cell_spec] * len(operands),
        out_specs=pl.BlockSpec((2 * width + 8, width), lambda step: (0, 0)),
        scratch_shapes=[pltpu.VMEM((acc_rows, width), jnp.float32)],
        cost_estimate=pl.CostEstimate(
            flops=2 * acc_rows * width * cells,
            transcendentals=0,
            bytes_accessed=4 * width * cells * len(operands),
        ),
    )(*operands)


def pair_terms(mine, theirs):
    width, cells = mine.shape
    tile = min(cells, 2048)
    cell_spec = pl.BlockSpec((width, tile), lambda step: (0, step))
    return pl.pallas_call(
        gram_kernel,
        out_shape=jax.ShapeDtypeStruct((2 * width + 8, width), jnp.float32),
        grid=(cells // tile,),
        in_specs=[cell_spec, cell_spec],
        out_specs=pl.BlockSpec((2 * width + 8, width), lambda step: (0, 0)),
        scratch_shapes=[pltpu.VMEM((2 * width, 2 * width), jnp.float32)],
        cost_estimate=pl.CostEstimate(
            flops=8 * width * width * cells, transcendentals=0, bytes_accessed=8 * width * cells
        ),
    )(mine, theirs)


def row_total(part):
    count = lax.axis_size("rows")
    bit = 1
    while bit < count:
        pairs = [(source, source ^ bit) for source in range(count)]
        part = part + lax.ppermute(part, "rows", pairs)
        bit *= 2
    return part


CHUNKS = 4


def lay_kernel(chunk_ids, piece, source_ref, *out_refs):
    if len(chunk_ids) == 1:
        out_refs[0][...] = source_ref[...]
        return
    for chunk, out_ref in zip(chunk_ids, out_refs):
        out_ref[...] = source_ref[:, chunk * piece : (chunk + 1) * piece]


def lay_out(snapshots, rows_n, chunks, chunk_ids):
    local_rows, cells = snapshots.shape
    width = cells // rows_n
    piece = width // chunks
    out_spec = pl.BlockSpec((None, local_rows, piece), lambda dest: (dest, 0, 0))
    return pl.pallas_call(
        functools.partial(lay_kernel, tuple(chunk_ids), piece),
        out_shape=[jax.ShapeDtypeStruct((rows_n, local_rows, piece), snapshots.dtype)] * len(chunk_ids),
        grid=(rows_n,),
        in_specs=[
            pl.BlockSpec((local_rows, piece), lambda dest: (0, dest * chunks + chunk_ids[0]))
            if len(chunk_ids) == 1
            else pl.BlockSpec((local_rows, width), lambda dest: (0, dest))
        ],
        out_specs=[out_spec] * len(chunk_ids),
        cost_estimate=pl.CostEstimate(
            flops=0, transcendentals=0, bytes_accessed=8 * local_rows * piece * rows_n * len(chunk_ids)
        ),
    )(snapshots)


def exchange(bit_pos, snapshots):
    chunks = 1 if bit_pos == 0 else CHUNKS
    rows_n = lax.axis_size("rows")
    local_rows, cells = snapshots.shape
    width = cells // rows_n
    piece = width // chunks

    if chunks == 1:
        mine = lax.all_to_all(snapshots, "rows", split_axis=1, concat_axis=0, tiled=True)
        block_rows = mine.shape[0]
        own_terms = split_terms(mine_kernel, (mine,), block_rows)
        theirs = partner_2(mine, "cols", bit_pos)
        return mine, theirs, own_terms + split_terms(rest_kernel, (mine, theirs), 2 * block_rows)

    sends = lay_out(snapshots, rows_n, chunks, [0]) + lay_out(snapshots, rows_n, chunks, list(range(1, chunks)))

    def laid(chunk):
        return sends[chunk]

    def spread(sent):
        got = lax.all_to_all(sent, "rows", split_axis=0, concat_axis=0)
        return got.reshape(rows_n * local_rows, piece)

    own_parts = [spread(laid(0))]
    other_parts = []
    for chunk in range(1, chunks):
        held = (own_parts[-1], laid(chunk)) + tuple(other_parts[-1:])
        held = lax.optimization_barrier(held)
        own_parts[-1] = held[0]
        if other_parts:
            other_parts[-1] = held[2]
        other_parts.append(partner_2(held[0], "cols", bit_pos))
        own_parts.append(spread(held[1]))
    other_parts.append(partner_2(own_parts[-1], "cols", bit_pos))
    own_full = jnp.zeros((rows_n * local_rows, width), snapshots.dtype)
    other_full = jnp.zeros((rows_n * local_rows, width), snapshots.dtype)
    terms = None
    for chunk, (mine, theirs) in enumerate(zip(own_parts, other_parts)):
        part, own_full, other_full = pair_terms_stored(mine, theirs, own_full, other_full, chunk)
        terms = part if terms is None else terms + part
    return own_full, other_full, terms


def unpack_terms(packed, width):
    row = lax.broadcasted_iota(jnp.int32, (width, width), 0)
    col = lax.broadcasted_iota(jnp.int32, (width, width), 1)
    shared = packed[:width]
    gram_mixed = packed[width : 2 * width]
    diag_theirs = packed[2 * width : 2 * width + 1]
    gram_mine = jnp.where(row <= col, shared, shared.T)
    gram_theirs = jnp.where(row > col, shared, jnp.where(row < col, shared.T, diag_theirs))
    return gram_mine, gram_mixed, gram_theirs


def assemble(terms, own_low):
    gram_mine, gram_mixed, gram_theirs = unpack_terms(row_total(terms), terms.shape[1])
    upper_left = jnp.where(own_low, gram_mine, gram_theirs)
    lower_right = jnp.where(own_low, gram_theirs, gram_mine)
    upper_right = jnp.where(own_low, gram_mixed, gram_mixed.T)
    top_rows = jnp.concatenate([upper_left, upper_right], 1)
    bottom_rows = jnp.concatenate([upper_right.T, lower_right], 1)
    return jnp.concatenate([top_rows, bottom_rows], 0)


def rotate_kernel(coef_ref, mine_ref, theirs_ref, out_ref):
    stacked = jnp.concatenate([mine_ref[...], theirs_ref[...]], 0)
    out_ref[...] = jnp.dot(
        coef_ref[...], stacked, precision=lax.Precision.HIGHEST, preferred_element_type=jnp.float32
    )


def rotate_part(columns_sel, own_low, mine, theirs):
    width, cells = mine.shape
    coef_mine = jnp.where(own_low, columns_sel[:width], columns_sel[width:])
    coef_theirs = jnp.where(own_low, columns_sel[width:], columns_sel[:width])
    coef = jnp.concatenate([coef_mine, coef_theirs], 0).T
    tile = min(cells, 2048)
    coef_spec = pl.BlockSpec((width, 2 * width), lambda step: (0, 0))
    cell_spec = pl.BlockSpec((width, tile), lambda step: (0, step))
    return pl.pallas_call(
        rotate_kernel,
        out_shape=jax.ShapeDtypeStruct((width, cells), jnp.float32),
        grid=(cells // tile,),
        in_specs=[coef_spec, cell_spec, cell_spec],
        out_specs=cell_spec,
        cost_estimate=pl.CostEstimate(
            flops=4 * width * width * cells, transcendentals=0, bytes_accessed=12 * width * cells
        ),
    )(coef, mine, theirs)


def shards(snapshots, pair_table):
    bit_count = lax.axis_size("cols").bit_length() - 1
    column = lax.axis_index("cols")
    mask_val = pair_table[0]
    bit_index = jnp.int32(0)
    for bit_pos in range(bit_count):
        bit_index = bit_index + (mask_val >> bit_pos & 1) * bit_pos
    partner = jnp.bitwise_xor(column, mask_val)
    own_low = column < partner
    branches = [functools.partial(exchange, bit_pos) for bit_pos in range(bit_count)]
    own_parts, other_parts, terms = lax.switch(bit_index, branches, snapshots)
    rotation = jacobi_pallas(own_low.astype(jnp.int32).reshape(1), row_total(terms))
    width = own_parts.shape[0]
    own_columns = jnp.where(own_low, rotation[:, :width], rotation[:, width:])
    return rotate_part(own_columns, own_low, own_parts, other_parts)


def solution(mesh):
    in_specs = (P(("cols", "rows"), None), P())
    out_specs = P("cols", "rows")
    return jax.shard_map(shards, mesh=mesh, in_specs=in_specs, out_specs=out_specs, check_vma=False)
```

```python
import functools

import jax
import jax.numpy as jnp
import numpy as np
from jax import lax
from jax.experimental import pallas as pl
from jax.experimental.pallas import tpu as pltpu
from jax.sharding import PartitionSpec as P

ROUNDS = 8


def partner_2(value, axis, bit):
    mask = 2**bit
    pairs = [(source, source ^ mask) for source in range(lax.axis_size(axis))]
    return lax.ppermute(value, axis, pairs)


def packed_gram(low, packed):
    width = packed.shape[1]
    row = lax.broadcasted_iota(jnp.int32, (width, width), 0)
    col = lax.broadcasted_iota(jnp.int32, (width, width), 1)
    shared = packed[:width]
    shared_t = shared.T
    gram_mixed = packed[width : 2 * width]
    diag_theirs = packed[2 * width : 2 * width + 1]
    gram_mine = jnp.where(row <= col, shared, shared_t)
    gram_theirs = jnp.where(row > col, shared, jnp.where(row < col, shared_t, diag_theirs))
    upper_left = jnp.where(low, gram_mine, gram_theirs)
    lower_right = jnp.where(low, gram_theirs, gram_mine)
    upper_right = jnp.where(low, gram_mixed, gram_mixed.T)
    top_rows = jnp.concatenate([upper_left, upper_right], 1)
    bottom_rows = jnp.concatenate([upper_right.T, lower_right], 1)
    return jnp.concatenate([top_rows, bottom_rows], 0)


def jacobi_kernel(low_ref, packed_ref, rotation_ref):
    highest = lax.Precision.HIGHEST
    gram = packed_gram(low_ref[0] != 0, packed_ref[...])
    order_dim = gram.shape[0]
    last_idx = order_dim - 1
    width = order_dim // 2
    row_col = lax.broadcasted_iota(jnp.int32, (order_dim, 1), 0)
    row_full = lax.broadcasted_iota(jnp.int32, (order_dim, order_dim), 0)
    col_full = lax.broadcasted_iota(jnp.int32, (order_dim, order_dim), 1)
    eye = row_full == col_full
    rotation = None
    for round_idx in range(ROUNDS):
        fixed = round_idx % last_idx
        mirror = 2 * fixed - row_col
        mirror = jnp.where(mirror < 0, mirror + last_idx, mirror)
        partner = jnp.where(row_col == fixed, last_idx, jnp.where(row_col == last_idx, fixed, mirror))
        offset = row_col - fixed
        offset = jnp.where(offset < 0, offset + last_idx, offset)
        is_first = (row_col == last_idx) | ((row_col != fixed) & (offset >= 1) & (offset <= width - 1))
        swap = (col_full == partner).astype(jnp.float32)
        on_diag = jnp.where(eye, gram, 0.0)
        diag_own = jnp.sum(on_diag, axis=1, keepdims=True)
        diag_row = jnp.sum(on_diag, axis=0, keepdims=True)
        diag_mate = jnp.sum(swap * diag_row, axis=1, keepdims=True)
        picked = gram * swap
        cross_second = jnp.sum(picked, axis=1, keepdims=True)
        cross_row = jnp.sum(picked, axis=0, keepdims=True)
        cross_first = jnp.sum(jnp.where(eye, cross_row, 0.0), axis=1, keepdims=True)
        cross_val = jnp.where(is_first, cross_first, cross_second)
        spread = jnp.where(is_first, diag_mate - diag_own, diag_own - diag_mate)
        hypot_val = jnp.sqrt(spread * spread + 4.0 * cross_val * cross_val)
        denom = jnp.sqrt(2.0 * hypot_val * (hypot_val + jnp.abs(spread)))
        sign_val = jnp.where(spread >= 0.0, 1.0, -1.0)
        cosine = (hypot_val + jnp.abs(spread)) / denom
        sine_val = 2.0 * cross_val * sign_val / denom
        signed = jnp.where(is_first, sine_val, -sine_val)
        diag_part = jnp.where(eye, cosine, 0.0)
        turn = diag_part + swap * signed
        turn_t = diag_part - swap * signed
        gram = jnp.dot(
            turn_t,
            jnp.dot(gram, turn, precision=highest, preferred_element_type=jnp.float32),
            precision=highest,
            preferred_element_type=jnp.float32,
        )
        rotation = turn if rotation is None else jnp.dot(
            rotation, turn, precision=highest, preferred_element_type=jnp.float32
        )
    rotation_ref[...] = rotation

def jacobi_pallas(low, packed):
    order_dim = 2 * packed.shape[1]
    return pl.pallas_call(
        jacobi_kernel,
        out_shape=jax.ShapeDtypeStruct((order_dim, order_dim), jnp.float32),
        in_specs=[pl.BlockSpec(memory_space=pltpu.SMEM), pl.BlockSpec(memory_space=pltpu.VMEM)],
        out_specs=pl.BlockSpec(memory_space=pltpu.VMEM),
    )(low, packed)


def gram_kernel(mine_ref, theirs_ref, out_ref, acc_ref):
    step = pl.program_id(0)

    @pl.when(step == 0)
    def _():
        acc_ref[...] = jnp.zeros_like(acc_ref)

    stacked = jnp.concatenate([mine_ref[...], theirs_ref[...]], 0)
    acc_ref[...] += lax.dot_general(
        stacked,
        stacked,
        (((1,), (1,)), ((), ())),
        precision=lax.Precision.HIGHEST,
        preferred_element_type=jnp.float32,
    )

    @pl.when(step == pl.num_programs(0) - 1)
    def _():
        width = mine_ref.shape[0]
        row = lax.broadcasted_iota(jnp.int32, (width, width), 0)
        col = lax.broadcasted_iota(jnp.int32, (width, width), 1)
        gram_theirs = acc_ref[width:, width:]
        out_ref[:width, :] = jnp.where(row <= col, acc_ref[:width, :width], gram_theirs)
        out_ref[width : 2 * width, :] = acc_ref[:width, width:]
        diag_theirs = jnp.sum(jnp.where(row == col, gram_theirs, 0.0), axis=0, keepdims=True)
        out_ref[2 * width :, :] = jnp.broadcast_to(diag_theirs, (8, width))


def gram_store_kernel(mine_ref, theirs_ref, own_in, other_in, out_ref, own_ref, other_ref, acc_ref):
    del own_in, other_in
    gram_kernel(mine_ref, theirs_ref, out_ref, acc_ref)
    own_ref[...] = mine_ref[...]
    other_ref[...] = theirs_ref[...]


def pair_terms_stored(mine, theirs, own_full, other_full, chunk):
    width, piece = mine.shape
    cell_spec = pl.BlockSpec((width, piece), lambda step: (0, 0))
    full_spec = pl.BlockSpec((width, piece), lambda step: (0, chunk))
    return pl.pallas_call(
        gram_store_kernel,
        out_shape=[
            jax.ShapeDtypeStruct((2 * width + 8, width), jnp.float32),
            jax.ShapeDtypeStruct(own_full.shape, own_full.dtype),
            jax.ShapeDtypeStruct(other_full.shape, other_full.dtype),
        ],
        grid=(1,),
        in_specs=[cell_spec, cell_spec, pl.BlockSpec(memory_space=pl.ANY), pl.BlockSpec(memory_space=pl.ANY)],
        out_specs=[pl.BlockSpec((2 * width + 8, width), lambda step: (0, 0)), full_spec, full_spec],
        scratch_shapes=[pltpu.VMEM((2 * width, 2 * width), jnp.float32)],
        input_output_aliases={2: 1, 3: 2},
        cost_estimate=pl.CostEstimate(
            flops=8 * width * width * piece, transcendentals=0, bytes_accessed=16 * width * piece
        ),
    )(mine, theirs, own_full, other_full)


def mine_kernel(mine_ref, out_ref, acc_ref):
    step = pl.program_id(0)

    @pl.when(step == 0)
    def _():
        acc_ref[...] = jnp.zeros_like(acc_ref)

    acc_ref[...] += lax.dot_general(
        mine_ref[...],
        mine_ref[...],
        (((1,), (1,)), ((), ())),
        precision=lax.Precision.HIGHEST,
        preferred_element_type=jnp.float32,
    )

    @pl.when(step == pl.num_programs(0) - 1)
    def _():
        width = mine_ref.shape[0]
        row = lax.broadcasted_iota(jnp.int32, (width, width), 0)
        col = lax.broadcasted_iota(jnp.int32, (width, width), 1)
        out_ref[:width, :] = jnp.where(row <= col, acc_ref[...], 0.0)
        out_ref[width:, :] = jnp.zeros((width + 8, width), jnp.float32)


def rest_kernel(mine_ref, theirs_ref, out_ref, acc_ref):
    step = pl.program_id(0)

    @pl.when(step == 0)
    def _():
        acc_ref[...] = jnp.zeros_like(acc_ref)

    stacked = jnp.concatenate([mine_ref[...], theirs_ref[...]], 0)
    acc_ref[...] += lax.dot_general(
        stacked,
        theirs_ref[...],
        (((1,), (1,)), ((), ())),
        precision=lax.Precision.HIGHEST,
        preferred_element_type=jnp.float32,
    )

    @pl.when(step == pl.num_programs(0) - 1)
    def _():
        width = mine_ref.shape[0]
        row = lax.broadcasted_iota(jnp.int32, (width, width), 0)
        col = lax.broadcasted_iota(jnp.int32, (width, width), 1)
        gram_theirs = acc_ref[width:, :]
        out_ref[:width, :] = jnp.where(row > col, gram_theirs, 0.0)
        out_ref[width : 2 * width, :] = acc_ref[:width, :]
        diag_theirs = jnp.sum(jnp.where(row == col, gram_theirs, 0.0), axis=0, keepdims=True)
        out_ref[2 * width :, :] = jnp.broadcast_to(diag_theirs, (8, width))


def split_terms(kernel, operands, acc_rows):
    width, cells = operands[0].shape
    tile = min(cells, 2048)
    cell_spec = pl.BlockSpec((width, tile), lambda step: (0, step))
    return pl.pallas_call(
        kernel,
        out_shape=jax.ShapeDtypeStruct((2 * width + 8, width), jnp.float32),
        grid=(cells // tile,),
        in_specs=[cell_spec] * len(operands),
        out_specs=pl.BlockSpec((2 * width + 8, width), lambda step: (0, 0)),
        scratch_shapes=[pltpu.VMEM((acc_rows, width), jnp.float32)],
        cost_estimate=pl.CostEstimate(
            flops=2 * acc_rows * width * cells,
            transcendentals=0,
            bytes_accessed=4 * width * cells * len(operands),
        ),
    )(*operands)


def pair_terms(mine, theirs):
    width, cells = mine.shape
    tile = min(cells, 2048)
    cell_spec = pl.BlockSpec((width, tile), lambda step: (0, step))
    return pl.pallas_call(
        gram_kernel,
        out_shape=jax.ShapeDtypeStruct((2 * width + 8, width), jnp.float32),
        grid=(cells // tile,),
        in_specs=[cell_spec, cell_spec],
        out_specs=pl.BlockSpec((2 * width + 8, width), lambda step: (0, 0)),
        scratch_shapes=[pltpu.VMEM((2 * width, 2 * width), jnp.float32)],
        cost_estimate=pl.CostEstimate(
            flops=8 * width * width * cells, transcendentals=0, bytes_accessed=8 * width * cells
        ),
    )(mine, theirs)


def row_total(part):
    count = lax.axis_size("rows")
    bit = 1
    while bit < count:
        pairs = [(source, source ^ bit) for source in range(count)]
        part = part + lax.ppermute(part, "rows", pairs)
        bit *= 2
    return part


CHUNKS = 4


def lay_kernel(chunk_ids, piece, source_ref, *out_refs):
    if len(chunk_ids) == 1:
        out_refs[0][...] = source_ref[...]
        return
    for chunk, out_ref in zip(chunk_ids, out_refs):
        out_ref[...] = source_ref[:, chunk * piece : (chunk + 1) * piece]


def lay_out(snapshots, rows_n, chunks, chunk_ids):
    local_rows, cells = snapshots.shape
    width = cells // rows_n
    piece = width // chunks
    out_spec = pl.BlockSpec((None, local_rows, piece), lambda dest: (dest, 0, 0))
    return pl.pallas_call(
        functools.partial(lay_kernel, tuple(chunk_ids), piece),
        out_shape=[jax.ShapeDtypeStruct((rows_n, local_rows, piece), snapshots.dtype)] * len(chunk_ids),
        grid=(rows_n,),
        in_specs=[
            pl.BlockSpec((local_rows, piece), lambda dest: (0, dest * chunks + chunk_ids[0]))
            if len(chunk_ids) == 1
            else pl.BlockSpec((local_rows, width), lambda dest: (0, dest))
        ],
        out_specs=[out_spec] * len(chunk_ids),
        cost_estimate=pl.CostEstimate(
            flops=0, transcendentals=0, bytes_accessed=8 * local_rows * piece * rows_n * len(chunk_ids)
        ),
    )(snapshots)


def exchange(bit_pos, snapshots):
    chunks = 1 if bit_pos == 0 else CHUNKS
    rows_n = lax.axis_size("rows")
    local_rows, cells = snapshots.shape
    width = cells // rows_n
    piece = width // chunks

    if chunks == 1:
        mine = lax.all_to_all(snapshots, "rows", split_axis=1, concat_axis=0, tiled=True)
        block_rows = mine.shape[0]
        own_terms = split_terms(mine_kernel, (mine,), block_rows)
        theirs = partner_2(mine, "cols", bit_pos)
        return mine, theirs, own_terms + split_terms(rest_kernel, (mine, theirs), 2 * block_rows)

    sends = lay_out(snapshots, rows_n, chunks, [0]) + lay_out(snapshots, rows_n, chunks, list(range(1, chunks)))

    def laid(chunk):
        return sends[chunk]

    def spread(sent):
        got = lax.all_to_all(sent, "rows", split_axis=0, concat_axis=0)
        return got.reshape(rows_n * local_rows, piece)

    own_parts = [spread(laid(0))]
    other_parts = []
    for chunk in range(1, chunks):
        held = (own_parts[-1], laid(chunk)) + tuple(other_parts[-1:])
        held = lax.optimization_barrier(held)
        own_parts[-1] = held[0]
        if other_parts:
            other_parts[-1] = held[2]
        other_parts.append(partner_2(held[0], "cols", bit_pos))
        own_parts.append(spread(held[1]))
    other_parts.append(partner_2(own_parts[-1], "cols", bit_pos))
    own_full = jnp.zeros((rows_n * local_rows, width), snapshots.dtype)
    other_full = jnp.zeros((rows_n * local_rows, width), snapshots.dtype)
    terms = None
    for chunk, (mine, theirs) in enumerate(zip(own_parts, other_parts)):
        part, own_full, other_full = pair_terms_stored(mine, theirs, own_full, other_full, chunk)
        terms = part if terms is None else terms + part
    return own_full, other_full, terms


def unpack_terms(packed, width):
    row = lax.broadcasted_iota(jnp.int32, (width, width), 0)
    col = lax.broadcasted_iota(jnp.int32, (width, width), 1)
    shared = packed[:width]
    gram_mixed = packed[width : 2 * width]
    diag_theirs = packed[2 * width : 2 * width + 1]
    gram_mine = jnp.where(row <= col, shared, shared.T)
    gram_theirs = jnp.where(row > col, shared, jnp.where(row < col, shared.T, diag_theirs))
    return gram_mine, gram_mixed, gram_theirs


def assemble(terms, own_low):
    gram_mine, gram_mixed, gram_theirs = unpack_terms(row_total(terms), terms.shape[1])
    upper_left = jnp.where(own_low, gram_mine, gram_theirs)
    lower_right = jnp.where(own_low, gram_theirs, gram_mine)
    upper_right = jnp.where(own_low, gram_mixed, gram_mixed.T)
    top_rows = jnp.concatenate([upper_left, upper_right], 1)
    bottom_rows = jnp.concatenate([upper_right.T, lower_right], 1)
    return jnp.concatenate([top_rows, bottom_rows], 0)


def rotate_kernel(low_ref, rotation_ref, mine_ref, theirs_ref, out_ref):
    low = low_ref[0] != 0
    rotation = rotation_ref[...]
    width = mine_ref.shape[0]
    own_columns = jnp.where(low, rotation[:, :width], rotation[:, width:])
    coef_mine = jnp.where(low, own_columns[:width], own_columns[width:])
    coef_theirs = jnp.where(low, own_columns[width:], own_columns[:width])
    coef = jnp.concatenate([coef_mine, coef_theirs], 0).T
    stacked = jnp.concatenate([mine_ref[...], theirs_ref[...]], 0)
    out_ref[...] = jnp.dot(
        coef, stacked, precision=lax.Precision.HIGHEST, preferred_element_type=jnp.float32
    )


def rotate_part(rotation, low, mine, theirs):
    width, cells = mine.shape
    tile = min(cells, 2048)
    cell_spec = pl.BlockSpec((width, tile), lambda step: (0, step))
    return pl.pallas_call(
        rotate_kernel,
        out_shape=jax.ShapeDtypeStruct((width, cells), jnp.float32),
        grid=(cells // tile,),
        in_specs=[
            pl.BlockSpec(memory_space=pltpu.SMEM),
            pl.BlockSpec(rotation.shape, lambda step: (0, 0)),
            cell_spec,
            cell_spec,
        ],
        out_specs=cell_spec,
        cost_estimate=pl.CostEstimate(
            flops=4 * width * width * cells, transcendentals=0, bytes_accessed=12 * width * cells
        ),
    )(low, rotation, mine, theirs)


def shards(snapshots, pair_table):
    bit_count = lax.axis_size("cols").bit_length() - 1
    column = lax.axis_index("cols")
    mask_val = pair_table[0]
    bit_index = jnp.int32(0)
    for bit_pos in range(bit_count):
        bit_index = bit_index + (mask_val >> bit_pos & 1) * bit_pos
    partner = jnp.bitwise_xor(column, mask_val)
    own_low = column < partner
    branches = [functools.partial(exchange, bit_pos) for bit_pos in range(bit_count)]
    own_parts, other_parts, terms = lax.switch(bit_index, branches, snapshots)
    low = own_low.astype(jnp.int32).reshape(1)
    rotation = jacobi_pallas(low, row_total(terms))
    return rotate_part(rotation, low, own_parts, other_parts)


def solution(mesh):
    in_specs = (P(("cols", "rows"), None), P())
    out_specs = P("cols", "rows")
    return jax.shard_map(shards, mesh=mesh, in_specs=in_specs, out_specs=out_specs, check_vma=False)
```

```python
import functools

import jax
import jax.numpy as jnp
import numpy as np
from jax import lax
from jax.experimental import pallas as pl
from jax.experimental.pallas import tpu as pltpu
from jax.sharding import PartitionSpec as P

ROUNDS = 8


def partner_2(value, axis, bit):
    mask = 2**bit
    pairs = [(source, source ^ mask) for source in range(lax.axis_size(axis))]
    return lax.ppermute(value, axis, pairs)


def packed_gram(low, packed):
    width = packed.shape[1]
    row = lax.broadcasted_iota(jnp.int32, (width, width), 0)
    col = lax.broadcasted_iota(jnp.int32, (width, width), 1)
    shared = packed[:width]
    shared_t = shared.T
    gram_mixed = packed[width : 2 * width]
    diag_theirs = packed[2 * width : 2 * width + 1]
    gram_mine = jnp.where(row <= col, shared, shared_t)
    gram_theirs = jnp.where(row > col, shared, jnp.where(row < col, shared_t, diag_theirs))
    upper_left = jnp.where(low, gram_mine, gram_theirs)
    lower_right = jnp.where(low, gram_theirs, gram_mine)
    upper_right = jnp.where(low, gram_mixed, gram_mixed.T)
    top_rows = jnp.concatenate([upper_left, upper_right], 1)
    bottom_rows = jnp.concatenate([upper_right.T, lower_right], 1)
    return jnp.concatenate([top_rows, bottom_rows], 0)


def jacobi_kernel(low_ref, packed_ref, rotation_ref):
    highest = lax.Precision.HIGHEST
    gram = packed_gram(low_ref[0] != 0, packed_ref[...])
    order_dim = gram.shape[0]
    last_idx = order_dim - 1
    width = order_dim // 2
    row_col = lax.broadcasted_iota(jnp.int32, (order_dim, 1), 0)
    row_full = lax.broadcasted_iota(jnp.int32, (order_dim, order_dim), 0)
    col_full = lax.broadcasted_iota(jnp.int32, (order_dim, order_dim), 1)
    eye = row_full == col_full
    rotation = None
    for round_idx in range(ROUNDS):
        fixed = round_idx % last_idx
        mirror = 2 * fixed - row_col
        mirror = jnp.where(mirror < 0, mirror + last_idx, mirror)
        partner = jnp.where(row_col == fixed, last_idx, jnp.where(row_col == last_idx, fixed, mirror))
        offset = row_col - fixed
        offset = jnp.where(offset < 0, offset + last_idx, offset)
        is_first = (row_col == last_idx) | ((row_col != fixed) & (offset >= 1) & (offset <= width - 1))
        swap = (col_full == partner).astype(jnp.float32)
        on_diag = jnp.where(eye, gram, 0.0)
        diag_own = jnp.sum(on_diag, axis=1, keepdims=True)
        diag_row = jnp.sum(on_diag, axis=0, keepdims=True)
        diag_mate = jnp.sum(swap * diag_row, axis=1, keepdims=True)
        picked = gram * swap
        cross_second = jnp.sum(picked, axis=1, keepdims=True)
        cross_row = jnp.sum(picked, axis=0, keepdims=True)
        cross_first = jnp.sum(jnp.where(eye, cross_row, 0.0), axis=1, keepdims=True)
        cross_val = jnp.where(is_first, cross_first, cross_second)
        spread = jnp.where(is_first, diag_mate - diag_own, diag_own - diag_mate)
        hypot_val = jnp.sqrt(spread * spread + 4.0 * cross_val * cross_val)
        denom = jnp.sqrt(2.0 * hypot_val * (hypot_val + jnp.abs(spread)))
        sign_val = jnp.where(spread >= 0.0, 1.0, -1.0)
        cosine = (hypot_val + jnp.abs(spread)) / denom
        sine_val = 2.0 * cross_val * sign_val / denom
        signed = jnp.where(is_first, sine_val, -sine_val)
        diag_part = jnp.where(eye, cosine, 0.0)
        turn = diag_part + swap * signed
        turn_t = diag_part - swap * signed
        gram = jnp.dot(
            turn_t,
            jnp.dot(gram, turn, precision=highest, preferred_element_type=jnp.float32),
            precision=highest,
            preferred_element_type=jnp.float32,
        )
        rotation = turn if rotation is None else jnp.dot(
            rotation, turn, precision=highest, preferred_element_type=jnp.float32
        )
    rotation_ref[...] = rotation

def jacobi_pallas(low, packed):
    order_dim = 2 * packed.shape[1]
    return pl.pallas_call(
        jacobi_kernel,
        out_shape=jax.ShapeDtypeStruct((order_dim, order_dim), jnp.float32),
        in_specs=[pl.BlockSpec(memory_space=pltpu.SMEM), pl.BlockSpec(memory_space=pltpu.VMEM)],
        out_specs=pl.BlockSpec(memory_space=pltpu.VMEM),
    )(low, packed)


def gram_kernel(mine_ref, theirs_ref, out_ref, acc_ref):
    step = pl.program_id(0)

    @pl.when(step == 0)
    def _():
        acc_ref[...] = jnp.zeros_like(acc_ref)

    stacked = jnp.concatenate([mine_ref[...], theirs_ref[...]], 0)
    acc_ref[...] += lax.dot_general(
        stacked,
        stacked,
        (((1,), (1,)), ((), ())),
        precision=lax.Precision.HIGHEST,
        preferred_element_type=jnp.float32,
    )

    @pl.when(step == pl.num_programs(0) - 1)
    def _():
        width = mine_ref.shape[0]
        row = lax.broadcasted_iota(jnp.int32, (width, width), 0)
        col = lax.broadcasted_iota(jnp.int32, (width, width), 1)
        gram_theirs = acc_ref[width:, width:]
        out_ref[:width, :] = jnp.where(row <= col, acc_ref[:width, :width], gram_theirs)
        out_ref[width : 2 * width, :] = acc_ref[:width, width:]
        diag_theirs = jnp.sum(jnp.where(row == col, gram_theirs, 0.0), axis=0, keepdims=True)
        out_ref[2 * width :, :] = jnp.broadcast_to(diag_theirs, (8, width))


def gram_store_kernel(
    mine_ref, theirs_ref, own_in, other_in, terms_in, out_ref, own_ref, other_ref, acc_ref
):
    del own_in, other_in
    gram_kernel(mine_ref, theirs_ref, out_ref, acc_ref)
    out_ref[...] = out_ref[...] + terms_in[...]
    own_ref[...] = mine_ref[...]
    other_ref[...] = theirs_ref[...]


def pair_terms_stored(mine, theirs, own_full, other_full, terms, chunk):
    width, piece = mine.shape
    cell_spec = pl.BlockSpec((width, piece), lambda step: (0, 0))
    full_spec = pl.BlockSpec((width, piece), lambda step: (0, chunk))
    return pl.pallas_call(
        gram_store_kernel,
        out_shape=[
            jax.ShapeDtypeStruct((2 * width + 8, width), jnp.float32),
            jax.ShapeDtypeStruct(own_full.shape, own_full.dtype),
            jax.ShapeDtypeStruct(other_full.shape, other_full.dtype),
        ],
        grid=(1,),
        in_specs=[
            cell_spec,
            cell_spec,
            pl.BlockSpec(memory_space=pl.ANY),
            pl.BlockSpec(memory_space=pl.ANY),
            pl.BlockSpec((2 * width + 8, width), lambda step: (0, 0)),
        ],
        out_specs=[pl.BlockSpec((2 * width + 8, width), lambda step: (0, 0)), full_spec, full_spec],
        scratch_shapes=[pltpu.VMEM((2 * width, 2 * width), jnp.float32)],
        input_output_aliases={2: 1, 3: 2, 4: 0},
        cost_estimate=pl.CostEstimate(
            flops=8 * width * width * piece, transcendentals=0, bytes_accessed=16 * width * piece
        ),
    )(mine, theirs, own_full, other_full, terms)


def mine_kernel(mine_ref, out_ref, acc_ref):
    step = pl.program_id(0)

    @pl.when(step == 0)
    def _():
        acc_ref[...] = jnp.zeros_like(acc_ref)

    acc_ref[...] += lax.dot_general(
        mine_ref[...],
        mine_ref[...],
        (((1,), (1,)), ((), ())),
        precision=lax.Precision.HIGHEST,
        preferred_element_type=jnp.float32,
    )

    @pl.when(step == pl.num_programs(0) - 1)
    def _():
        width = mine_ref.shape[0]
        row = lax.broadcasted_iota(jnp.int32, (width, width), 0)
        col = lax.broadcasted_iota(jnp.int32, (width, width), 1)
        out_ref[:width, :] = jnp.where(row <= col, acc_ref[...], 0.0)
        out_ref[width:, :] = jnp.zeros((width + 8, width), jnp.float32)


def rest_kernel(mine_ref, theirs_ref, out_ref, acc_ref):
    step = pl.program_id(0)

    @pl.when(step == 0)
    def _():
        acc_ref[...] = jnp.zeros_like(acc_ref)

    stacked = jnp.concatenate([mine_ref[...], theirs_ref[...]], 0)
    acc_ref[...] += lax.dot_general(
        stacked,
        theirs_ref[...],
        (((1,), (1,)), ((), ())),
        precision=lax.Precision.HIGHEST,
        preferred_element_type=jnp.float32,
    )

    @pl.when(step == pl.num_programs(0) - 1)
    def _():
        width = mine_ref.shape[0]
        row = lax.broadcasted_iota(jnp.int32, (width, width), 0)
        col = lax.broadcasted_iota(jnp.int32, (width, width), 1)
        gram_theirs = acc_ref[width:, :]
        out_ref[:width, :] = jnp.where(row > col, gram_theirs, 0.0)
        out_ref[width : 2 * width, :] = acc_ref[:width, :]
        diag_theirs = jnp.sum(jnp.where(row == col, gram_theirs, 0.0), axis=0, keepdims=True)
        out_ref[2 * width :, :] = jnp.broadcast_to(diag_theirs, (8, width))


def split_terms(kernel, operands, acc_rows):
    width, cells = operands[0].shape
    tile = min(cells, 2048)
    cell_spec = pl.BlockSpec((width, tile), lambda step: (0, step))
    return pl.pallas_call(
        kernel,
        out_shape=jax.ShapeDtypeStruct((2 * width + 8, width), jnp.float32),
        grid=(cells // tile,),
        in_specs=[cell_spec] * len(operands),
        out_specs=pl.BlockSpec((2 * width + 8, width), lambda step: (0, 0)),
        scratch_shapes=[pltpu.VMEM((acc_rows, width), jnp.float32)],
        cost_estimate=pl.CostEstimate(
            flops=2 * acc_rows * width * cells,
            transcendentals=0,
            bytes_accessed=4 * width * cells * len(operands),
        ),
    )(*operands)


def pair_terms(mine, theirs):
    width, cells = mine.shape
    tile = min(cells, 2048)
    cell_spec = pl.BlockSpec((width, tile), lambda step: (0, step))
    return pl.pallas_call(
        gram_kernel,
        out_shape=jax.ShapeDtypeStruct((2 * width + 8, width), jnp.float32),
        grid=(cells // tile,),
        in_specs=[cell_spec, cell_spec],
        out_specs=pl.BlockSpec((2 * width + 8, width), lambda step: (0, 0)),
        scratch_shapes=[pltpu.VMEM((2 * width, 2 * width), jnp.float32)],
        cost_estimate=pl.CostEstimate(
            flops=8 * width * width * cells, transcendentals=0, bytes_accessed=8 * width * cells
        ),
    )(mine, theirs)


def row_total(part):
    count = lax.axis_size("rows")
    bit = 1
    while bit < count:
        pairs = [(source, source ^ bit) for source in range(count)]
        part = part + lax.ppermute(part, "rows", pairs)
        bit *= 2
    return part


CHUNKS = 4


def lay_kernel(chunk_ids, piece, source_ref, *out_refs):
    if len(chunk_ids) == 1:
        out_refs[0][...] = source_ref[...]
        return
    for chunk, out_ref in zip(chunk_ids, out_refs):
        out_ref[...] = source_ref[:, chunk * piece : (chunk + 1) * piece]


def lay_out(snapshots, rows_n, chunks, chunk_ids):
    local_rows, cells = snapshots.shape
    width = cells // rows_n
    piece = width // chunks
    out_spec = pl.BlockSpec((None, local_rows, piece), lambda dest: (dest, 0, 0))
    return pl.pallas_call(
        functools.partial(lay_kernel, tuple(chunk_ids), piece),
        out_shape=[jax.ShapeDtypeStruct((rows_n, local_rows, piece), snapshots.dtype)] * len(chunk_ids),
        grid=(rows_n,),
        in_specs=[
            pl.BlockSpec((local_rows, piece), lambda dest: (0, dest * chunks + chunk_ids[0]))
            if len(chunk_ids) == 1
            else pl.BlockSpec((local_rows, width), lambda dest: (0, dest))
        ],
        out_specs=[out_spec] * len(chunk_ids),
        cost_estimate=pl.CostEstimate(
            flops=0, transcendentals=0, bytes_accessed=8 * local_rows * piece * rows_n * len(chunk_ids)
        ),
    )(snapshots)


def exchange(bit_pos, snapshots):
    chunks = 1 if bit_pos == 0 else CHUNKS
    rows_n = lax.axis_size("rows")
    local_rows, cells = snapshots.shape
    width = cells // rows_n
    piece = width // chunks

    if chunks == 1:
        mine = lax.all_to_all(snapshots, "rows", split_axis=1, concat_axis=0, tiled=True)
        block_rows = mine.shape[0]
        own_terms = split_terms(mine_kernel, (mine,), block_rows)
        theirs = partner_2(mine, "cols", bit_pos)
        return mine, theirs, own_terms + split_terms(rest_kernel, (mine, theirs), 2 * block_rows)

    sends = lay_out(snapshots, rows_n, chunks, [0]) + lay_out(snapshots, rows_n, chunks, list(range(1, chunks)))

    def laid(chunk):
        return sends[chunk]

    def spread(sent):
        got = lax.all_to_all(sent, "rows", split_axis=0, concat_axis=0)
        return got.reshape(rows_n * local_rows, piece)

    own_parts = [spread(laid(0))]
    other_parts = []
    for chunk in range(1, chunks):
        held = (own_parts[-1], laid(chunk)) + tuple(other_parts[-1:])
        held = lax.optimization_barrier(held)
        own_parts[-1] = held[0]
        if other_parts:
            other_parts[-1] = held[2]
        other_parts.append(partner_2(held[0], "cols", bit_pos))
        own_parts.append(spread(held[1]))
    other_parts.append(partner_2(own_parts[-1], "cols", bit_pos))
    own_full = jnp.zeros((rows_n * local_rows, width), snapshots.dtype)
    other_full = jnp.zeros((rows_n * local_rows, width), snapshots.dtype)
    width_rows = rows_n * local_rows
    terms = jnp.zeros((2 * width_rows + 8, width_rows), jnp.float32)
    for chunk, (mine, theirs) in enumerate(zip(own_parts, other_parts)):
        terms, own_full, other_full = pair_terms_stored(mine, theirs, own_full, other_full, terms, chunk)
    return own_full, other_full, terms


def unpack_terms(packed, width):
    row = lax.broadcasted_iota(jnp.int32, (width, width), 0)
    col = lax.broadcasted_iota(jnp.int32, (width, width), 1)
    shared = packed[:width]
    gram_mixed = packed[width : 2 * width]
    diag_theirs = packed[2 * width : 2 * width + 1]
    gram_mine = jnp.where(row <= col, shared, shared.T)
    gram_theirs = jnp.where(row > col, shared, jnp.where(row < col, shared.T, diag_theirs))
    return gram_mine, gram_mixed, gram_theirs


def assemble(terms, own_low):
    gram_mine, gram_mixed, gram_theirs = unpack_terms(row_total(terms), terms.shape[1])
    upper_left = jnp.where(own_low, gram_mine, gram_theirs)
    lower_right = jnp.where(own_low, gram_theirs, gram_mine)
    upper_right = jnp.where(own_low, gram_mixed, gram_mixed.T)
    top_rows = jnp.concatenate([upper_left, upper_right], 1)
    bottom_rows = jnp.concatenate([upper_right.T, lower_right], 1)
    return jnp.concatenate([top_rows, bottom_rows], 0)


def rotate_kernel(low_ref, rotation_ref, mine_ref, theirs_ref, out_ref):
    low = low_ref[0] != 0
    rotation = rotation_ref[...]
    width = mine_ref.shape[0]
    own_columns = jnp.where(low, rotation[:, :width], rotation[:, width:])
    coef_mine = jnp.where(low, own_columns[:width], own_columns[width:])
    coef_theirs = jnp.where(low, own_columns[width:], own_columns[:width])
    coef = jnp.concatenate([coef_mine, coef_theirs], 0).T
    stacked = jnp.concatenate([mine_ref[...], theirs_ref[...]], 0)
    out_ref[...] = jnp.dot(
        coef, stacked, precision=lax.Precision.HIGHEST, preferred_element_type=jnp.float32
    )


def rotate_part(rotation, low, mine, theirs):
    width, cells = mine.shape
    tile = min(cells, 2048)
    cell_spec = pl.BlockSpec((width, tile), lambda step: (0, step))
    return pl.pallas_call(
        rotate_kernel,
        out_shape=jax.ShapeDtypeStruct((width, cells), jnp.float32),
        grid=(cells // tile,),
        in_specs=[
            pl.BlockSpec(memory_space=pltpu.SMEM),
            pl.BlockSpec(rotation.shape, lambda step: (0, 0)),
            cell_spec,
            cell_spec,
        ],
        out_specs=cell_spec,
        cost_estimate=pl.CostEstimate(
            flops=4 * width * width * cells, transcendentals=0, bytes_accessed=12 * width * cells
        ),
    )(low, rotation, mine, theirs)


def shards(snapshots, pair_table):
    bit_count = lax.axis_size("cols").bit_length() - 1
    column = lax.axis_index("cols")
    mask_val = pair_table[0]
    bit_index = jnp.int32(0)
    for bit_pos in range(bit_count):
        bit_index = bit_index + (mask_val >> bit_pos & 1) * bit_pos
    partner = jnp.bitwise_xor(column, mask_val)
    own_low = column < partner
    branches = [functools.partial(exchange, bit_pos) for bit_pos in range(bit_count)]
    own_parts, other_parts, terms = lax.switch(bit_index, branches, snapshots)
    low = own_low.astype(jnp.int32).reshape(1)
    rotation = jacobi_pallas(low, row_total(terms))
    return rotate_part(rotation, low, own_parts, other_parts)


def solution(mesh):
    in_specs = (P(("cols", "rows"), None), P())
    out_specs = P("cols", "rows")
    return jax.shard_map(shards, mesh=mesh, in_specs=in_specs, out_specs=out_specs, check_vma=False)
```

```python
import functools

import jax
import jax.numpy as jnp
import numpy as np
from jax import lax
from jax.experimental import pallas as pl
from jax.experimental.pallas import tpu as pltpu
from jax.sharding import PartitionSpec as P

ROUNDS = 8


def partner_2(value, axis, bit):
    mask = 2**bit
    pairs = [(source, source ^ mask) for source in range(lax.axis_size(axis))]
    return lax.ppermute(value, axis, pairs)


def packed_gram(low, packed):
    width = packed.shape[1]
    row = lax.broadcasted_iota(jnp.int32, (width, width), 0)
    col = lax.broadcasted_iota(jnp.int32, (width, width), 1)
    shared = packed[:width]
    shared_t = shared.T
    gram_mixed = packed[width : 2 * width]
    diag_theirs = packed[2 * width : 2 * width + 1]
    gram_mine = jnp.where(row <= col, shared, shared_t)
    gram_theirs = jnp.where(row > col, shared, jnp.where(row < col, shared_t, diag_theirs))
    upper_left = jnp.where(low, gram_mine, gram_theirs)
    lower_right = jnp.where(low, gram_theirs, gram_mine)
    upper_right = jnp.where(low, gram_mixed, gram_mixed.T)
    top_rows = jnp.concatenate([upper_left, upper_right], 1)
    bottom_rows = jnp.concatenate([upper_right.T, lower_right], 1)
    return jnp.concatenate([top_rows, bottom_rows], 0)


def jacobi_kernel(low_ref, packed_ref, rotation_ref):
    highest = lax.Precision.HIGHEST
    gram = packed_gram(low_ref[0] != 0, packed_ref[...])
    order_dim = gram.shape[0]
    last_idx = order_dim - 1
    width = order_dim // 2
    row_col = lax.broadcasted_iota(jnp.int32, (order_dim, 1), 0)
    row_full = lax.broadcasted_iota(jnp.int32, (order_dim, order_dim), 0)
    col_full = lax.broadcasted_iota(jnp.int32, (order_dim, order_dim), 1)
    eye = row_full == col_full
    rotation = None
    for round_idx in range(ROUNDS):
        fixed = round_idx % last_idx
        mirror = 2 * fixed - row_col
        mirror = jnp.where(mirror < 0, mirror + last_idx, mirror)
        partner = jnp.where(row_col == fixed, last_idx, jnp.where(row_col == last_idx, fixed, mirror))
        offset = row_col - fixed
        offset = jnp.where(offset < 0, offset + last_idx, offset)
        is_first = (row_col == last_idx) | ((row_col != fixed) & (offset >= 1) & (offset <= width - 1))
        swap = (col_full == partner).astype(jnp.float32)
        on_diag = jnp.where(eye, gram, 0.0)
        diag_own = jnp.sum(on_diag, axis=1, keepdims=True)
        diag_row = jnp.sum(on_diag, axis=0, keepdims=True)
        diag_mate = jnp.sum(swap * diag_row, axis=1, keepdims=True)
        picked = gram * swap
        cross_second = jnp.sum(picked, axis=1, keepdims=True)
        cross_row = jnp.sum(picked, axis=0, keepdims=True)
        cross_first = jnp.sum(jnp.where(eye, cross_row, 0.0), axis=1, keepdims=True)
        cross_val = jnp.where(is_first, cross_first, cross_second)
        spread = jnp.where(is_first, diag_mate - diag_own, diag_own - diag_mate)
        hypot_val = jnp.sqrt(spread * spread + 4.0 * cross_val * cross_val)
        denom = jnp.sqrt(2.0 * hypot_val * (hypot_val + jnp.abs(spread)))
        sign_val = jnp.where(spread >= 0.0, 1.0, -1.0)
        cosine = (hypot_val + jnp.abs(spread)) / denom
        sine_val = 2.0 * cross_val * sign_val / denom
        signed = jnp.where(is_first, sine_val, -sine_val)
        diag_part = jnp.where(eye, cosine, 0.0)
        turn = diag_part + swap * signed
        turn_t = diag_part - swap * signed
        gram = jnp.dot(
            turn_t,
            jnp.dot(gram, turn, precision=highest, preferred_element_type=jnp.float32),
            precision=highest,
            preferred_element_type=jnp.float32,
        )
        rotation = turn if rotation is None else jnp.dot(
            rotation, turn, precision=highest, preferred_element_type=jnp.float32
        )
    rotation_ref[...] = rotation

def jacobi_pallas(low, packed):
    order_dim = 2 * packed.shape[1]
    return pl.pallas_call(
        jacobi_kernel,
        out_shape=jax.ShapeDtypeStruct((order_dim, order_dim), jnp.float32),
        in_specs=[pl.BlockSpec(memory_space=pltpu.SMEM), pl.BlockSpec(memory_space=pltpu.VMEM)],
        out_specs=pl.BlockSpec(memory_space=pltpu.VMEM),
    )(low, packed)


def gram_kernel(mine_ref, theirs_ref, out_ref, acc_ref):
    step = pl.program_id(0)

    @pl.when(step == 0)
    def _():
        acc_ref[...] = jnp.zeros_like(acc_ref)

    stacked = jnp.concatenate([mine_ref[...], theirs_ref[...]], 0)
    acc_ref[...] += lax.dot_general(
        stacked,
        stacked,
        (((1,), (1,)), ((), ())),
        precision=lax.Precision.HIGHEST,
        preferred_element_type=jnp.float32,
    )

    @pl.when(step == pl.num_programs(0) - 1)
    def _():
        width = mine_ref.shape[0]
        row = lax.broadcasted_iota(jnp.int32, (width, width), 0)
        col = lax.broadcasted_iota(jnp.int32, (width, width), 1)
        gram_theirs = acc_ref[width:, width:]
        out_ref[:width, :] = jnp.where(row <= col, acc_ref[:width, :width], gram_theirs)
        out_ref[width : 2 * width, :] = acc_ref[:width, width:]
        diag_theirs = jnp.sum(jnp.where(row == col, gram_theirs, 0.0), axis=0, keepdims=True)
        out_ref[2 * width :, :] = jnp.broadcast_to(diag_theirs, (8, width))


def gram_store_kernel(mine_ref, theirs_ref, own_in, other_in, out_ref, own_ref, other_ref, acc_ref):
    del own_in, other_in
    gram_kernel(mine_ref, theirs_ref, out_ref, acc_ref)
    own_ref[...] = mine_ref[...]
    other_ref[...] = theirs_ref[...]


def pair_terms_stored(mine, theirs, own_full, other_full, chunk):
    width, piece = mine.shape
    cell_spec = pl.BlockSpec((width, piece), lambda step: (0, 0))
    full_spec = pl.BlockSpec((width, piece), lambda step: (0, chunk))
    return pl.pallas_call(
        gram_store_kernel,
        out_shape=[
            jax.ShapeDtypeStruct((2 * width + 8, width), jnp.float32),
            jax.ShapeDtypeStruct(own_full.shape, own_full.dtype),
            jax.ShapeDtypeStruct(other_full.shape, other_full.dtype),
        ],
        grid=(1,),
        in_specs=[cell_spec, cell_spec, pl.BlockSpec(memory_space=pl.ANY), pl.BlockSpec(memory_space=pl.ANY)],
        out_specs=[pl.BlockSpec((2 * width + 8, width), lambda step: (0, 0)), full_spec, full_spec],
        scratch_shapes=[pltpu.VMEM((2 * width, 2 * width), jnp.float32)],
        input_output_aliases={2: 1, 3: 2},
        cost_estimate=pl.CostEstimate(
            flops=8 * width * width * piece, transcendentals=0, bytes_accessed=16 * width * piece
        ),
    )(mine, theirs, own_full, other_full)


def mine_kernel(mine_ref, out_ref, acc_ref):
    step = pl.program_id(0)

    @pl.when(step == 0)
    def _():
        acc_ref[...] = jnp.zeros_like(acc_ref)

    acc_ref[...] += lax.dot_general(
        mine_ref[...],
        mine_ref[...],
        (((1,), (1,)), ((), ())),
        precision=lax.Precision.HIGHEST,
        preferred_element_type=jnp.float32,
    )

    @pl.when(step == pl.num_programs(0) - 1)
    def _():
        width = mine_ref.shape[0]
        row = lax.broadcasted_iota(jnp.int32, (width, width), 0)
        col = lax.broadcasted_iota(jnp.int32, (width, width), 1)
        out_ref[:width, :] = jnp.where(row <= col, acc_ref[...], 0.0)
        out_ref[width:, :] = jnp.zeros((width + 8, width), jnp.float32)


def rest_kernel(mine_ref, theirs_ref, out_ref, acc_ref):
    step = pl.program_id(0)

    @pl.when(step == 0)
    def _():
        acc_ref[...] = jnp.zeros_like(acc_ref)

    stacked = jnp.concatenate([mine_ref[...], theirs_ref[...]], 0)
    acc_ref[...] += lax.dot_general(
        stacked,
        theirs_ref[...],
        (((1,), (1,)), ((), ())),
        precision=lax.Precision.HIGHEST,
        preferred_element_type=jnp.float32,
    )

    @pl.when(step == pl.num_programs(0) - 1)
    def _():
        width = mine_ref.shape[0]
        row = lax.broadcasted_iota(jnp.int32, (width, width), 0)
        col = lax.broadcasted_iota(jnp.int32, (width, width), 1)
        gram_theirs = acc_ref[width:, :]
        out_ref[:width, :] = jnp.where(row > col, gram_theirs, 0.0)
        out_ref[width : 2 * width, :] = acc_ref[:width, :]
        diag_theirs = jnp.sum(jnp.where(row == col, gram_theirs, 0.0), axis=0, keepdims=True)
        out_ref[2 * width :, :] = jnp.broadcast_to(diag_theirs, (8, width))


def split_terms(kernel, operands, acc_rows):
    width, cells = operands[0].shape
    tile = min(cells, 2048)
    cell_spec = pl.BlockSpec((width, tile), lambda step: (0, step))
    return pl.pallas_call(
        kernel,
        out_shape=jax.ShapeDtypeStruct((2 * width + 8, width), jnp.float32),
        grid=(cells // tile,),
        in_specs=[cell_spec] * len(operands),
        out_specs=pl.BlockSpec((2 * width + 8, width), lambda step: (0, 0)),
        scratch_shapes=[pltpu.VMEM((acc_rows, width), jnp.float32)],
        cost_estimate=pl.CostEstimate(
            flops=2 * acc_rows * width * cells,
            transcendentals=0,
            bytes_accessed=4 * width * cells * len(operands),
        ),
    )(*operands)


def pair_terms(mine, theirs):
    width, cells = mine.shape
    tile = min(cells, 2048)
    cell_spec = pl.BlockSpec((width, tile), lambda step: (0, step))
    return pl.pallas_call(
        gram_kernel,
        out_shape=jax.ShapeDtypeStruct((2 * width + 8, width), jnp.float32),
        grid=(cells // tile,),
        in_specs=[cell_spec, cell_spec],
        out_specs=pl.BlockSpec((2 * width + 8, width), lambda step: (0, 0)),
        scratch_shapes=[pltpu.VMEM((2 * width, 2 * width), jnp.float32)],
        cost_estimate=pl.CostEstimate(
            flops=8 * width * width * cells, transcendentals=0, bytes_accessed=8 * width * cells
        ),
    )(mine, theirs)


def row_total(part):
    count = lax.axis_size("rows")
    bit = 1
    while bit < count:
        pairs = [(source, source ^ bit) for source in range(count)]
        part = part + lax.ppermute(part, "rows", pairs)
        bit *= 2
    return part


CHUNKS = 4


def lay_kernel(chunk_ids, piece, source_ref, *out_refs):
    if len(chunk_ids) == 1:
        out_refs[0][...] = source_ref[...]
        return
    for chunk, out_ref in zip(chunk_ids, out_refs):
        out_ref[...] = source_ref[:, chunk * piece : (chunk + 1) * piece]


def lay_out(snapshots, rows_n, chunks, chunk_ids):
    local_rows, cells = snapshots.shape
    width = cells // rows_n
    piece = width // chunks
    out_spec = pl.BlockSpec((None, local_rows, piece), lambda dest: (dest, 0, 0))
    return pl.pallas_call(
        functools.partial(lay_kernel, tuple(chunk_ids), piece),
        out_shape=[jax.ShapeDtypeStruct((rows_n, local_rows, piece), snapshots.dtype)] * len(chunk_ids),
        grid=(rows_n,),
        in_specs=[
            pl.BlockSpec((local_rows, piece), lambda dest: (0, dest * chunks + chunk_ids[0]))
            if len(chunk_ids) == 1
            else pl.BlockSpec((local_rows, width), lambda dest: (0, dest))
        ],
        out_specs=[out_spec] * len(chunk_ids),
        cost_estimate=pl.CostEstimate(
            flops=0, transcendentals=0, bytes_accessed=8 * local_rows * piece * rows_n * len(chunk_ids)
        ),
    )(snapshots)


def exchange(bit_pos, snapshots):
    chunks = 1 if bit_pos == 0 else CHUNKS
    rows_n = lax.axis_size("rows")
    local_rows, cells = snapshots.shape
    width = cells // rows_n
    piece = width // chunks

    if chunks == 1:
        mine = lax.all_to_all(snapshots, "rows", split_axis=1, concat_axis=0, tiled=True)
        block_rows = mine.shape[0]
        own_terms = split_terms(mine_kernel, (mine,), block_rows)
        theirs = partner_2(mine, "cols", bit_pos)
        return mine, theirs, own_terms + split_terms(rest_kernel, (mine, theirs), 2 * block_rows)

    sends = lay_out(snapshots, rows_n, chunks, [0]) + lay_out(snapshots, rows_n, chunks, list(range(1, chunks)))

    def laid(chunk):
        return sends[chunk]

    def spread(sent):
        got = lax.all_to_all(sent, "rows", split_axis=0, concat_axis=0)
        return got.reshape(rows_n * local_rows, piece)

    own_parts = [spread(laid(0))]
    other_parts = []
    for chunk in range(1, chunks):
        held = (own_parts[-1], laid(chunk)) + tuple(other_parts[-1:])
        held = lax.optimization_barrier(held)
        own_parts[-1] = held[0]
        if other_parts:
            other_parts[-1] = held[2]
        other_parts.append(partner_2(held[0], "cols", bit_pos))
        own_parts.append(spread(held[1]))
    other_parts.append(partner_2(own_parts[-1], "cols", bit_pos))
    own_full = jnp.zeros((rows_n * local_rows, width), snapshots.dtype)
    other_full = jnp.zeros((rows_n * local_rows, width), snapshots.dtype)
    terms = None
    for chunk, (mine, theirs) in enumerate(zip(own_parts, other_parts)):
        part, own_full, other_full = pair_terms_stored(mine, theirs, own_full, other_full, chunk)
        terms = part if terms is None else terms + part
    return own_full, other_full, terms


def unpack_terms(packed, width):
    row = lax.broadcasted_iota(jnp.int32, (width, width), 0)
    col = lax.broadcasted_iota(jnp.int32, (width, width), 1)
    shared = packed[:width]
    gram_mixed = packed[width : 2 * width]
    diag_theirs = packed[2 * width : 2 * width + 1]
    gram_mine = jnp.where(row <= col, shared, shared.T)
    gram_theirs = jnp.where(row > col, shared, jnp.where(row < col, shared.T, diag_theirs))
    return gram_mine, gram_mixed, gram_theirs


def assemble(terms, own_low):
    gram_mine, gram_mixed, gram_theirs = unpack_terms(row_total(terms), terms.shape[1])
    upper_left = jnp.where(own_low, gram_mine, gram_theirs)
    lower_right = jnp.where(own_low, gram_theirs, gram_mine)
    upper_right = jnp.where(own_low, gram_mixed, gram_mixed.T)
    top_rows = jnp.concatenate([upper_left, upper_right], 1)
    bottom_rows = jnp.concatenate([upper_right.T, lower_right], 1)
    return jnp.concatenate([top_rows, bottom_rows], 0)


def rotate_kernel(low_ref, rotation_ref, mine_ref, theirs_ref, out_ref, coef_ref):
    @pl.when(pl.program_id(0) == 0)
    def _():
        low = low_ref[0] != 0
        rotation = rotation_ref[...]
        width = mine_ref.shape[0]
        own_columns = jnp.where(low, rotation[:, :width], rotation[:, width:])
        coef_mine = jnp.where(low, own_columns[:width], own_columns[width:])
        coef_theirs = jnp.where(low, own_columns[width:], own_columns[:width])
        coef_ref[...] = jnp.concatenate([coef_mine, coef_theirs], 0).T

    stacked = jnp.concatenate([mine_ref[...], theirs_ref[...]], 0)
    out_ref[...] = jnp.dot(
        coef_ref[...], stacked, precision=lax.Precision.HIGHEST, preferred_element_type=jnp.float32
    )


def rotate_part(rotation, low, mine, theirs):
    width, cells = mine.shape
    tile = min(cells, 2048)
    cell_spec = pl.BlockSpec((width, tile), lambda step: (0, step))
    return pl.pallas_call(
        rotate_kernel,
        out_shape=jax.ShapeDtypeStruct((width, cells), jnp.float32),
        grid=(cells // tile,),
        in_specs=[
            pl.BlockSpec(memory_space=pltpu.SMEM),
            pl.BlockSpec(rotation.shape, lambda step: (0, 0)),
            cell_spec,
            cell_spec,
        ],
        out_specs=cell_spec,
        scratch_shapes=[pltpu.VMEM((width, 2 * width), jnp.float32)],
        cost_estimate=pl.CostEstimate(
            flops=4 * width * width * cells, transcendentals=0, bytes_accessed=12 * width * cells
        ),
    )(low, rotation, mine, theirs)


def shards(snapshots, pair_table):
    bit_count = lax.axis_size("cols").bit_length() - 1
    column = lax.axis_index("cols")
    mask_val = pair_table[0]
    bit_index = jnp.int32(0)
    for bit_pos in range(bit_count):
        bit_index = bit_index + (mask_val >> bit_pos & 1) * bit_pos
    partner = jnp.bitwise_xor(column, mask_val)
    own_low = column < partner
    branches = [functools.partial(exchange, bit_pos) for bit_pos in range(bit_count)]
    own_parts, other_parts, terms = lax.switch(bit_index, branches, snapshots)
    low = own_low.astype(jnp.int32).reshape(1)
    rotation = jacobi_pallas(low, row_total(terms))
    return rotate_part(rotation, low, own_parts, other_parts)


def solution(mesh):
    in_specs = (P(("cols", "rows"), None), P())
    out_specs = P("cols", "rows")
    return jax.shard_map(shards, mesh=mesh, in_specs=in_specs, out_specs=out_specs, check_vma=False)
```
